32 devices in a mesh: groups: 2 (over y), space: 8 (over z, core), member: 2 (over x).
Axes of the slice: x: 2, y: 2, z: 4, core: 2. Of those that a mesh axis runs over, the one named last changes fastest.
Arguments:
- features: bfloat16 [4, 256, 128, 256], P(('groups', 'member'), None, 'space'), parts along dimension 0, may hold values from -6 to 6
- views: int32 [4], P('groups'), parts along dimension 0, may hold values from 8 to 29
- conv_first: bfloat16 [3, 3, 256, 256], replicated, may hold values from -0.125 to 0.125
- bias_first: float32 [256], replicated, may hold values from -3 to 3
- conv_second: bfloat16 [3, 3, 256, 256], replicated, may hold values from -0.125 to 0.125
- bias_second: float32 [256], replicated, may hold values from -3 to 3
- classify: bfloat16 [19, 256], replicated, may hold values from -0.375 to 0.375
- class_bias: float32 [19], replicated, may hold values from -3 to 3
Outputs:
- ensemble_logits: float32 [1024, 19, 1024], P(('groups', 'space', 'member')), parts along dimension 0
The draws below stay inside these ranges and needn't reach their ends.
There are 2 independent parts, one for each index of `groups`. The reference program is written for one: setup_inputs(seed, part) draws one part's arguments, and reference() takes and returns one part's arrays. A program takes and returns all parts, laid end to end along the dimension named above; an argument that names none is the same for every part. Nothing has to cross between parts.
All inputs are finite; a program needn't handle non-finite values.
Results may differ from the reference program's by a relative error of at most 0.0035.
Values may be sent and summed in bfloat16 or wider, within the bound.
No kernel may reach another device: no remote copies, remote signals or barrier semaphores. Data moves between devices by JAX's collectives and lax.ppermute only.
A program may use at most 128 MiB of HBM per device.

```python
import jax
import jax.numpy as jnp
from jax import lax

C = 256
CLS = 19
FW = 256
M = 2
FH = 128
OH = 512
OW = 1024


def level_of(key, shape, shards, low, top_value):
    loudness = 1.0
    for position, shards_of in shards:
        heights = jax.random.uniform(jax.random.fold_in(jax.random.fold_in(key, 6), position), (shards_of,), jnp.float32, low / len(shards), top_value / len(shards))
        loudness = loudness * jnp.repeat(jnp.exp(heights), shape[position] // shards_of).reshape((-1,) + (1,) * (len(shape) - 1 - position))
    return loudness


def normal_values(rng, extent, spread, most, shards=(), kind=jnp.bfloat16):
    result = spread * jax.random.normal(rng, extent, jnp.float32)
    if shards:
        result = result * level_of(rng, extent, shards, -0.22, 0.18)
    return jnp.clip(result, -most, most).astype(kind)


def setup_inputs(seed: int = 0, part: int = 0) -> dict:
    key_list = jax.random.split(jax.random.key(seed), 9)
    part_splits = jax.random.split(jax.random.fold_in(key_list[8], part), 9)
    features = normal_values(part_splits[0], (M, C, FH, FW), 1.0, 6.0, ((0, 2), (2, 8)))
    views = jax.random.randint(part_splits[1], (M,), 8, 30).astype(jnp.int32)
    conv_first = normal_values(key_list[2], (3, 3, C, C), (9 * C) ** -0.5, 0.125)
    bias_first = normal_values(key_list[3], (C,), 0.5, 3.0, (), jnp.float32)
    conv_second = normal_values(key_list[4], (3, 3, C, C), (9 * C) ** -0.5, 0.125)
    bias_second = normal_values(key_list[5], (C,), 0.5, 3.0, (), jnp.float32)
    classify = normal_values(key_list[6], (CLS, C), C ** -0.5, 0.375)
    class_bias = normal_values(key_list[7], (CLS,), 0.5, 3.0, (), jnp.float32)
    return {"features": features, "views": views, "conv_first": conv_first, "bias_first": bias_first, "conv_second": conv_second, "bias_second": bias_second, "classify": classify, "class_bias": class_bias}


def resize_matrix(positions, out_len, valid, in_len):
    numer = (2 * positions + 1) * valid - out_len
    denom = 2 * out_len
    lower = numer // denom
    frac = (numer - lower * denom).astype(jnp.float32) / denom
    below = numer < 0
    frac = jnp.where(below, jnp.float32(0.0), frac)
    lower = jnp.where(below, 0, lower)
    top_index = valid - 1
    over = lower >= top_index
    frac = jnp.where(over, jnp.float32(0.0), frac)
    lower = jnp.where(over, top_index, lower)
    columns = jnp.arange(in_len, dtype=jnp.int32)
    first = jnp.where(columns[None, :] == lower[:, None], 1.0 - frac[:, None], jnp.float32(0.0))
    second = jnp.where(columns[None, :] == lower[:, None] + 1, frac[:, None], jnp.float32(0.0))
    return (first + second).astype(jnp.bfloat16)


def convolve(field, weights):
    height, width = field.shape[1], field.shape[2]
    padded = jnp.pad(field, ((0, 0), (1, 1), (1, 1))).astype(jnp.float32)
    total = jnp.zeros((weights.shape[2], height, width), jnp.float32)
    for row_tap in range(3):
        for col_tap in range(3):
            window = padded[:, row_tap:row_tap + height, col_tap:col_tap + width]
            total = total + jnp.einsum("oc,cyx->oyx", weights[row_tap, col_tap].astype(jnp.float32), window)
    return total


def reference(features, views, conv_first, bias_first, conv_second, bias_second, classify, class_bias):
    def member_step(carry, inputs):
        feat, code = inputs
        numer = code // 2
        flip = code % 2
        valid_rows = (FH * numer) // 14
        valid_cols = (FW * numer) // 14
        row_ok = jnp.arange(FH, dtype=jnp.int32) < valid_rows
        col_ok = jnp.arange(FW, dtype=jnp.int32) < valid_cols
        mask = (row_ok[:, None] & col_ok[None, :]).astype(jnp.float32)
        first = feat * mask.astype(jnp.bfloat16)
        hidden = (jax.nn.relu(convolve(first, conv_first) + bias_first[:, None, None]) * mask).astype(jnp.bfloat16)
        second = (jax.nn.relu(convolve(hidden, conv_second) + bias_second[:, None, None]) * mask).astype(jnp.bfloat16)
        logits = (jnp.einsum("kc,cyx->kyx", classify.astype(jnp.float32), second.astype(jnp.float32)) + class_bias[:, None, None]).astype(jnp.bfloat16)
        col_pos = jnp.arange(OW, dtype=jnp.int32)
        col_pos = jnp.where(flip == 1, OW - 1 - col_pos, col_pos)
        column_weights = resize_matrix(col_pos, OW, valid_cols, FW)
        row_weights = resize_matrix(jnp.arange(OH, dtype=jnp.int32), OH, valid_rows, FH)
        resized = jnp.einsum("cyx,jx->cyj", logits.astype(jnp.float32), column_weights.astype(jnp.float32)).astype(jnp.bfloat16)
        contrib = jnp.einsum("iy,cyj->icj", row_weights.astype(jnp.float32), resized.astype(jnp.float32))
        return carry + contrib, None

    start = jnp.zeros((OH, CLS, OW), jnp.float32)
    total, unused = lax.scan(member_step, start, (features, views))
    return total
```

```python
import jax
import jax.numpy as jnp
from jax import lax
from jax.sharding import PartitionSpec as P

UP = 4


def with_halo(block, sides, width):
    for axis, dim in sides:
        count = lax.axis_size(axis)
        forward = [(i, i + 1) for i in range(count - 1)]
        backward = [(target, source) for source, target in forward]
        low = lax.ppermute(
            lax.slice_in_dim(block, block.shape[dim] - width, None, axis=dim), axis, forward
        )
        high = lax.ppermute(lax.slice_in_dim(block, 0, width, axis=dim), axis, backward)
        block = jnp.concatenate([low, block, high], axis=dim)
    return block


def resize_matrix(positions, out_len, valid, in_len):
    numer = (2 * positions + 1) * valid - out_len
    denom = 2 * out_len
    lower = numer // denom
    frac = (numer - lower * denom).astype(jnp.float32) / denom
    below = numer < 0
    frac = jnp.where(below, jnp.float32(0.0), frac)
    lower = jnp.where(below, 0, lower)
    top_index = valid - 1
    over = lower >= top_index
    frac = jnp.where(over, jnp.float32(0.0), frac)
    lower = jnp.where(over, top_index, lower)
    columns = jnp.arange(in_len, dtype=jnp.int32)
    first = jnp.where(columns[None, :] == lower[:, None], 1.0 - frac[:, None], jnp.float32(0.0))
    second = jnp.where(columns[None, :] == lower[:, None] + 1, frac[:, None], jnp.float32(0.0))
    return (first + second).astype(jnp.bfloat16)


def convolve(field, weights):
    padded = with_halo(field, (("space", 1),), 1)
    out = lax.conv_general_dilated(
        padded[None],
        weights,
        window_strides=(1, 1),
        padding=((0, 0), (1, 1)),
        dimension_numbers=("NCHW", "HWOI", "NCHW"),
        preferred_element_type=jnp.float32,
    )
    return out[0]


def window_start(numer, first_row, full_rows, out_rows, window_rows):
    valid = full_rows * numer // 14
    numer_pos = (2 * first_row + 1) * valid - out_rows
    lower = numer_pos // (2 * out_rows)
    lower = jnp.where(numer_pos < 0, 0, lower)
    lower = jnp.where(lower >= valid - 1, valid - 1, lower)
    return jnp.clip(lower, 0, full_rows - window_rows)


def column_table(numer, flip, cols, out_cols):
    valid_cols = cols * numer // 14
    col_pos = jnp.arange(out_cols, dtype=jnp.int32)
    col_pos = jnp.where(flip == 1, out_cols - 1 - col_pos, col_pos)
    return resize_matrix(col_pos, out_cols, valid_cols, cols)


def shards(features, views, conv_first, bias_first, conv_second, bias_second, classify, class_bias):
    feat = features[0]
    rows_dev, cols = (feat.shape[1], feat.shape[2])
    spaces = lax.axis_size("space")
    full_rows = rows_dev * spaces
    place = lax.axis_index("space")
    member_index = lax.axis_index("member")
    members = views.shape[0]
    picked = jnp.arange(members, dtype=jnp.int32) == member_index
    code = jnp.sum(jnp.where(picked, views, 0))
    numer = code // 2
    valid_rows = full_rows * numer // 14
    valid_cols = cols * numer // 14
    row_ids = place * rows_dev + jnp.arange(rows_dev, dtype=jnp.int32)
    row_ok = row_ids < valid_rows
    col_ok = jnp.arange(cols, dtype=jnp.int32) < valid_cols
    mask = (row_ok[:, None] & col_ok[None, :]).astype(jnp.float32)
    first = feat * mask.astype(jnp.bfloat16)
    hidden = (jax.nn.relu(convolve(first, conv_first) + bias_first[:, None, None]) * mask).astype(
        jnp.bfloat16
    )
    second = (
        jax.nn.relu(convolve(hidden, conv_second) + bias_second[:, None, None]) * mask
    ).astype(jnp.bfloat16)
    logits = (
        jnp.einsum("kc,cyx->kyx", classify, second, preferred_element_type=jnp.float32)
        + class_bias[:, None, None]
    ).astype(jnp.bfloat16)
    out_rows = UP * full_rows
    out_cols = UP * cols
    own_rows = out_rows // spaces
    part_rows = own_rows // members
    window_rows = (part_rows - 1) // UP + 3
    gathered = lax.all_gather(logits, "space", axis=1, tiled=True)
    pieces = []
    for target in range(members):
        first_row = place * own_rows + target * part_rows
        begin = window_start(numer, first_row, full_rows, out_rows, window_rows)
        pieces.append(lax.dynamic_slice_in_dim(gathered, begin, window_rows, 1))
    outgoing = jnp.stack(pieces, 0)
    incoming = lax.all_to_all(outgoing, "member", split_axis=0, concat_axis=0, tiled=True)
    own_first = place * own_rows + member_index * part_rows
    positions = own_first + jnp.arange(part_rows, dtype=jnp.int32)
    result = jnp.zeros((part_rows, logits.shape[0], out_cols), jnp.float32)
    for source in range(members):
        source_numer = views[source] // 2
        source_flip = views[source] % 2
        source_valid = full_rows * source_numer // 14
        begin = window_start(source_numer, own_first, full_rows, out_rows, window_rows)
        source_cols = column_table(source_numer, source_flip, cols, out_cols)
        row_table = resize_matrix(positions, out_rows, source_valid, full_rows)
        row_part = lax.dynamic_slice_in_dim(row_table, begin, window_rows, 1)
        widened = jnp.einsum(
            "cyx,jx->cyj", incoming[source], source_cols, preferred_element_type=jnp.float32
        ).astype(jnp.bfloat16)
        result = result + jnp.einsum(
            "iy,cyj->icj", row_part, widened, preferred_element_type=jnp.float32
        )
    return result


def solution(mesh):
    placed = (
        P(("groups", "member"), None, "space", None),
        P("groups"),
        P(),
        P(),
        P(),
        P(),
        P(),
        P(),
    )
    return jax.shard_map(
        shards,
        mesh=mesh,
        in_specs=placed,
        out_specs=P(("groups", "space", "member"), None, None),
        check_vma=False,
    )
```

```python
import jax
import jax.numpy as jnp
from jax import lax
from jax.sharding import PartitionSpec as P

UP = 4


def with_halo(block, sides, width):
    for axis, dim in sides:
        count = lax.axis_size(axis)
        forward = [(i, i + 1) for i in range(count - 1)]
        backward = [(target, source) for source, target in forward]
        low = lax.ppermute(
            lax.slice_in_dim(block, block.shape[dim] - width, None, axis=dim), axis, forward
        )
        high = lax.ppermute(lax.slice_in_dim(block, 0, width, axis=dim), axis, backward)
        block = jnp.concatenate([low, block, high], axis=dim)
    return block


def gather_rows(block, axis):
    count = lax.axis_size(axis)
    if count & (count - 1):
        return lax.all_gather(block, axis, axis=0, tiled=True)
    me = lax.axis_index(axis)
    held = block[None]
    bit = count // 2
    while bit:
        other = lax.ppermute(held, axis, [(i, i ^ bit) for i in range(count)])
        upper = (me & bit) != 0
        held = jnp.where(upper, jnp.stack([other, held], 1), jnp.stack([held, other], 1))
        held = held.reshape((-1,) + block.shape)
        bit //= 2
    return held.reshape((count * block.shape[0],) + block.shape[1:])


def resize_matrix(positions, out_len, valid, in_len):
    numer = (2 * positions + 1) * valid - out_len
    denom = 2 * out_len
    lower = numer // denom
    frac = (numer - lower * denom).astype(jnp.float32) / denom
    below = numer < 0
    frac = jnp.where(below, jnp.float32(0.0), frac)
    lower = jnp.where(below, 0, lower)
    top_index = valid - 1
    over = lower >= top_index
    frac = jnp.where(over, jnp.float32(0.0), frac)
    lower = jnp.where(over, top_index, lower)
    columns = jnp.arange(in_len, dtype=jnp.int32)
    first = jnp.where(columns[None, :] == lower[:, None], 1.0 - frac[:, None], jnp.float32(0.0))
    second = jnp.where(columns[None, :] == lower[:, None] + 1, frac[:, None], jnp.float32(0.0))
    return (first + second).astype(jnp.bfloat16)


def convolve(field, weights):
    padded = with_halo(field, (("space", 0),), 1)
    out = lax.conv_general_dilated(
        padded[None],
        weights,
        window_strides=(1, 1),
        padding=((0, 0), (1, 1)),
        dimension_numbers=("NHWC", "HWOI", "NHWC"),
        preferred_element_type=jnp.float32,
    )
    return out[0]


def window_start(numer, first_row, full_rows, out_rows, window_rows):
    valid = full_rows * numer // 14
    numer_pos = (2 * first_row + 1) * valid - out_rows
    lower = numer_pos // (2 * out_rows)
    lower = jnp.where(numer_pos < 0, 0, lower)
    lower = jnp.where(lower >= valid - 1, valid - 1, lower)
    return jnp.clip(lower, 0, full_rows - window_rows)


def column_table(numer, flip, cols, out_cols):
    valid_cols = cols * numer // 14
    col_pos = jnp.arange(out_cols, dtype=jnp.int32)
    col_pos = jnp.where(flip == 1, out_cols - 1 - col_pos, col_pos)
    return resize_matrix(col_pos, out_cols, valid_cols, cols)


def shards(features, views, conv_first, bias_first, conv_second, bias_second, classify, class_bias):
    feat = features[0]
    rows_dev, cols = (feat.shape[1], feat.shape[2])
    spaces = lax.axis_size("space")
    full_rows = rows_dev * spaces
    place = lax.axis_index("space")
    member_index = lax.axis_index("member")
    members = views.shape[0]
    picked = jnp.arange(members, dtype=jnp.int32) == member_index
    code = jnp.sum(jnp.where(picked, views, 0))
    numer = code // 2
    valid_rows = full_rows * numer // 14
    valid_cols = cols * numer // 14
    row_ids = place * rows_dev + jnp.arange(rows_dev, dtype=jnp.int32)
    row_ok = row_ids < valid_rows
    col_ok = jnp.arange(cols, dtype=jnp.int32) < valid_cols
    mask = (row_ok[:, None] & col_ok[None, :]).astype(jnp.float32)
    first = jnp.transpose(feat * mask.astype(jnp.bfloat16), (1, 2, 0))
    cell = mask[:, :, None]
    hidden = (jax.nn.relu(convolve(first, conv_first) + bias_first) * cell).astype(jnp.bfloat16)
    second = (jax.nn.relu(convolve(hidden, conv_second) + bias_second) * cell).astype(jnp.bfloat16)
    logits = (
        jnp.einsum("kc,yxc->ykx", classify, second, preferred_element_type=jnp.float32)
        + class_bias[None, :, None]
    ).astype(jnp.bfloat16)
    out_rows = UP * full_rows
    out_cols = UP * cols
    own_rows = out_rows // spaces
    part_rows = own_rows // members
    window_rows = (part_rows - 1) // UP + 3
    gathered = gather_rows(logits, "space")
    pieces = []
    for target in range(members):
        first_row = place * own_rows + target * part_rows
        begin = window_start(numer, first_row, full_rows, out_rows, window_rows)
        pieces.append(lax.dynamic_slice_in_dim(gathered, begin, window_rows, 0))
    outgoing = jnp.stack(pieces, 0)
    own_first = place * own_rows + member_index * part_rows
    positions = own_first + jnp.arange(part_rows, dtype=jnp.int32)
    result = jnp.zeros((part_rows, logits.shape[1], out_cols), jnp.float32)
    for shift in range(members):
        if shift == 0:
            arrived = lax.dynamic_index_in_dim(outgoing, member_index, 0, keepdims=False)
        else:
            send = lax.dynamic_index_in_dim(
                outgoing, (member_index + shift) % members, 0, keepdims=False
            )
            arrived = lax.ppermute(
                send, "member", [(i, (i + shift) % members) for i in range(members)]
            )
        source = (member_index - shift) % members
        source_code = jnp.sum(jnp.where(jnp.arange(members) == source, views, 0))
        source_numer = source_code // 2
        source_flip = source_code % 2
        source_valid = full_rows * source_numer // 14
        begin = window_start(source_numer, own_first, full_rows, out_rows, window_rows)
        source_cols = column_table(source_numer, source_flip, cols, out_cols)
        row_table = resize_matrix(positions, out_rows, source_valid, full_rows)
        row_part = lax.dynamic_slice_in_dim(row_table, begin, window_rows, 1)
        widened = jnp.einsum(
            "ycx,jx->ycj", arrived, source_cols, preferred_element_type=jnp.float32
        ).astype(jnp.bfloat16)
        result = result + jnp.einsum(
            "iy,ycj->icj", row_part, widened, preferred_element_type=jnp.float32
        )
    return result


def solution(mesh):
    placed = (
        P(("groups", "member"), None, "space", None),
        P("groups"),
        P(),
        P(),
        P(),
        P(),
        P(),
        P(),
    )
    return jax.shard_map(
        shards,
        mesh=mesh,
        in_specs=placed,
        out_specs=P(("groups", "space", "member"), None, None),
        check_vma=False,
    )
```

```python
import functools

import jax
import jax.numpy as jnp
from jax import lax
from jax.experimental import pallas as pl
from jax.experimental.pallas import tpu as pltpu
from jax.sharding import PartitionSpec as P

UP = 4


def with_halo(block, sides, width):
    for axis, dim in sides:
        count = lax.axis_size(axis)
        forward = [(i, i + 1) for i in range(count - 1)]
        backward = [(target, source) for source, target in forward]
        low = lax.ppermute(
            lax.slice_in_dim(block, block.shape[dim] - width, None, axis=dim), axis, forward
        )
        high = lax.ppermute(lax.slice_in_dim(block, 0, width, axis=dim), axis, backward)
        block = jnp.concatenate([low, block, high], axis=dim)
    return block


def gather_rows(block, axis):
    count = lax.axis_size(axis)
    if count & (count - 1):
        return lax.all_gather(block, axis, axis=0, tiled=True)
    me = lax.axis_index(axis)
    held = block[None]
    bit = count // 2
    while bit:
        other = lax.ppermute(held, axis, [(i, i ^ bit) for i in range(count)])
        upper = (me & bit) != 0
        held = jnp.where(upper, jnp.stack([other, held], 1), jnp.stack([held, other], 1))
        held = held.reshape((-1,) + block.shape)
        bit //= 2
    return held.reshape((count * block.shape[0],) + block.shape[1:])


def resize_matrix(positions, out_len, valid, in_len):
    numer = (2 * positions + 1) * valid - out_len
    denom = 2 * out_len
    lower = numer // denom
    frac = (numer - lower * denom).astype(jnp.float32) / denom
    below = numer < 0
    frac = jnp.where(below, jnp.float32(0.0), frac)
    lower = jnp.where(below, 0, lower)
    top_index = valid - 1
    over = lower >= top_index
    frac = jnp.where(over, jnp.float32(0.0), frac)
    lower = jnp.where(over, top_index, lower)
    columns = jnp.arange(in_len, dtype=jnp.int32)
    first = jnp.where(columns[None, :] == lower[:, None], 1.0 - frac[:, None], jnp.float32(0.0))
    second = jnp.where(columns[None, :] == lower[:, None] + 1, frac[:, None], jnp.float32(0.0))
    return (first + second).astype(jnp.bfloat16)


def conv_body(x_ref, w_ref, b_ref, s_ref, o_ref, *, block, width):
    lo, hi, good_cols = s_ref[0], s_ref[1], s_ref[2]
    chans = x_ref.shape[2]
    flat = block * width
    place = lax.broadcasted_iota(jnp.int32, (flat, 1), 0)
    col = place % width
    bias = b_ref[...]

    def step(i, carry):
        r0 = i * block
        taps = []
        for b in range(3):
            acc = None
            for a in range(3):
                xs = x_ref[pl.ds(r0 + a, block), :, :].reshape(flat, chans)
                d = lax.dot_general(
                    xs, w_ref[a, b], (((1,), (1,)), ((), ())), preferred_element_type=jnp.float32
                )
                acc = d if acc is None else acc + d
            taps.append(acc)
        left = jnp.where(col == 0, 0.0, pltpu.roll(taps[0], 1, 0))
        right = jnp.where(col == width - 1, 0.0, pltpu.roll(taps[2], flat - 1, 0))
        total = jnp.maximum(taps[1] + left + right + bias, 0.0)
        row = r0 + place // width
        keep = (row >= lo) & (row < hi) & (col < good_cols)
        out = jnp.where(keep, total, 0.0)
        o_ref[pl.ds(r0, block), :, :] = out.reshape(block, width, -1).astype(o_ref.dtype)
        return carry

    lax.fori_loop(0, o_ref.shape[0] // block, step, 0)


def conv_layer(x, weights, bias, limits):
    rows_in, width, chans = x.shape
    rows_out = rows_in - 2
    outs = weights.shape[2]
    block = next(k for k in (4, 3, 2, 1) if rows_out % k == 0)
    vmem = pl.BlockSpec(memory_space=pltpu.VMEM)
    cost = pl.CostEstimate(
        flops=2 * 9 * rows_out * width * chans * outs,
        bytes_accessed=2 * (x.size + weights.size + rows_out * width * outs),
        transcendentals=0,
    )
    return pl.pallas_call(
        functools.partial(conv_body, block=block, width=width),
        out_shape=jax.ShapeDtypeStruct((rows_out, width, outs), jnp.bfloat16),
        in_specs=[vmem, vmem, vmem, pl.BlockSpec(memory_space=pltpu.SMEM)],
        out_specs=vmem,
        cost_estimate=cost,
    )(x, weights, bias.reshape(1, -1), limits)


def window_start(numer, first_row, full_rows, out_rows, window_rows):
    valid = full_rows * numer // 14
    numer_pos = (2 * first_row + 1) * valid - out_rows
    lower = numer_pos // (2 * out_rows)
    lower = jnp.where(numer_pos < 0, 0, lower)
    lower = jnp.where(lower >= valid - 1, valid - 1, lower)
    return jnp.clip(lower, 0, full_rows - window_rows)


def column_table(numer, flip, cols, out_cols):
    valid_cols = cols * numer // 14
    col_pos = jnp.arange(out_cols, dtype=jnp.int32)
    col_pos = jnp.where(flip == 1, out_cols - 1 - col_pos, col_pos)
    return resize_matrix(col_pos, out_cols, valid_cols, cols)


def shards(features, views, conv_first, bias_first, conv_second, bias_second, classify, class_bias):
    feat = features[0]
    rows_dev, cols = (feat.shape[1], feat.shape[2])
    spaces = lax.axis_size("space")
    full_rows = rows_dev * spaces
    place = lax.axis_index("space")
    member_index = lax.axis_index("member")
    members = views.shape[0]
    picked = jnp.arange(members, dtype=jnp.int32) == member_index
    code = jnp.sum(jnp.where(picked, views, 0))
    numer = code // 2
    valid_rows = full_rows * numer // 14
    valid_cols = cols * numer // 14
    row_ids = place * rows_dev + jnp.arange(rows_dev, dtype=jnp.int32)
    row_ok = row_ids < valid_rows
    col_ok = jnp.arange(cols, dtype=jnp.int32) < valid_cols
    mask = (row_ok[:, None] & col_ok[None, :]).astype(jnp.bfloat16)
    first = jnp.transpose(feat * mask, (1, 2, 0))
    padded = with_halo(first, (("space", 0),), 2)
    top = place * rows_dev
    limits_first = jnp.stack([1 - top, valid_rows - top + 1, valid_cols]).astype(jnp.int32)
    limits_second = jnp.stack([-top, valid_rows - top, valid_cols]).astype(jnp.int32)
    hidden = conv_layer(padded, conv_first, bias_first, limits_first)
    second = conv_layer(hidden, conv_second, bias_second, limits_second)
    logits = (
        jnp.einsum("kc,yxc->ykx", classify, second, preferred_element_type=jnp.float32)
        + class_bias[None, :, None]
    ).astype(jnp.bfloat16)
    out_rows = UP * full_rows
    out_cols = UP * cols
    own_rows = out_rows // spaces
    part_rows = own_rows // members
    window_rows = (part_rows - 1) // UP + 3
    gathered = gather_rows(logits, "space")
    pieces = []
    for target in range(members):
        first_row = place * own_rows + target * part_rows
        begin = window_start(numer, first_row, full_rows, out_rows, window_rows)
        pieces.append(lax.dynamic_slice_in_dim(gathered, begin, window_rows, 0))
    outgoing = jnp.stack(pieces, 0)
    own_first = place * own_rows + member_index * part_rows
    positions = own_first + jnp.arange(part_rows, dtype=jnp.int32)
    result = jnp.zeros((part_rows, logits.shape[1], out_cols), jnp.float32)
    for shift in range(members):
        if shift == 0:
            arrived = lax.dynamic_index_in_dim(outgoing, member_index, 0, keepdims=False)
        else:
            send = lax.dynamic_index_in_dim(
                outgoing, (member_index + shift) % members, 0, keepdims=False
            )
            arrived = lax.ppermute(
                send, "member", [(i, (i + shift) % members) for i in range(members)]
            )
        source = (member_index - shift) % members
        source_code = jnp.sum(jnp.where(jnp.arange(members) == source, views, 0))
        source_numer = source_code // 2
        source_flip = source_code % 2
        source_valid = full_rows * source_numer // 14
        begin = window_start(source_numer, own_first, full_rows, out_rows, window_rows)
        source_cols = column_table(source_numer, source_flip, cols, out_cols)
        row_table = resize_matrix(positions, out_rows, source_valid, full_rows)
        row_part = lax.dynamic_slice_in_dim(row_table, begin, window_rows, 1)
        widened = jnp.einsum(
            "ycx,jx->ycj", arrived, source_cols, preferred_element_type=jnp.float32
        ).astype(jnp.bfloat16)
        result = result + jnp.einsum(
            "iy,ycj->icj", row_part, widened, preferred_element_type=jnp.float32
        )
    return result


def solution(mesh):
    placed = (
        P(("groups", "member"), None, "space", None),
        P("groups"),
        P(),
        P(),
        P(),
        P(),
        P(),
        P(),
    )
    return jax.shard_map(
        shards,
        mesh=mesh,
        in_specs=placed,
        out_specs=P(("groups", "space", "member"), None, None),
        check_vma=False,
    )
```

```python
import functools

import jax
import jax.numpy as jnp
from jax import lax
from jax.experimental import pallas as pl
from jax.experimental.pallas import tpu as pltpu
from jax.sharding import PartitionSpec as P

UP = 4


def with_halo(block, sides, width):
    for axis, dim in sides:
        count = lax.axis_size(axis)
        forward = [(i, i + 1) for i in range(count - 1)]
        backward = [(target, source) for source, target in forward]
        low = lax.ppermute(
            lax.slice_in_dim(block, block.shape[dim] - width, None, axis=dim), axis, forward
        )
        high = lax.ppermute(lax.slice_in_dim(block, 0, width, axis=dim), axis, backward)
        block = jnp.concatenate([low, block, high], axis=dim)
    return block


def gather_rows(block, axis):
    count = lax.axis_size(axis)
    if count & (count - 1):
        return lax.all_gather(block, axis, axis=1, tiled=True)
    me = lax.axis_index(axis)
    lead, rows, rest = block.shape[0], block.shape[1], block.shape[2:]
    held = block[:, None]
    bit = count // 2
    while bit:
        other = lax.ppermute(held, axis, [(i, i ^ bit) for i in range(count)])
        upper = (me & bit) != 0
        held = jnp.where(upper, jnp.stack([other, held], 2), jnp.stack([held, other], 2))
        held = held.reshape((lead, -1, rows) + rest)
        bit //= 2
    return held.reshape((lead, count * rows) + rest)


def resize_matrix(positions, out_len, valid, in_len):
    numer = (2 * positions + 1) * valid - out_len
    denom = 2 * out_len
    lower = numer // denom
    frac = (numer - lower * denom).astype(jnp.float32) / denom
    below = numer < 0
    frac = jnp.where(below, jnp.float32(0.0), frac)
    lower = jnp.where(below, 0, lower)
    top_index = valid - 1
    over = lower >= top_index
    frac = jnp.where(over, jnp.float32(0.0), frac)
    lower = jnp.where(over, top_index, lower)
    columns = jnp.arange(in_len, dtype=jnp.int32)
    first = jnp.where(columns[None, :] == lower[:, None], 1.0 - frac[:, None], jnp.float32(0.0))
    second = jnp.where(columns[None, :] == lower[:, None] + 1, frac[:, None], jnp.float32(0.0))
    return (first + second).astype(jnp.bfloat16)


def conv_body(*refs, block, width, project):
    if project:
        x_ref, w_ref, b_ref, k_ref, kb_ref, s_ref, o_ref = refs
    else:
        x_ref, w_ref, b_ref, s_ref, o_ref = refs
    lo, hi, good_cols = s_ref[0], s_ref[1], s_ref[2]
    flat = block * width
    place = lax.broadcasted_iota(jnp.int32, (1, flat), 1)
    col = place % width
    bias = b_ref[...]

    def step(i, carry):
        r0 = i * block
        taps = []
        for b in range(3):
            acc = None
            for a in range(3):
                start = pl.multiple_of((r0 + a) * width, width)
                xs = x_ref[:, pl.ds(start, flat)]
                d = jnp.dot(w_ref[a, b], xs, preferred_element_type=jnp.float32)
                acc = d if acc is None else acc + d
            taps.append(acc)
        left = jnp.where(col == 0, 0.0, pltpu.roll(taps[0], 1, 1))
        right = jnp.where(col == width - 1, 0.0, pltpu.roll(taps[2], flat - 1, 1))
        total = jnp.maximum(taps[1] + left + right + bias, 0.0)
        row = r0 + place // width
        keep = (row >= lo) & (row < hi) & (col < good_cols)
        out = jnp.where(keep, total, 0.0).astype(jnp.bfloat16)
        if project:
            out = jnp.dot(k_ref[...], out, preferred_element_type=jnp.float32) + kb_ref[...]
        o_ref[:, pl.ds(pl.multiple_of(r0 * width, width), flat)] = out.astype(o_ref.dtype)
        return carry

    lax.fori_loop(0, o_ref.shape[1] // flat, step, 0)


def conv_layer(x, weights, bias, limits, head=None):
    chans, rows_in, width = x.shape
    rows_out = rows_in - 2
    outs = weights.shape[2]
    block = next(k for k in (4, 3, 2, 1) if rows_out % k == 0)
    vmem = pl.BlockSpec(memory_space=pltpu.VMEM)
    args = [x.reshape(chans, rows_in * width), weights, bias.reshape(-1, 1)]
    flops = 2 * 9 * rows_out * width * chans * outs
    final = outs
    if head is not None:
        args += [head[0], head[1].reshape(-1, 1)]
        final = head[0].shape[0]
        flops += 2 * rows_out * width * outs * final
    cost = pl.CostEstimate(
        flops=flops,
        bytes_accessed=2 * (x.size + weights.size + rows_out * width * final),
        transcendentals=0,
    )
    out = pl.pallas_call(
        functools.partial(conv_body, block=block, width=width, project=head is not None),
        out_shape=jax.ShapeDtypeStruct((final, rows_out * width), jnp.bfloat16),
        in_specs=[vmem] * len(args) + [pl.BlockSpec(memory_space=pltpu.SMEM)],
        out_specs=vmem,
        cost_estimate=cost,
    )(*args, limits)
    return out.reshape(final, rows_out, width)


def window_start(numer, first_row, full_rows, out_rows, window_rows):
    valid = full_rows * numer // 14
    numer_pos = (2 * first_row + 1) * valid - out_rows
    lower = numer_pos // (2 * out_rows)
    lower = jnp.where(numer_pos < 0, 0, lower)
    lower = jnp.where(lower >= valid - 1, valid - 1, lower)
    return jnp.clip(lower, 0, full_rows - window_rows)


def column_table(numer, flip, cols, out_cols):
    valid_cols = cols * numer // 14
    col_pos = jnp.arange(out_cols, dtype=jnp.int32)
    col_pos = jnp.where(flip == 1, out_cols - 1 - col_pos, col_pos)
    return resize_matrix(col_pos, out_cols, valid_cols, cols)


def shards(features, views, conv_first, bias_first, conv_second, bias_second, classify, class_bias):
    feat = features[0]
    rows_dev, cols = (feat.shape[1], feat.shape[2])
    spaces = lax.axis_size("space")
    full_rows = rows_dev * spaces
    place = lax.axis_index("space")
    member_index = lax.axis_index("member")
    members = views.shape[0]
    picked = jnp.arange(members, dtype=jnp.int32) == member_index
    code = jnp.sum(jnp.where(picked, views, 0))
    numer = code // 2
    valid_rows = full_rows * numer // 14
    valid_cols = cols * numer // 14
    row_ids = place * rows_dev + jnp.arange(rows_dev, dtype=jnp.int32)
    row_ok = row_ids < valid_rows
    col_ok = jnp.arange(cols, dtype=jnp.int32) < valid_cols
    mask = (row_ok[:, None] & col_ok[None, :]).astype(jnp.bfloat16)
    first = feat * mask
    padded = with_halo(first, (("space", 1),), 2)
    top = place * rows_dev
    limits_first = jnp.stack([1 - top, valid_rows - top + 1, valid_cols]).astype(jnp.int32)
    limits_second = jnp.stack([-top, valid_rows - top, valid_cols]).astype(jnp.int32)
    hidden = conv_layer(padded, conv_first, bias_first, limits_first)
    logits = conv_layer(hidden, conv_second, bias_second, limits_second, (classify, class_bias))
    out_rows = UP * full_rows
    out_cols = UP * cols
    own_rows = out_rows // spaces
    part_rows = own_rows // members
    window_rows = (part_rows - 1) // UP + 3
    gathered = gather_rows(logits, "space")
    pieces = []
    for target in range(members):
        first_row = place * own_rows + target * part_rows
        begin = window_start(numer, first_row, full_rows, out_rows, window_rows)
        pieces.append(lax.dynamic_slice_in_dim(gathered, begin, window_rows, 1))
    outgoing = jnp.stack(pieces, 0)
    own_first = place * own_rows + member_index * part_rows
    positions = own_first + jnp.arange(part_rows, dtype=jnp.int32)
    result = jnp.zeros((part_rows, logits.shape[0], out_cols), jnp.float32)
    for shift in range(members):
        if shift == 0:
            arrived = lax.dynamic_index_in_dim(outgoing, member_index, 0, keepdims=False)
        else:
            send = lax.dynamic_index_in_dim(
                outgoing, (member_index + shift) % members, 0, keepdims=False
            )
            arrived = lax.ppermute(
                send, "member", [(i, (i + shift) % members) for i in range(members)]
            )
        source = (member_index - shift) % members
        source_code = jnp.sum(jnp.where(jnp.arange(members) == source, views, 0))
        source_numer = source_code // 2
        source_flip = source_code % 2
        source_valid = full_rows * source_numer // 14
        begin = window_start(source_numer, own_first, full_rows, out_rows, window_rows)
        source_cols = column_table(source_numer, source_flip, cols, out_cols)
        row_table = resize_matrix(positions, out_rows, source_valid, full_rows)
        row_part = lax.dynamic_slice_in_dim(row_table, begin, window_rows, 1)
        widened = jnp.einsum(
            "cyx,jx->cyj", arrived, source_cols, preferred_element_type=jnp.float32
        ).astype(jnp.bfloat16)
        result = result + jnp.einsum(
            "iy,cyj->icj", row_part, widened, preferred_element_type=jnp.float32
        )
    return result


def solution(mesh):
    placed = (
        P(("groups", "member"), None, "space", None),
        P("groups"),
        P(),
        P(),
        P(),
        P(),
        P(),
        P(),
    )
    return jax.shard_map(
        shards,
        mesh=mesh,
        in_specs=placed,
        out_specs=P(("groups", "space", "member"), None, None),
        check_vma=False,
    )
```

```python
import functools

import jax
import jax.numpy as jnp
from jax import lax
from jax.experimental import pallas as pl
from jax.experimental.pallas import tpu as pltpu
from jax.sharding import PartitionSpec as P

UP = 4


def with_halo(block, sides, width):
    for axis, dim in sides:
        count = lax.axis_size(axis)
        forward = [(i, i + 1) for i in range(count - 1)]
        backward = [(target, source) for source, target in forward]
        low = lax.ppermute(
            lax.slice_in_dim(block, block.shape[dim] - width, None, axis=dim), axis, forward
        )
        high = lax.ppermute(lax.slice_in_dim(block, 0, width, axis=dim), axis, backward)
        block = jnp.concatenate([low, block, high], axis=dim)
    return block


def gather_rows(block, axis):
    count = lax.axis_size(axis)
    if count & (count - 1):
        return lax.all_gather(block, axis, axis=1, tiled=True)
    me = lax.axis_index(axis)
    lead, rows, rest = block.shape[0], block.shape[1], block.shape[2:]
    held = block[:, None]
    bit = count // 2
    while bit:
        other = lax.ppermute(held, axis, [(i, i ^ bit) for i in range(count)])
        upper = (me & bit) != 0
        held = jnp.where(upper, jnp.stack([other, held], 2), jnp.stack([held, other], 2))
        held = held.reshape((lead, -1, rows) + rest)
        bit //= 2
    return held.reshape((lead, count * rows) + rest)


def resize_matrix(positions, out_len, valid, in_len):
    numer = (2 * positions + 1) * valid - out_len
    denom = 2 * out_len
    lower = numer // denom
    frac = (numer - lower * denom).astype(jnp.float32) / denom
    below = numer < 0
    frac = jnp.where(below, jnp.float32(0.0), frac)
    lower = jnp.where(below, 0, lower)
    top_index = valid - 1
    over = lower >= top_index
    frac = jnp.where(over, jnp.float32(0.0), frac)
    lower = jnp.where(over, top_index, lower)
    columns = jnp.arange(in_len, dtype=jnp.int32)
    first = jnp.where(columns[None, :] == lower[:, None], 1.0 - frac[:, None], jnp.float32(0.0))
    second = jnp.where(columns[None, :] == lower[:, None] + 1, frac[:, None], jnp.float32(0.0))
    return (first + second).astype(jnp.bfloat16)


def run_conv(x_ref, w_ref, bias, lo, hi, good_cols, o_ref, width, block, head=None):
    flat = block * width
    place = lax.broadcasted_iota(jnp.int32, (1, flat), 1)
    col = place % width

    def step(i, carry):
        r0 = i * block
        taps = []
        for b in range(3):
            acc = None
            for a in range(3):
                start = pl.multiple_of((r0 + a) * width, width)
                xs = x_ref[:, pl.ds(start, flat)]
                d = jnp.dot(w_ref[a, b], xs, preferred_element_type=jnp.float32)
                acc = d if acc is None else acc + d
            taps.append(acc)
        left = jnp.where(col == 0, 0.0, pltpu.roll(taps[0], 1, 1))
        right = jnp.where(col == width - 1, 0.0, pltpu.roll(taps[2], flat - 1, 1))
        total = jnp.maximum(taps[1] + left + right + bias, 0.0)
        row = r0 + place // width
        keep = (row >= lo) & (row < hi) & (col < good_cols)
        out = jnp.where(keep, total, 0.0).astype(jnp.bfloat16)
        if head is not None:
            out = jnp.dot(head[0], out, preferred_element_type=jnp.float32) + head[1]
        o_ref[:, pl.ds(pl.multiple_of(r0 * width, width), flat)] = out.astype(o_ref.dtype)
        return carry

    lax.fori_loop(0, o_ref.shape[1] // flat, step, 0)


def first_body(main_ref, top_ref, low_ref, w_ref, b_ref, s_ref, o_ref, x_ref, *, width, block, halo):
    lo_in, hi_in, good_cols, lo, hi = s_ref[0], s_ref[1], s_ref[2], s_ref[3], s_ref[4]
    chans = main_ref.shape[0]
    rows_main = main_ref.shape[1] // width

    def put(src, offset, rows):
        place = lax.broadcasted_iota(jnp.int32, (1, rows * width), 1)
        row = offset + place // width
        keep = (row >= lo_in) & (row < hi_in) & (place % width < good_cols)
        x_ref[:, pl.ds(pl.multiple_of(offset * width, width), rows * width)] = jnp.where(
            keep, src, jnp.zeros_like(src)
        )

    put(top_ref[...], 0, halo)
    put(low_ref[...], halo + rows_main, halo)

    def chunk(i, carry):
        start = pl.multiple_of(i * 2 * width, width)
        put(main_ref[:, pl.ds(start, 2 * width)], halo + 2 * i, 2)
        return carry

    lax.fori_loop(0, rows_main // 2, chunk, 0)
    run_conv(x_ref, w_ref, b_ref[pl.ds(0, chans), :], lo, hi, good_cols, o_ref, width, block)


def second_body(x_ref, w_ref, b_ref, k_ref, s_ref, o_ref, *, width, block):
    chans = x_ref.shape[0]
    classes = k_ref.shape[0]
    head = (k_ref[...], b_ref[pl.ds(2 * chans, classes), :])
    lo, hi, good_cols = s_ref[3], s_ref[4], s_ref[2]
    run_conv(x_ref, w_ref, b_ref[pl.ds(chans, chans), :], lo, hi, good_cols, o_ref, width, block, head)


def pick_block(rows):
    return next(k for k in (4, 3, 2, 1) if rows % k == 0)


def conv_first_layer(feat, top, low, weights, biases, limits):
    chans, rows_main, width = feat.shape
    halo = top.shape[1]
    rows_in = rows_main + 2 * halo
    rows_out = rows_in - 2
    outs = weights.shape[2]
    block = pick_block(rows_out)
    vmem = pl.BlockSpec(memory_space=pltpu.VMEM)
    cost = pl.CostEstimate(
        flops=2 * 9 * rows_out * width * chans * outs,
        bytes_accessed=2 * (chans * rows_in * width + weights.size + rows_out * width * outs),
        transcendentals=0,
    )
    out = pl.pallas_call(
        functools.partial(first_body, width=width, block=block, halo=halo),
        out_shape=jax.ShapeDtypeStruct((outs, rows_out * width), jnp.bfloat16),
        in_specs=[vmem] * 5 + [pl.BlockSpec(memory_space=pltpu.SMEM)],
        out_specs=vmem,
        scratch_shapes=[pltpu.VMEM((chans, rows_in * width), jnp.bfloat16)],
        cost_estimate=cost,
    )(
        feat.reshape(chans, rows_main * width),
        top.reshape(chans, halo * width),
        low.reshape(chans, halo * width),
        weights,
        biases,
        limits,
    )
    return out


def conv_second_layer(x, width, weights, biases, head, limits):
    chans, flat_in = x.shape
    rows_out = flat_in // width - 2
    outs = weights.shape[2]
    classes = head.shape[0]
    block = pick_block(rows_out)
    vmem = pl.BlockSpec(memory_space=pltpu.VMEM)
    cost = pl.CostEstimate(
        flops=2 * 9 * rows_out * width * chans * outs + 2 * rows_out * width * outs * classes,
        bytes_accessed=2 * (x.size + weights.size + rows_out * width * classes),
        transcendentals=0,
    )
    out = pl.pallas_call(
        functools.partial(second_body, width=width, block=block),
        out_shape=jax.ShapeDtypeStruct((classes, rows_out * width), jnp.bfloat16),
        in_specs=[vmem] * 4 + [pl.BlockSpec(memory_space=pltpu.SMEM)],
        out_specs=vmem,
        cost_estimate=cost,
    )(x, weights, biases, head, limits)
    return out.reshape(classes, rows_out, width)


def window_start(numer, first_row, full_rows, out_rows, window_rows):
    valid = full_rows * numer // 14
    numer_pos = (2 * first_row + 1) * valid - out_rows
    lower = numer_pos // (2 * out_rows)
    lower = jnp.where(numer_pos < 0, 0, lower)
    lower = jnp.where(lower >= valid - 1, valid - 1, lower)
    return jnp.clip(lower, 0, full_rows - window_rows)


def column_table(numer, flip, cols, out_cols):
    valid_cols = cols * numer // 14
    col_pos = jnp.arange(out_cols, dtype=jnp.int32)
    col_pos = jnp.where(flip == 1, out_cols - 1 - col_pos, col_pos)
    return resize_matrix(col_pos, out_cols, valid_cols, cols)


def shards(features, views, conv_first, bias_first, conv_second, bias_second, classify, class_bias):
    feat = features[0]
    rows_dev, cols = (feat.shape[1], feat.shape[2])
    spaces = lax.axis_size("space")
    full_rows = rows_dev * spaces
    place = lax.axis_index("space")
    member_index = lax.axis_index("member")
    members = views.shape[0]
    picked = jnp.arange(members, dtype=jnp.int32) == member_index
    code = jnp.sum(jnp.where(picked, views, 0))
    numer = code // 2
    valid_rows = full_rows * numer // 14
    valid_cols = cols * numer // 14
    count = lax.axis_size("space")
    halo = 2
    forward = [(i, i + 1) for i in range(count - 1)]
    backward = [(target, source) for source, target in forward]
    top_rows = lax.ppermute(lax.slice_in_dim(feat, rows_dev - halo, None, axis=1), "space", forward)
    low_rows = lax.ppermute(lax.slice_in_dim(feat, 0, halo, axis=1), "space", backward)
    top = place * rows_dev
    limits = jnp.stack(
        [halo - top, valid_rows - top + halo, valid_cols, 1 - top, valid_rows - top + 1, -top, valid_rows - top]
    ).astype(jnp.int32)
    limits_second = limits[jnp.array([0, 1, 2, 5, 6])]
    biases = jnp.concatenate([bias_first, bias_second, class_bias]).reshape(-1, 1)
    hidden = conv_first_layer(feat, top_rows, low_rows, conv_first, biases, limits[:5])
    logits = conv_second_layer(hidden, cols, conv_second, biases, classify, limits_second)
    out_rows = UP * full_rows
    out_cols = UP * cols
    own_rows = out_rows // spaces
    part_rows = own_rows // members
    window_rows = (part_rows - 1) // UP + 3
    gathered = gather_rows(logits, "space")
    pieces = []
    for target in range(members):
        first_row = place * own_rows + target * part_rows
        begin = window_start(numer, first_row, full_rows, out_rows, window_rows)
        pieces.append(lax.dynamic_slice_in_dim(gathered, begin, window_rows, 1))
    outgoing = jnp.stack(pieces, 0)
    own_first = place * own_rows + member_index * part_rows
    positions = own_first + jnp.arange(part_rows, dtype=jnp.int32)
    result = jnp.zeros((part_rows, logits.shape[0], out_cols), jnp.float32)
    for shift in range(members):
        if shift == 0:
            arrived = lax.dynamic_index_in_dim(outgoing, member_index, 0, keepdims=False)
        else:
            send = lax.dynamic_index_in_dim(
                outgoing, (member_index + shift) % members, 0, keepdims=False
            )
            arrived = lax.ppermute(
                send, "member", [(i, (i + shift) % members) for i in range(members)]
            )
        source = (member_index - shift) % members
        source_code = jnp.sum(jnp.where(jnp.arange(members) == source, views, 0))
        source_numer = source_code // 2
        source_flip = source_code % 2
        source_valid = full_rows * source_numer // 14
        begin = window_start(source_numer, own_first, full_rows, out_rows, window_rows)
        source_cols = column_table(source_numer, source_flip, cols, out_cols)
        row_table = resize_matrix(positions, out_rows, source_valid, full_rows)
        row_part = lax.dynamic_slice_in_dim(row_table, begin, window_rows, 1)
        widened = jnp.einsum(
            "cyx,jx->cyj", arrived, source_cols, preferred_element_type=jnp.float32
        ).astype(jnp.bfloat16)
        result = result + jnp.einsum(
            "iy,cyj->icj", row_part, widened, preferred_element_type=jnp.float32
        )
    return result


def solution(mesh):
    placed = (
        P(("groups", "member"), None, "space", None),
        P("groups"),
        P(),
        P(),
        P(),
        P(),
        P(),
        P(),
    )
    return jax.shard_map(
        shards,
        mesh=mesh,
        in_specs=placed,
        out_specs=P(("groups", "space", "member"), None, None),
        check_vma=False,
    )
```

```python
import functools

import jax
import jax.numpy as jnp
from jax import lax
from jax.experimental import pallas as pl
from jax.experimental.pallas import tpu as pltpu
from jax.sharding import PartitionSpec as P

UP = 4


def with_halo(block, sides, width):
    for axis, dim in sides:
        count = lax.axis_size(axis)
        forward = [(i, i + 1) for i in range(count - 1)]
        backward = [(target, source) for source, target in forward]
        low = lax.ppermute(
            lax.slice_in_dim(block, block.shape[dim] - width, None, axis=dim), axis, forward
        )
        high = lax.ppermute(lax.slice_in_dim(block, 0, width, axis=dim), axis, backward)
        block = jnp.concatenate([low, block, high], axis=dim)
    return block


def gather_rows(block, axis):
    count = lax.axis_size(axis)
    if count & (count - 1):
        return lax.all_gather(block, axis, axis=1, tiled=True)
    me = lax.axis_index(axis)
    lead, rows, rest = block.shape[0], block.shape[1], block.shape[2:]
    held = block[:, None]
    bit = count // 2
    while bit:
        other = lax.ppermute(held, axis, [(i, i ^ bit) for i in range(count)])
        upper = (me & bit) != 0
        held = jnp.where(upper, jnp.stack([other, held], 2), jnp.stack([held, other], 2))
        held = held.reshape((lead, -1, rows) + rest)
        bit //= 2
    return held.reshape((lead, count * rows) + rest)


def resize_matrix(positions, out_len, valid, in_len):
    numer = (2 * positions + 1) * valid - out_len
    denom = 2 * out_len
    lower = numer // denom
    frac = (numer - lower * denom).astype(jnp.float32) / denom
    below = numer < 0
    frac = jnp.where(below, jnp.float32(0.0), frac)
    lower = jnp.where(below, 0, lower)
    top_index = valid - 1
    over = lower >= top_index
    frac = jnp.where(over, jnp.float32(0.0), frac)
    lower = jnp.where(over, top_index, lower)
    columns = jnp.arange(in_len, dtype=jnp.int32)
    first = jnp.where(columns[None, :] == lower[:, None], 1.0 - frac[:, None], jnp.float32(0.0))
    second = jnp.where(columns[None, :] == lower[:, None] + 1, frac[:, None], jnp.float32(0.0))
    return (first + second).astype(jnp.bfloat16)


def run_conv(x_ref, w_ref, bias, lo, hi, good_cols, o_ref, width, block, head=None):
    flat = block * width
    outs = w_ref.shape[2]
    place = lax.broadcasted_iota(jnp.int32, (1, flat), 1)
    col = place % width
    stacked = jnp.concatenate(
        [jnp.concatenate([w_ref[a, b] for a in range(3)], axis=1) for b in range(3)], axis=0
    )

    def step(i, carry):
        r0 = i * block
        rhs = jnp.concatenate(
            [x_ref[:, pl.ds(pl.multiple_of((r0 + a) * width, width), flat)] for a in range(3)],
            axis=0,
        )
        res = jnp.dot(stacked, rhs, preferred_element_type=jnp.float32)
        taps = [res[b * outs:(b + 1) * outs] for b in range(3)]
        left = jnp.where(col == 0, 0.0, pltpu.roll(taps[0], 1, 1))
        right = jnp.where(col == width - 1, 0.0, pltpu.roll(taps[2], flat - 1, 1))
        total = jnp.maximum(taps[1] + left + right + bias, 0.0)
        row = r0 + place // width
        keep = (row >= lo) & (row < hi) & (col < good_cols)
        out = jnp.where(keep, total, 0.0).astype(jnp.bfloat16)
        if head is not None:
            out = jnp.dot(head[0], out, preferred_element_type=jnp.float32) + head[1]
        o_ref[:, pl.ds(pl.multiple_of(r0 * width, width), flat)] = out.astype(o_ref.dtype)
        return carry

    lax.fori_loop(0, o_ref.shape[1] // flat, step, 0)


def first_body(main_ref, top_ref, low_ref, w_ref, b_ref, s_ref, o_ref, x_ref, *, width, block, halo):
    lo_in, hi_in, good_cols, lo, hi = s_ref[0], s_ref[1], s_ref[2], s_ref[3], s_ref[4]
    chans = main_ref.shape[0]
    rows_main = main_ref.shape[1] // width

    def put(src, offset, rows):
        place = lax.broadcasted_iota(jnp.int32, (1, rows * width), 1)
        row = offset + place // width
        keep = (row >= lo_in) & (row < hi_in) & (place % width < good_cols)
        x_ref[:, pl.ds(pl.multiple_of(offset * width, width), rows * width)] = jnp.where(
            keep, src, jnp.zeros_like(src)
        )

    put(top_ref[...], 0, halo)
    put(low_ref[...], halo + rows_main, halo)

    def chunk(i, carry):
        start = pl.multiple_of(i * 2 * width, width)
        put(main_ref[:, pl.ds(start, 2 * width)], halo + 2 * i, 2)
        return carry

    lax.fori_loop(0, rows_main // 2, chunk, 0)
    run_conv(x_ref, w_ref, b_ref[pl.ds(0, chans), :], lo, hi, good_cols, o_ref, width, block)


def second_body(x_ref, w_ref, b_ref, k_ref, s_ref, o_ref, *, width, block):
    chans = x_ref.shape[0]
    classes = k_ref.shape[0]
    head = (k_ref[...], b_ref[pl.ds(2 * chans, classes), :])
    lo, hi, good_cols = s_ref[3], s_ref[4], s_ref[2]
    run_conv(x_ref, w_ref, b_ref[pl.ds(chans, chans), :], lo, hi, good_cols, o_ref, width, block, head)


def pick_block(rows):
    return next(k for k in (4, 3, 2, 1) if rows % k == 0)


def conv_first_layer(feat, top, low, weights, biases, limits):
    chans, rows_main, width = feat.shape
    halo = top.shape[1]
    rows_in = rows_main + 2 * halo
    rows_out = rows_in - 2
    outs = weights.shape[2]
    block = pick_block(rows_out)
    vmem = pl.BlockSpec(memory_space=pltpu.VMEM)
    cost = pl.CostEstimate(
        flops=2 * 9 * rows_out * width * chans * outs,
        bytes_accessed=2 * (chans * rows_in * width + weights.size + rows_out * width * outs),
        transcendentals=0,
    )
    out = pl.pallas_call(
        functools.partial(first_body, width=width, block=block, halo=halo),
        out_shape=jax.ShapeDtypeStruct((outs, rows_out * width), jnp.bfloat16),
        in_specs=[vmem] * 5 + [pl.BlockSpec(memory_space=pltpu.SMEM)],
        out_specs=vmem,
        scratch_shapes=[pltpu.VMEM((chans, rows_in * width), jnp.bfloat16)],
        cost_estimate=cost,
    )(
        feat.reshape(chans, rows_main * width),
        top.reshape(chans, halo * width),
        low.reshape(chans, halo * width),
        weights,
        biases,
        limits,
    )
    return out


def conv_second_layer(x, width, weights, biases, head, limits):
    chans, flat_in = x.shape
    rows_out = flat_in // width - 2
    outs = weights.shape[2]
    classes = head.shape[0]
    block = pick_block(rows_out)
    vmem = pl.BlockSpec(memory_space=pltpu.VMEM)
    cost = pl.CostEstimate(
        flops=2 * 9 * rows_out * width * chans * outs + 2 * rows_out * width * outs * classes,
        bytes_accessed=2 * (x.size + weights.size + rows_out * width * classes),
        transcendentals=0,
    )
    out = pl.pallas_call(
        functools.partial(second_body, width=width, block=block),
        out_shape=jax.ShapeDtypeStruct((classes, rows_out * width), jnp.bfloat16),
        in_specs=[vmem] * 4 + [pl.BlockSpec(memory_space=pltpu.SMEM)],
        out_specs=vmem,
        cost_estimate=cost,
    )(x, weights, biases, head, limits)
    return out.reshape(classes, rows_out, width)


def window_start(numer, first_row, full_rows, out_rows, window_rows):
    valid = full_rows * numer // 14
    numer_pos = (2 * first_row + 1) * valid - out_rows
    lower = numer_pos // (2 * out_rows)
    lower = jnp.where(numer_pos < 0, 0, lower)
    lower = jnp.where(lower >= valid - 1, valid - 1, lower)
    return jnp.clip(lower, 0, full_rows - window_rows)


def column_table(numer, flip, cols, out_cols):
    valid_cols = cols * numer // 14
    col_pos = jnp.arange(out_cols, dtype=jnp.int32)
    col_pos = jnp.where(flip == 1, out_cols - 1 - col_pos, col_pos)
    return resize_matrix(col_pos, out_cols, valid_cols, cols)


def shards(features, views, conv_first, bias_first, conv_second, bias_second, classify, class_bias):
    feat = features[0]
    rows_dev, cols = (feat.shape[1], feat.shape[2])
    spaces = lax.axis_size("space")
    full_rows = rows_dev * spaces
    place = lax.axis_index("space")
    member_index = lax.axis_index("member")
    members = views.shape[0]
    picked = jnp.arange(members, dtype=jnp.int32) == member_index
    code = jnp.sum(jnp.where(picked, views, 0))
    numer = code // 2
    valid_rows = full_rows * numer // 14
    valid_cols = cols * numer // 14
    count = lax.axis_size("space")
    halo = 2
    forward = [(i, i + 1) for i in range(count - 1)]
    backward = [(target, source) for source, target in forward]
    top_rows = lax.ppermute(lax.slice_in_dim(feat, rows_dev - halo, None, axis=1), "space", forward)
    low_rows = lax.ppermute(lax.slice_in_dim(feat, 0, halo, axis=1), "space", backward)
    top = place * rows_dev
    limits = jnp.stack(
        [halo - top, valid_rows - top + halo, valid_cols, 1 - top, valid_rows - top + 1, -top, valid_rows - top]
    ).astype(jnp.int32)
    limits_second = limits[jnp.array([0, 1, 2, 5, 6])]
    biases = jnp.concatenate([bias_first, bias_second, class_bias]).reshape(-1, 1)
    hidden = conv_first_layer(feat, top_rows, low_rows, conv_first, biases, limits[:5])
    logits = conv_second_layer(hidden, cols, conv_second, biases, classify, limits_second)
    out_rows = UP * full_rows
    out_cols = UP * cols
    own_rows = out_rows // spaces
    part_rows = own_rows // members
    window_rows = (part_rows - 1) // UP + 3
    gathered = gather_rows(logits, "space")
    pieces = []
    for target in range(members):
        first_row = place * own_rows + target * part_rows
        begin = window_start(numer, first_row, full_rows, out_rows, window_rows)
        pieces.append(lax.dynamic_slice_in_dim(gathered, begin, window_rows, 1))
    outgoing = jnp.stack(pieces, 0)
    own_first = place * own_rows + member_index * part_rows
    positions = own_first + jnp.arange(part_rows, dtype=jnp.int32)
    result = jnp.zeros((part_rows, logits.shape[0], out_cols), jnp.float32)
    for shift in range(members):
        if shift == 0:
            arrived = lax.dynamic_index_in_dim(outgoing, member_index, 0, keepdims=False)
        else:
            send = lax.dynamic_index_in_dim(
                outgoing, (member_index + shift) % members, 0, keepdims=False
            )
            arrived = lax.ppermute(
                send, "member", [(i, (i + shift) % members) for i in range(members)]
            )
        source = (member_index - shift) % members
        source_code = jnp.sum(jnp.where(jnp.arange(members) == source, views, 0))
        source_numer = source_code // 2
        source_flip = source_code % 2
        source_valid = full_rows * source_numer // 14
        begin = window_start(source_numer, own_first, full_rows, out_rows, window_rows)
        source_cols = column_table(source_numer, source_flip, cols, out_cols)
        row_table = resize_matrix(positions, out_rows, source_valid, full_rows)
        row_part = lax.dynamic_slice_in_dim(row_table, begin, window_rows, 1)
        widened = jnp.einsum(
            "cyx,jx->cyj", arrived, source_cols, preferred_element_type=jnp.float32
        ).astype(jnp.bfloat16)
        result = result + jnp.einsum(
            "iy,cyj->icj", row_part, widened, preferred_element_type=jnp.float32
        )
    return result


def solution(mesh):
    placed = (
        P(("groups", "member"), None, "space", None),
        P("groups"),
        P(),
        P(),
        P(),
        P(),
        P(),
        P(),
    )
    return jax.shard_map(
        shards,
        mesh=mesh,
        in_specs=placed,
        out_specs=P(("groups", "space", "member"), None, None),
        check_vma=False,
    )
```

```python
import functools

import jax
import jax.numpy as jnp
from jax import lax
from jax.experimental import pallas as pl
from jax.experimental.pallas import tpu as pltpu
from jax.sharding import PartitionSpec as P

UP = 4


def with_halo(block, sides, width):
    for axis, dim in sides:
        count = lax.axis_size(axis)
        forward = [(i, i + 1) for i in range(count - 1)]
        backward = [(target, source) for source, target in forward]
        low = lax.ppermute(
            lax.slice_in_dim(block, block.shape[dim] - width, None, axis=dim), axis, forward
        )
        high = lax.ppermute(lax.slice_in_dim(block, 0, width, axis=dim), axis, backward)
        block = jnp.concatenate([low, block, high], axis=dim)
    return block


def gather_rows(block, axis):
    count = lax.axis_size(axis)
    if count & (count - 1):
        return lax.all_gather(block, axis, axis=1, tiled=True)
    me = lax.axis_index(axis)
    lead, rows, rest = block.shape[0], block.shape[1], block.shape[2:]
    held = block[:, None]
    bit = count // 2
    while bit:
        other = lax.ppermute(held, axis, [(i, i ^ bit) for i in range(count)])
        upper = (me & bit) != 0
        held = jnp.where(upper, jnp.stack([other, held], 2), jnp.stack([held, other], 2))
        held = held.reshape((lead, -1, rows) + rest)
        bit //= 2
    return held.reshape((lead, count * rows) + rest)


def resize_matrix(positions, out_len, valid, in_len):
    numer = (2 * positions + 1) * valid - out_len
    denom = 2 * out_len
    lower = numer // denom
    frac = (numer - lower * denom).astype(jnp.float32) / denom
    below = numer < 0
    frac = jnp.where(below, jnp.float32(0.0), frac)
    lower = jnp.where(below, 0, lower)
    top_index = valid - 1
    over = lower >= top_index
    frac = jnp.where(over, jnp.float32(0.0), frac)
    lower = jnp.where(over, top_index, lower)
    columns = jnp.arange(in_len, dtype=jnp.int32)
    first = jnp.where(columns[None, :] == lower[:, None], 1.0 - frac[:, None], jnp.float32(0.0))
    second = jnp.where(columns[None, :] == lower[:, None] + 1, frac[:, None], jnp.float32(0.0))
    return (first + second).astype(jnp.bfloat16)


def run_conv(x_ref, w_ref, bias, lo, hi, good_cols, o_ref, width, block, head=None):
    flat = block * width
    outs = w_ref.shape[2]
    place = lax.broadcasted_iota(jnp.int32, (1, flat), 1)
    col = place % width
    stacked = jnp.concatenate(
        [jnp.concatenate([w_ref[a, b] for a in range(3)], axis=1) for b in range(3)], axis=0
    )

    def step(i, carry):
        r0 = i * block
        rhs = jnp.concatenate(
            [x_ref[:, pl.ds(pl.multiple_of((r0 + a) * width, width), flat)] for a in range(3)],
            axis=0,
        )
        res = jnp.dot(stacked, rhs, preferred_element_type=jnp.float32)
        taps = [res[b * outs:(b + 1) * outs] for b in range(3)]
        left = jnp.where(col == 0, 0.0, pltpu.roll(taps[0], 1, 1))
        right = jnp.where(col == width - 1, 0.0, pltpu.roll(taps[2], flat - 1, 1))
        total = jnp.maximum(taps[1] + left + right + bias, 0.0)
        row = r0 + place // width
        keep = (row >= lo) & (row < hi) & (col < good_cols)
        out = jnp.where(keep, total, 0.0).astype(jnp.bfloat16)
        if head is not None:
            out = jnp.dot(head[0], out, preferred_element_type=jnp.float32) + head[1]
        o_ref[:, pl.ds(pl.multiple_of(r0 * width, width), flat)] = out.astype(o_ref.dtype)
        return carry

    lax.fori_loop(0, o_ref.shape[1] // flat, step, 0, unroll=True)


def first_body(main_ref, top_ref, low_ref, w_ref, b_ref, s_ref, o_ref, x_ref, *, width, block, halo):
    lo_in, hi_in, good_cols, lo, hi = s_ref[0], s_ref[1], s_ref[2], s_ref[3], s_ref[4]
    chans = main_ref.shape[0]
    rows_main = main_ref.shape[1] // width

    def put(src, offset, rows):
        place = lax.broadcasted_iota(jnp.int32, (1, rows * width), 1)
        row = offset + place // width
        keep = (row >= lo_in) & (row < hi_in) & (place % width < good_cols)
        x_ref[:, pl.ds(pl.multiple_of(offset * width, width), rows * width)] = jnp.where(
            keep, src, jnp.zeros_like(src)
        )

    put(top_ref[...], 0, halo)
    put(low_ref[...], halo + rows_main, halo)

    def chunk(i, carry):
        start = pl.multiple_of(i * 2 * width, width)
        put(main_ref[:, pl.ds(start, 2 * width)], halo + 2 * i, 2)
        return carry

    lax.fori_loop(0, rows_main // 2, chunk, 0)
    run_conv(x_ref, w_ref, b_ref[pl.ds(0, chans), :], lo, hi, good_cols, o_ref, width, block)


def second_body(x_ref, w_ref, b_ref, k_ref, s_ref, o_ref, *, width, block):
    chans = x_ref.shape[0]
    classes = k_ref.shape[0]
    head = (k_ref[...], b_ref[pl.ds(2 * chans, classes), :])
    lo, hi, good_cols = s_ref[3], s_ref[4], s_ref[2]
    run_conv(x_ref, w_ref, b_ref[pl.ds(chans, chans), :], lo, hi, good_cols, o_ref, width, block, head)


def pick_block(rows):
    return next(k for k in (4, 3, 2, 1) if rows % k == 0)


def conv_first_layer(feat, top, low, weights, biases, limits):
    chans, rows_main, width = feat.shape
    halo = top.shape[1]
    rows_in = rows_main + 2 * halo
    rows_out = rows_in - 2
    outs = weights.shape[2]
    block = pick_block(rows_out)
    vmem = pl.BlockSpec(memory_space=pltpu.VMEM)
    cost = pl.CostEstimate(
        flops=2 * 9 * rows_out * width * chans * outs,
        bytes_accessed=2 * (chans * rows_in * width + weights.size + rows_out * width * outs),
        transcendentals=0,
    )
    out = pl.pallas_call(
        functools.partial(first_body, width=width, block=block, halo=halo),
        out_shape=jax.ShapeDtypeStruct((outs, rows_out * width), jnp.bfloat16),
        in_specs=[vmem] * 5 + [pl.BlockSpec(memory_space=pltpu.SMEM)],
        out_specs=vmem,
        scratch_shapes=[pltpu.VMEM((chans, rows_in * width), jnp.bfloat16)],
        cost_estimate=cost,
    )(
        feat.reshape(chans, rows_main * width),
        top.reshape(chans, halo * width),
        low.reshape(chans, halo * width),
        weights,
        biases,
        limits,
    )
    return out


def conv_second_layer(x, width, weights, biases, head, limits):
    chans, flat_in = x.shape
    rows_out = flat_in // width - 2
    outs = weights.shape[2]
    classes = head.shape[0]
    block = pick_block(rows_out)
    vmem = pl.BlockSpec(memory_space=pltpu.VMEM)
    cost = pl.CostEstimate(
        flops=2 * 9 * rows_out * width * chans * outs + 2 * rows_out * width * outs * classes,
        bytes_accessed=2 * (x.size + weights.size + rows_out * width * classes),
        transcendentals=0,
    )
    out = pl.pallas_call(
        functools.partial(second_body, width=width, block=block),
        out_shape=jax.ShapeDtypeStruct((classes, rows_out * width), jnp.bfloat16),
        in_specs=[vmem] * 4 + [pl.BlockSpec(memory_space=pltpu.SMEM)],
        out_specs=vmem,
        cost_estimate=cost,
    )(x, weights, biases, head, limits)
    return out.reshape(classes, rows_out, width)


def window_start(numer, first_row, full_rows, out_rows, window_rows):
    valid = full_rows * numer // 14
    numer_pos = (2 * first_row + 1) * valid - out_rows
    lower = numer_pos // (2 * out_rows)
    lower = jnp.where(numer_pos < 0, 0, lower)
    lower = jnp.where(lower >= valid - 1, valid - 1, lower)
    return jnp.clip(lower, 0, full_rows - window_rows)


def column_table(numer, flip, cols, out_cols):
    valid_cols = cols * numer // 14
    col_pos = jnp.arange(out_cols, dtype=jnp.int32)
    col_pos = jnp.where(flip == 1, out_cols - 1 - col_pos, col_pos)
    return resize_matrix(col_pos, out_cols, valid_cols, cols)


def shards(features, views, conv_first, bias_first, conv_second, bias_second, classify, class_bias):
    feat = features[0]
    rows_dev, cols = (feat.shape[1], feat.shape[2])
    spaces = lax.axis_size("space")
    full_rows = rows_dev * spaces
    place = lax.axis_index("space")
    member_index = lax.axis_index("member")
    members = views.shape[0]
    picked = jnp.arange(members, dtype=jnp.int32) == member_index
    code = jnp.sum(jnp.where(picked, views, 0))
    numer = code // 2
    valid_rows = full_rows * numer // 14
    valid_cols = cols * numer // 14
    count = lax.axis_size("space")
    halo = 2
    forward = [(i, i + 1) for i in range(count - 1)]
    backward = [(target, source) for source, target in forward]
    top_rows = lax.ppermute(lax.slice_in_dim(feat, rows_dev - halo, None, axis=1), "space", forward)
    low_rows = lax.ppermute(lax.slice_in_dim(feat, 0, halo, axis=1), "space", backward)
    top = place * rows_dev
    limits = jnp.stack(
        [halo - top, valid_rows - top + halo, valid_cols, 1 - top, valid_rows - top + 1, -top, valid_rows - top]
    ).astype(jnp.int32)
    limits_second = limits[jnp.array([0, 1, 2, 5, 6])]
    biases = jnp.concatenate([bias_first, bias_second, class_bias]).reshape(-1, 1)
    hidden = conv_first_layer(feat, top_rows, low_rows, conv_first, biases, limits[:5])
    logits = conv_second_layer(hidden, cols, conv_second, biases, classify, limits_second)
    out_rows = UP * full_rows
    out_cols = UP * cols
    own_rows = out_rows // spaces
    part_rows = own_rows // members
    window_rows = (part_rows - 1) // UP + 3
    gathered = gather_rows(logits, "space")
    pieces = []
    for target in range(members):
        first_row = place * own_rows + target * part_rows
        begin = window_start(numer, first_row, full_rows, out_rows, window_rows)
        pieces.append(lax.dynamic_slice_in_dim(gathered, begin, window_rows, 1))
    outgoing = jnp.stack(pieces, 0)
    own_first = place * own_rows + member_index * part_rows
    positions = own_first + jnp.arange(part_rows, dtype=jnp.int32)
    result = jnp.zeros((part_rows, logits.shape[0], out_cols), jnp.float32)
    for shift in range(members):
        if shift == 0:
            arrived = lax.dynamic_index_in_dim(outgoing, member_index, 0, keepdims=False)
        else:
            send = lax.dynamic_index_in_dim(
                outgoing, (member_index + shift) % members, 0, keepdims=False
            )
            arrived = lax.ppermute(
                send, "member", [(i, (i + shift) % members) for i in range(members)]
            )
        source = (member_index - shift) % members
        source_code = jnp.sum(jnp.where(jnp.arange(members) == source, views, 0))
        source_numer = source_code // 2
        source_flip = source_code % 2
        source_valid = full_rows * source_numer // 14
        begin = window_start(source_numer, own_first, full_rows, out_rows, window_rows)
        source_cols = column_table(source_numer, source_flip, cols, out_cols)
        row_table = resize_matrix(positions, out_rows, source_valid, full_rows)
        row_part = lax.dynamic_slice_in_dim(row_table, begin, window_rows, 1)
        widened = jnp.einsum(
            "cyx,jx->cyj", arrived, source_cols, preferred_element_type=jnp.float32
        ).astype(jnp.bfloat16)
        result = result + jnp.einsum(
            "iy,cyj->icj", row_part, widened, preferred_element_type=jnp.float32
        )
    return result


def solution(mesh):
    placed = (
        P(("groups", "member"), None, "space", None),
        P("groups"),
        P(),
        P(),
        P(),
        P(),
        P(),
        P(),
    )
    return jax.shard_map(
        shards,
        mesh=mesh,
        in_specs=placed,
        out_specs=P(("groups", "space", "member"), None, None),
        check_vma=False,
    )
```

```python
import functools

import jax
import jax.numpy as jnp
from jax import lax
from jax.experimental import pallas as pl
from jax.experimental.pallas import tpu as pltpu
from jax.sharding import PartitionSpec as P

UP = 4


def with_halo(block, sides, width):
    for axis, dim in sides:
        count = lax.axis_size(axis)
        forward = [(i, i + 1) for i in range(count - 1)]
        backward = [(target, source) for source, target in forward]
        low = lax.ppermute(
            lax.slice_in_dim(block, block.shape[dim] - width, None, axis=dim), axis, forward
        )
        high = lax.ppermute(lax.slice_in_dim(block, 0, width, axis=dim), axis, backward)
        block = jnp.concatenate([low, block, high], axis=dim)
    return block


def gather_rows(block, axis):
    count = lax.axis_size(axis)
    if count & (count - 1):
        return lax.all_gather(block, axis, axis=1, tiled=True)
    me = lax.axis_index(axis)
    lead, rows, rest = block.shape[0], block.shape[1], block.shape[2:]
    held = block[:, None]
    bit = count // 2
    while bit:
        other = lax.ppermute(held, axis, [(i, i ^ bit) for i in range(count)])
        upper = (me & bit) != 0
        held = jnp.where(upper, jnp.stack([other, held], 2), jnp.stack([held, other], 2))
        held = held.reshape((lead, -1, rows) + rest)
        bit //= 2
    return held.reshape((lead, count * rows) + rest)


def resize_matrix(positions, out_len, valid, in_len):
    numer = (2 * positions + 1) * valid - out_len
    denom = 2 * out_len
    lower = numer // denom
    frac = (numer - lower * denom).astype(jnp.float32) / denom
    below = numer < 0
    frac = jnp.where(below, jnp.float32(0.0), frac)
    lower = jnp.where(below, 0, lower)
    top_index = valid - 1
    over = lower >= top_index
    frac = jnp.where(over, jnp.float32(0.0), frac)
    lower = jnp.where(over, top_index, lower)
    columns = jnp.arange(in_len, dtype=jnp.int32)
    first = jnp.where(columns[None, :] == lower[:, None], 1.0 - frac[:, None], jnp.float32(0.0))
    second = jnp.where(columns[None, :] == lower[:, None] + 1, frac[:, None], jnp.float32(0.0))
    return (first + second).astype(jnp.bfloat16)


def run_conv(x_ref, w_ref, bias, lo, hi, good_cols, o_ref, width, block, head=None):
    flat = block * width
    outs = w_ref.shape[2]
    place = lax.broadcasted_iota(jnp.int32, (1, flat), 1)
    col = place % width
    stacked = jnp.concatenate(
        [jnp.concatenate([w_ref[a, b] for a in range(3)], axis=1) for b in range(3)], axis=0
    )

    def step(i, carry):
        r0 = i * block
        rhs = jnp.concatenate(
            [x_ref[:, pl.ds(pl.multiple_of((r0 + a) * width, width), flat)] for a in range(3)],
            axis=0,
        )
        res = jnp.dot(stacked, rhs, preferred_element_type=jnp.float32)
        taps = [res[b * outs:(b + 1) * outs] for b in range(3)]
        left = jnp.where(col == 0, 0.0, pltpu.roll(taps[0], 1, 1))
        right = jnp.where(col == width - 1, 0.0, pltpu.roll(taps[2], flat - 1, 1))
        total = jnp.maximum(taps[1] + left + right + bias, 0.0)
        row = r0 + place // width
        keep = (row >= lo) & (row < hi) & (col < good_cols)
        out = jnp.where(keep, total, 0.0).astype(jnp.bfloat16)
        if head is not None:
            out = jnp.dot(head[0], out, preferred_element_type=jnp.float32) + head[1]
        o_ref[:, pl.ds(pl.multiple_of(r0 * width, width), flat)] = out.astype(o_ref.dtype)
        return carry

    lax.fori_loop(0, o_ref.shape[1] // flat, step, 0, unroll=True)


def first_body(main_ref, top_ref, low_ref, w_ref, b_ref, s_ref, o_ref, x_ref, *, width, block, halo):
    lo_in, hi_in, good_cols, lo, hi = s_ref[0], s_ref[1], s_ref[2], s_ref[3], s_ref[4]
    chans = main_ref.shape[0]
    rows_main = main_ref.shape[1] // width

    def put(src, offset, rows):
        place = lax.broadcasted_iota(jnp.int32, (1, rows * width), 1)
        row = offset + place // width
        keep = (row >= lo_in) & (row < hi_in) & (place % width < good_cols)
        x_ref[:, pl.ds(pl.multiple_of(offset * width, width), rows * width)] = jnp.where(
            keep, src, jnp.zeros_like(src)
        )

    put(top_ref[...], 0, halo)
    put(low_ref[...], halo + rows_main, halo)

    def chunk(i, carry):
        start = pl.multiple_of(i * 2 * width, width)
        put(main_ref[:, pl.ds(start, 2 * width)], halo + 2 * i, 2)
        return carry

    lax.fori_loop(0, rows_main // 2, chunk, 0)
    run_conv(x_ref, w_ref, b_ref[pl.ds(0, chans), :], lo, hi, good_cols, o_ref, width, block)


def second_body(x_ref, w_ref, b_ref, k_ref, s_ref, o_ref, *, width, block):
    chans = x_ref.shape[0]
    classes = k_ref.shape[0]
    head = (k_ref[...], b_ref[pl.ds(2 * chans, classes), :])
    lo, hi, good_cols = s_ref[5], s_ref[6], s_ref[2]
    run_conv(x_ref, w_ref, b_ref[pl.ds(chans, chans), :], lo, hi, good_cols, o_ref, width, block, head)


def pick_block(rows):
    return next(k for k in (4, 3, 2, 1) if rows % k == 0)


def conv_first_layer(feat, top, low, width, weights, biases, limits):
    chans = feat.shape[0]
    rows_main = feat.shape[1] // width
    halo = top.shape[1] // width
    rows_in = rows_main + 2 * halo
    rows_out = rows_in - 2
    outs = weights.shape[2]
    block = pick_block(rows_out)
    vmem = pl.BlockSpec(memory_space=pltpu.VMEM)
    cost = pl.CostEstimate(
        flops=2 * 9 * rows_out * width * chans * outs,
        bytes_accessed=2 * (chans * rows_in * width + weights.size + rows_out * width * outs),
        transcendentals=0,
    )
    out = pl.pallas_call(
        functools.partial(first_body, width=width, block=block, halo=halo),
        out_shape=jax.ShapeDtypeStruct((outs, rows_out * width), jnp.bfloat16),
        in_specs=[vmem] * 5 + [pl.BlockSpec(memory_space=pltpu.SMEM)],
        out_specs=vmem,
        scratch_shapes=[pltpu.VMEM((chans, rows_in * width), jnp.bfloat16)],
        cost_estimate=cost,
    )(
        feat,
        top,
        low,
        weights,
        biases,
        limits,
    )
    return out


def conv_second_layer(x, width, weights, biases, head, limits):
    chans, flat_in = x.shape
    rows_out = flat_in // width - 2
    outs = weights.shape[2]
    classes = head.shape[0]
    block = pick_block(rows_out)
    vmem = pl.BlockSpec(memory_space=pltpu.VMEM)
    cost = pl.CostEstimate(
        flops=2 * 9 * rows_out * width * chans * outs + 2 * rows_out * width * outs * classes,
        bytes_accessed=2 * (x.size + weights.size + rows_out * width * classes),
        transcendentals=0,
    )
    out = pl.pallas_call(
        functools.partial(second_body, width=width, block=block),
        out_shape=jax.ShapeDtypeStruct((classes, rows_out * width), jnp.bfloat16),
        in_specs=[vmem] * 4 + [pl.BlockSpec(memory_space=pltpu.SMEM)],
        out_specs=vmem,
        cost_estimate=cost,
    )(x, weights, biases, head, limits)
    return out.reshape(classes, rows_out, width)


def window_start(numer, first_row, full_rows, out_rows, window_rows):
    valid = full_rows * numer // 14
    numer_pos = (2 * first_row + 1) * valid - out_rows
    lower = numer_pos // (2 * out_rows)
    lower = jnp.where(numer_pos < 0, 0, lower)
    lower = jnp.where(lower >= valid - 1, valid - 1, lower)
    return jnp.clip(lower, 0, full_rows - window_rows)


def column_table(numer, flip, cols, out_cols):
    valid_cols = cols * numer // 14
    col_pos = jnp.arange(out_cols, dtype=jnp.int32)
    col_pos = jnp.where(flip == 1, out_cols - 1 - col_pos, col_pos)
    return resize_matrix(col_pos, out_cols, valid_cols, cols)


def shards(features, views, conv_first, bias_first, conv_second, bias_second, classify, class_bias):
    feat = features[0]
    rows_dev, cols = (feat.shape[1], feat.shape[2])
    spaces = lax.axis_size("space")
    full_rows = rows_dev * spaces
    place = lax.axis_index("space")
    member_index = lax.axis_index("member")
    members = views.shape[0]
    picked = jnp.arange(members, dtype=jnp.int32) == member_index
    code = jnp.sum(jnp.where(picked, views, 0))
    numer = code // 2
    valid_rows = full_rows * numer // 14
    valid_cols = cols * numer // 14
    count = lax.axis_size("space")
    halo = 2
    forward = [(i, i + 1) for i in range(count - 1)]
    backward = [(target, source) for source, target in forward]
    flat_feat = feat.reshape(feat.shape[0], rows_dev * cols)
    top_rows = lax.ppermute(flat_feat[:, (rows_dev - halo) * cols:], "space", forward)
    low_rows = lax.ppermute(flat_feat[:, : halo * cols], "space", backward)
    top = place * rows_dev
    limits = jnp.stack(
        [halo - top, valid_rows - top + halo, valid_cols, 1 - top, valid_rows - top + 1, -top, valid_rows - top]
    ).astype(jnp.int32)
    biases = jnp.concatenate([bias_first, bias_second, class_bias]).reshape(-1, 1)
    hidden = conv_first_layer(flat_feat, top_rows, low_rows, cols, conv_first, biases, limits)
    logits = conv_second_layer(hidden, cols, conv_second, biases, classify, limits)
    out_rows = UP * full_rows
    out_cols = UP * cols
    own_rows = out_rows // spaces
    part_rows = own_rows // members
    window_rows = (part_rows - 1) // UP + 3
    gathered = gather_rows(logits, "space")
    pieces = []
    for target in range(members):
        first_row = place * own_rows + target * part_rows
        begin = window_start(numer, first_row, full_rows, out_rows, window_rows)
        pieces.append(lax.dynamic_slice_in_dim(gathered, begin, window_rows, 1))
    outgoing = jnp.stack(pieces, 0)
    own_first = place * own_rows + member_index * part_rows
    positions = own_first + jnp.arange(part_rows, dtype=jnp.int32)
    result = jnp.zeros((part_rows, logits.shape[0], out_cols), jnp.float32)
    for shift in range(members):
        if shift == 0:
            arrived = lax.dynamic_index_in_dim(outgoing, member_index, 0, keepdims=False)
        else:
            send = lax.dynamic_index_in_dim(
                outgoing, (member_index + shift) % members, 0, keepdims=False
            )
            arrived = lax.ppermute(
                send, "member", [(i, (i + shift) % members) for i in range(members)]
            )
        source = (member_index - shift) % members
        source_code = jnp.sum(jnp.where(jnp.arange(members) == source, views, 0))
        source_numer = source_code // 2
        source_flip = source_code % 2
        source_valid = full_rows * source_numer // 14
        begin = window_start(source_numer, own_first, full_rows, out_rows, window_rows)
        source_cols = column_table(source_numer, source_flip, cols, out_cols)
        row_table = resize_matrix(positions, out_rows, source_valid, full_rows)
        row_part = lax.dynamic_slice_in_dim(row_table, begin, window_rows, 1)
        widened = jnp.einsum(
            "cyx,jx->cyj", arrived, source_cols, preferred_element_type=jnp.float32
        ).astype(jnp.bfloat16)
        result = result + jnp.einsum(
            "iy,cyj->icj", row_part, widened, preferred_element_type=jnp.float32
        )
    return result


def solution(mesh):
    placed = (
        P(("groups", "member"), None, "space", None),
        P("groups"),
        P(),
        P(),
        P(),
        P(),
        P(),
        P(),
    )
    return jax.shard_map(
        shards,
        mesh=mesh,
        in_specs=placed,
        out_specs=P(("groups", "space", "member"), None, None),
        check_vma=False,
    )
```

```python
import functools

import jax
import jax.numpy as jnp
from jax import lax
from jax.experimental import pallas as pl
from jax.experimental.pallas import tpu as pltpu
from jax.sharding import PartitionSpec as P

UP = 4
LOW_CODE = 8
HIGH_CODE = 29


def with_halo(block, sides, width):
    for axis, dim in sides:
        count = lax.axis_size(axis)
        forward = [(i, i + 1) for i in range(count - 1)]
        backward = [(target, source) for source, target in forward]
        low = lax.ppermute(
            lax.slice_in_dim(block, block.shape[dim] - width, None, axis=dim), axis, forward
        )
        high = lax.ppermute(lax.slice_in_dim(block, 0, width, axis=dim), axis, backward)
        block = jnp.concatenate([low, block, high], axis=dim)
    return block


def gather_rows(block, axis, need):
    count = lax.axis_size(axis)
    if count & (count - 1):
        return lax.all_gather(block, axis, axis=1, tiled=True)
    me = lax.axis_index(axis)
    lead, rows, rest = block.shape[0], block.shape[1], block.shape[2:]
    held = block[:, None]
    bit = count // 2
    while bit:
        span = 2 * bit
        routes = {}
        for p in range(held.shape[1]):
            pairs = []
            for i in range(count):
                j = i ^ bit
                source = p * span + i % span
                if any(source in need[g] for g in range(count) if g // bit == j // bit):
                    pairs.append((i, j))
            routes.setdefault(tuple(pairs), []).append(p)
        parts = [None] * held.shape[1]
        for pairs, places in routes.items():
            if not pairs:
                continue
            sent = lax.ppermute(held[:, jnp.array(places)] if len(places) > 1 else held[:, places[0]:places[0] + 1], axis, list(pairs))
            for n, p in enumerate(places):
                parts[p] = sent[:, n:n + 1]
        empty = jnp.zeros_like(held[:, :1])
        other = jnp.concatenate([empty if x is None else x for x in parts], 1)
        upper = (me & bit) != 0
        held = jnp.where(upper, jnp.stack([other, held], 2), jnp.stack([held, other], 2))
        held = held.reshape((lead, -1, rows) + rest)
        bit //= 2
    return held.reshape((lead, count * rows) + rest)


def block_needs(spaces, members, rows_dev, low_code, high_code):
    full_rows = rows_dev * spaces
    out_rows = UP * full_rows
    own_rows = out_rows // spaces
    part_rows = own_rows // members
    window_rows = (part_rows - 1) // UP + 3
    need = []
    for place in range(spaces):
        blocks = set()
        for numer in range(low_code // 2, high_code // 2 + 1):
            valid = full_rows * numer // 14
            for target in range(members):
                first_row = place * own_rows + target * part_rows
                pos = (2 * first_row + 1) * valid - out_rows
                lower = 0 if pos < 0 else pos // (2 * out_rows)
                lower = valid - 1 if lower >= valid - 1 else lower
                begin = min(max(lower, 0), full_rows - window_rows)
                blocks |= set(range(begin // rows_dev, (begin + window_rows - 1) // rows_dev + 1))
        need.append(blocks)
    return need


def resize_matrix(positions, out_len, valid, in_len):
    numer = (2 * positions + 1) * valid - out_len
    denom = 2 * out_len
    lower = numer // denom
    frac = (numer - lower * denom).astype(jnp.float32) / denom
    below = numer < 0
    frac = jnp.where(below, jnp.float32(0.0), frac)
    lower = jnp.where(below, 0, lower)
    top_index = valid - 1
    over = lower >= top_index
    frac = jnp.where(over, jnp.float32(0.0), frac)
    lower = jnp.where(over, top_index, lower)
    columns = jnp.arange(in_len, dtype=jnp.int32)
    first = jnp.where(columns[None, :] == lower[:, None], 1.0 - frac[:, None], jnp.float32(0.0))
    second = jnp.where(columns[None, :] == lower[:, None] + 1, frac[:, None], jnp.float32(0.0))
    return (first + second).astype(jnp.bfloat16)


def run_conv(x_ref, w_ref, bias, lo, hi, good_cols, o_ref, width, block, head=None):
    flat = block * width
    outs = w_ref.shape[2]
    place = lax.broadcasted_iota(jnp.int32, (1, flat), 1)
    col = place % width
    stacked = jnp.concatenate(
        [jnp.concatenate([w_ref[a, b] for a in range(3)], axis=1) for b in range(3)], axis=0
    )

    def step(i, carry):
        r0 = i * block
        rhs = jnp.concatenate(
            [x_ref[:, pl.ds(pl.multiple_of((r0 + a) * width, width), flat)] for a in range(3)],
            axis=0,
        )
        res = jnp.dot(stacked, rhs, preferred_element_type=jnp.float32)
        taps = [res[b * outs:(b + 1) * outs] for b in range(3)]
        left = jnp.where(col == 0, 0.0, pltpu.roll(taps[0], 1, 1))
        right = jnp.where(col == width - 1, 0.0, pltpu.roll(taps[2], flat - 1, 1))
        total = jnp.maximum(taps[1] + left + right + bias, 0.0)
        row = r0 + place // width
        keep = (row >= lo) & (row < hi) & (col < good_cols)
        out = jnp.where(keep, total, 0.0).astype(jnp.bfloat16)
        if head is not None:
            out = jnp.dot(head[0], out, preferred_element_type=jnp.float32) + head[1]
        o_ref[:, pl.ds(pl.multiple_of(r0 * width, width), flat)] = out.astype(o_ref.dtype)
        return carry

    lax.fori_loop(0, o_ref.shape[1] // flat, step, 0, unroll=True)


def first_body(main_ref, top_ref, low_ref, w_ref, b_ref, s_ref, o_ref, x_ref, *, width, block, halo):
    lo_in, hi_in, good_cols, lo, hi = s_ref[0], s_ref[1], s_ref[2], s_ref[3], s_ref[4]
    chans = main_ref.shape[0]
    rows_main = main_ref.shape[1] // width

    def put(src, offset, rows):
        place = lax.broadcasted_iota(jnp.int32, (1, rows * width), 1)
        row = offset + place // width
        keep = (row >= lo_in) & (row < hi_in) & (place % width < good_cols)
        x_ref[:, pl.ds(pl.multiple_of(offset * width, width), rows * width)] = jnp.where(
            keep, src, jnp.zeros_like(src)
        )

    put(top_ref[...], 0, halo)
    put(low_ref[...], halo + rows_main, halo)

    def chunk(i, carry):
        start = pl.multiple_of(i * 2 * width, width)
        put(main_ref[:, pl.ds(start, 2 * width)], halo + 2 * i, 2)
        return carry

    lax.fori_loop(0, rows_main // 2, chunk, 0)
    run_conv(x_ref, w_ref, b_ref[pl.ds(0, chans), :], lo, hi, good_cols, o_ref, width, block)


def second_body(x_ref, w_ref, b_ref, k_ref, s_ref, o_ref, *, width, block):
    chans = x_ref.shape[0]
    classes = k_ref.shape[0]
    head = (k_ref[...], b_ref[pl.ds(2 * chans, classes), :])
    lo, hi, good_cols = s_ref[5], s_ref[6], s_ref[2]
    run_conv(x_ref, w_ref, b_ref[pl.ds(chans, chans), :], lo, hi, good_cols, o_ref, width, block, head)


def pick_block(rows):
    return next(k for k in (4, 3, 2, 1) if rows % k == 0)


def conv_first_layer(feat, top, low, width, weights, biases, limits):
    chans = feat.shape[0]
    rows_main = feat.shape[1] // width
    halo = top.shape[1] // width
    rows_in = rows_main + 2 * halo
    rows_out = rows_in - 2
    outs = weights.shape[2]
    block = pick_block(rows_out)
    vmem = pl.BlockSpec(memory_space=pltpu.VMEM)
    cost = pl.CostEstimate(
        flops=2 * 9 * rows_out * width * chans * outs,
        bytes_accessed=2 * (chans * rows_in * width + weights.size + rows_out * width * outs),
        transcendentals=0,
    )
    out = pl.pallas_call(
        functools.partial(first_body, width=width, block=block, halo=halo),
        out_shape=jax.ShapeDtypeStruct((outs, rows_out * width), jnp.bfloat16),
        in_specs=[vmem] * 5 + [pl.BlockSpec(memory_space=pltpu.SMEM)],
        out_specs=vmem,
        scratch_shapes=[pltpu.VMEM((chans, rows_in * width), jnp.bfloat16)],
        cost_estimate=cost,
    )(
        feat,
        top,
        low,
        weights,
        biases,
        limits,
    )
    return out


def conv_second_layer(x, width, weights, biases, head, limits):
    chans, flat_in = x.shape
    rows_out = flat_in // width - 2
    outs = weights.shape[2]
    classes = head.shape[0]
    block = pick_block(rows_out)
    vmem = pl.BlockSpec(memory_space=pltpu.VMEM)
    cost = pl.CostEstimate(
        flops=2 * 9 * rows_out * width * chans * outs + 2 * rows_out * width * outs * classes,
        bytes_accessed=2 * (x.size + weights.size + rows_out * width * classes),
        transcendentals=0,
    )
    out = pl.pallas_call(
        functools.partial(second_body, width=width, block=block),
        out_shape=jax.ShapeDtypeStruct((classes, rows_out * width), jnp.bfloat16),
        in_specs=[vmem] * 4 + [pl.BlockSpec(memory_space=pltpu.SMEM)],
        out_specs=vmem,
        cost_estimate=cost,
    )(x, weights, biases, head, limits)
    return out.reshape(classes, rows_out, width)


def window_start(numer, first_row, full_rows, out_rows, window_rows):
    valid = full_rows * numer // 14
    numer_pos = (2 * first_row + 1) * valid - out_rows
    lower = numer_pos // (2 * out_rows)
    lower = jnp.where(numer_pos < 0, 0, lower)
    lower = jnp.where(lower >= valid - 1, valid - 1, lower)
    return jnp.clip(lower, 0, full_rows - window_rows)


def column_table(numer, flip, cols, out_cols):
    valid_cols = cols * numer // 14
    col_pos = jnp.arange(out_cols, dtype=jnp.int32)
    col_pos = jnp.where(flip == 1, out_cols - 1 - col_pos, col_pos)
    return resize_matrix(col_pos, out_cols, valid_cols, cols)


def shards(features, views, conv_first, bias_first, conv_second, bias_second, classify, class_bias):
    feat = features[0]
    rows_dev, cols = (feat.shape[1], feat.shape[2])
    spaces = lax.axis_size("space")
    full_rows = rows_dev * spaces
    place = lax.axis_index("space")
    member_index = lax.axis_index("member")
    members = views.shape[0]
    picked = jnp.arange(members, dtype=jnp.int32) == member_index
    code = jnp.sum(jnp.where(picked, views, 0))
    numer = code // 2
    valid_rows = full_rows * numer // 14
    valid_cols = cols * numer // 14
    count = lax.axis_size("space")
    halo = 2
    forward = [(i, i + 1) for i in range(count - 1)]
    backward = [(target, source) for source, target in forward]
    flat_feat = feat.reshape(feat.shape[0], rows_dev * cols)
    top_rows = lax.ppermute(flat_feat[:, (rows_dev - halo) * cols:], "space", forward)
    low_rows = lax.ppermute(flat_feat[:, : halo * cols], "space", backward)
    top = place * rows_dev
    limits = jnp.stack(
        [halo - top, valid_rows - top + halo, valid_cols, 1 - top, valid_rows - top + 1, -top, valid_rows - top]
    ).astype(jnp.int32)
    biases = jnp.concatenate([bias_first, bias_second, class_bias]).reshape(-1, 1)
    hidden = conv_first_layer(flat_feat, top_rows, low_rows, cols, conv_first, biases, limits)
    logits = conv_second_layer(hidden, cols, conv_second, biases, classify, limits)
    out_rows = UP * full_rows
    out_cols = UP * cols
    own_rows = out_rows // spaces
    part_rows = own_rows // members
    window_rows = (part_rows - 1) // UP + 3
    need = block_needs(spaces, members, rows_dev, LOW_CODE, HIGH_CODE)
    gathered = gather_rows(logits, "space", need)
    pieces = []
    for target in range(members):
        first_row = place * own_rows + target * part_rows
        begin = window_start(numer, first_row, full_rows, out_rows, window_rows)
        pieces.append(lax.dynamic_slice_in_dim(gathered, begin, window_rows, 1))
    outgoing = jnp.stack(pieces, 0)
    own_first = place * own_rows + member_index * part_rows
    positions = own_first + jnp.arange(part_rows, dtype=jnp.int32)
    result = jnp.zeros((part_rows, logits.shape[0], out_cols), jnp.float32)
    for shift in range(members):
        if shift == 0:
            arrived = lax.dynamic_index_in_dim(outgoing, member_index, 0, keepdims=False)
        else:
            send = lax.dynamic_index_in_dim(
                outgoing, (member_index + shift) % members, 0, keepdims=False
            )
            arrived = lax.ppermute(
                send, "member", [(i, (i + shift) % members) for i in range(members)]
            )
        source = (member_index - shift) % members
        source_code = jnp.sum(jnp.where(jnp.arange(members) == source, views, 0))
        source_numer = source_code // 2
        source_flip = source_code % 2
        source_valid = full_rows * source_numer // 14
        begin = window_start(source_numer, own_first, full_rows, out_rows, window_rows)
        source_cols = column_table(source_numer, source_flip, cols, out_cols)
        row_table = resize_matrix(positions, out_rows, source_valid, full_rows)
        row_part = lax.dynamic_slice_in_dim(row_table, begin, window_rows, 1)
        widened = jnp.einsum(
            "cyx,jx->cyj", arrived, source_cols, preferred_element_type=jnp.float32
        ).astype(jnp.bfloat16)
        result = result + jnp.einsum(
            "iy,cyj->icj", row_part, widened, preferred_element_type=jnp.float32
        )
    return result


def solution(mesh):
    placed = (
        P(("groups", "member"), None, "space", None),
        P("groups"),
        P(),
        P(),
        P(),
        P(),
        P(),
        P(),
    )
    return jax.shard_map(
        shards,
        mesh=mesh,
        in_specs=placed,
        out_specs=P(("groups", "space", "member"), None, None),
        check_vma=False,
    )
```

```python
import functools

import jax
import jax.numpy as jnp
from jax import lax
from jax.experimental import pallas as pl
from jax.experimental.pallas import tpu as pltpu
from jax.sharding import PartitionSpec as P

UP = 4
LOW_CODE = 8
HIGH_CODE = 29


def with_halo(block, sides, width):
    for axis, dim in sides:
        count = lax.axis_size(axis)
        forward = [(i, i + 1) for i in range(count - 1)]
        backward = [(target, source) for source, target in forward]
        low = lax.ppermute(
            lax.slice_in_dim(block, block.shape[dim] - width, None, axis=dim), axis, forward
        )
        high = lax.ppermute(lax.slice_in_dim(block, 0, width, axis=dim), axis, backward)
        block = jnp.concatenate([low, block, high], axis=dim)
    return block


def gather_rows(block, axis, need):
    count = lax.axis_size(axis)
    if count & (count - 1):
        return lax.all_gather(block, axis, axis=1, tiled=True)
    me = lax.axis_index(axis)
    lead, rows, rest = block.shape[0], block.shape[1], block.shape[2:]
    held = block[:, None]
    bit = count // 2
    while bit:
        span = 2 * bit
        pairs = []
        for i in range(count):
            j = i ^ bit
            wanted = set().union(*[need[g] for g in range(count) if g // bit == j // bit])
            if any(p * span + i % span in wanted for p in range(held.shape[1])):
                pairs.append((i, j))
        other = lax.ppermute(held, axis, pairs)
        upper = (me & bit) != 0
        held = jnp.where(upper, jnp.stack([other, held], 2), jnp.stack([held, other], 2))
        held = held.reshape((lead, -1, rows) + rest)
        bit //= 2
    return held.reshape((lead, count * rows) + rest)


def block_needs(spaces, members, rows_dev, low_code, high_code):
    full_rows = rows_dev * spaces
    out_rows = UP * full_rows
    own_rows = out_rows // spaces
    part_rows = own_rows // members
    window_rows = (part_rows - 1) // UP + 3
    need = []
    for place in range(spaces):
        blocks = set()
        for numer in range(low_code // 2, high_code // 2 + 1):
            valid = full_rows * numer // 14
            for target in range(members):
                first_row = place * own_rows + target * part_rows
                pos = (2 * first_row + 1) * valid - out_rows
                lower = 0 if pos < 0 else pos // (2 * out_rows)
                lower = valid - 1 if lower >= valid - 1 else lower
                begin = min(max(lower, 0), full_rows - window_rows)
                blocks |= set(range(begin // rows_dev, (begin + window_rows - 1) // rows_dev + 1))
        need.append(blocks)
    return need


def resize_matrix(positions, out_len, valid, in_len):
    numer = (2 * positions + 1) * valid - out_len
    denom = 2 * out_len
    lower = numer // denom
    frac = (numer - lower * denom).astype(jnp.float32) / denom
    below = numer < 0
    frac = jnp.where(below, jnp.float32(0.0), frac)
    lower = jnp.where(below, 0, lower)
    top_index = valid - 1
    over = lower >= top_index
    frac = jnp.where(over, jnp.float32(0.0), frac)
    lower = jnp.where(over, top_index, lower)
    columns = jnp.arange(in_len, dtype=jnp.int32)
    first = jnp.where(columns[None, :] == lower[:, None], 1.0 - frac[:, None], jnp.float32(0.0))
    second = jnp.where(columns[None, :] == lower[:, None] + 1, frac[:, None], jnp.float32(0.0))
    return (first + second).astype(jnp.bfloat16)


def run_conv(x_ref, w_ref, bias, lo, hi, good_cols, o_ref, width, block, head=None):
    flat = block * width
    outs = w_ref.shape[2]
    place = lax.broadcasted_iota(jnp.int32, (1, flat), 1)
    col = place % width
    stacked = jnp.concatenate(
        [jnp.concatenate([w_ref[a, b] for a in range(3)], axis=1) for b in range(3)], axis=0
    )

    def step(i, carry):
        r0 = i * block
        rhs = jnp.concatenate(
            [x_ref[:, pl.ds(pl.multiple_of((r0 + a) * width, width), flat)] for a in range(3)],
            axis=0,
        )
        res = jnp.dot(stacked, rhs, preferred_element_type=jnp.float32)
        taps = [res[b * outs:(b + 1) * outs] for b in range(3)]
        left = jnp.where(col == 0, 0.0, pltpu.roll(taps[0], 1, 1))
        right = jnp.where(col == width - 1, 0.0, pltpu.roll(taps[2], flat - 1, 1))
        total = jnp.maximum(taps[1] + left + right + bias, 0.0)
        row = r0 + place // width
        keep = (row >= lo) & (row < hi) & (col < good_cols)
        out = jnp.where(keep, total, 0.0).astype(jnp.bfloat16)
        if head is not None:
            out = jnp.dot(head[0], out, preferred_element_type=jnp.float32) + head[1]
        o_ref[:, pl.ds(pl.multiple_of(r0 * width, width), flat)] = out.astype(o_ref.dtype)
        return carry

    lax.fori_loop(0, o_ref.shape[1] // flat, step, 0, unroll=True)


def first_body(main_ref, top_ref, low_ref, w_ref, b_ref, s_ref, o_ref, x_ref, *, width, block, halo):
    lo_in, hi_in, good_cols, lo, hi = s_ref[0], s_ref[1], s_ref[2], s_ref[3], s_ref[4]
    chans = main_ref.shape[0]
    rows_main = main_ref.shape[1] // width

    def put(src, offset, rows):
        place = lax.broadcasted_iota(jnp.int32, (1, rows * width), 1)
        row = offset + place // width
        keep = (row >= lo_in) & (row < hi_in) & (place % width < good_cols)
        x_ref[:, pl.ds(pl.multiple_of(offset * width, width), rows * width)] = jnp.where(
            keep, src, jnp.zeros_like(src)
        )

    put(top_ref[...], 0, halo)
    put(low_ref[...], halo + rows_main, halo)

    def chunk(i, carry):
        start = pl.multiple_of(i * 2 * width, width)
        put(main_ref[:, pl.ds(start, 2 * width)], halo + 2 * i, 2)
        return carry

    lax.fori_loop(0, rows_main // 2, chunk, 0)
    run_conv(x_ref, w_ref, b_ref[pl.ds(0, chans), :], lo, hi, good_cols, o_ref, width, block)


def second_body(x_ref, w_ref, b_ref, k_ref, s_ref, o_ref, *, width, block):
    chans = x_ref.shape[0]
    classes = k_ref.shape[0]
    head = (k_ref[...], b_ref[pl.ds(2 * chans, classes), :])
    lo, hi, good_cols = s_ref[5], s_ref[6], s_ref[2]
    run_conv(x_ref, w_ref, b_ref[pl.ds(chans, chans), :], lo, hi, good_cols, o_ref, width, block, head)


def pick_block(rows):
    return next(k for k in (4, 3, 2, 1) if rows % k == 0)


def conv_first_layer(feat, top, low, width, weights, biases, limits):
    chans = feat.shape[0]
    rows_main = feat.shape[1] // width
    halo = top.shape[1] // width
    rows_in = rows_main + 2 * halo
    rows_out = rows_in - 2
    outs = weights.shape[2]
    block = pick_block(rows_out)
    vmem = pl.BlockSpec(memory_space=pltpu.VMEM)
    cost = pl.CostEstimate(
        flops=2 * 9 * rows_out * width * chans * outs,
        bytes_accessed=2 * (chans * rows_in * width + weights.size + rows_out * width * outs),
        transcendentals=0,
    )
    out = pl.pallas_call(
        functools.partial(first_body, width=width, block=block, halo=halo),
        out_shape=jax.ShapeDtypeStruct((outs, rows_out * width), jnp.bfloat16),
        in_specs=[vmem] * 5 + [pl.BlockSpec(memory_space=pltpu.SMEM)],
        out_specs=vmem,
        scratch_shapes=[pltpu.VMEM((chans, rows_in * width), jnp.bfloat16)],
        cost_estimate=cost,
    )(
        feat,
        top,
        low,
        weights,
        biases,
        limits,
    )
    return out


def conv_second_layer(x, width, weights, biases, head, limits):
    chans, flat_in = x.shape
    rows_out = flat_in // width - 2
    outs = weights.shape[2]
    classes = head.shape[0]
    block = pick_block(rows_out)
    vmem = pl.BlockSpec(memory_space=pltpu.VMEM)
    cost = pl.CostEstimate(
        flops=2 * 9 * rows_out * width * chans * outs + 2 * rows_out * width * outs * classes,
        bytes_accessed=2 * (x.size + weights.size + rows_out * width * classes),
        transcendentals=0,
    )
    out = pl.pallas_call(
        functools.partial(second_body, width=width, block=block),
        out_shape=jax.ShapeDtypeStruct((classes, rows_out * width), jnp.bfloat16),
        in_specs=[vmem] * 4 + [pl.BlockSpec(memory_space=pltpu.SMEM)],
        out_specs=vmem,
        cost_estimate=cost,
    )(x, weights, biases, head, limits)
    return out.reshape(classes, rows_out, width)


def window_start(numer, first_row, full_rows, out_rows, window_rows):
    valid = full_rows * numer // 14
    numer_pos = (2 * first_row + 1) * valid - out_rows
    lower = numer_pos // (2 * out_rows)
    lower = jnp.where(numer_pos < 0, 0, lower)
    lower = jnp.where(lower >= valid - 1, valid - 1, lower)
    return jnp.clip(lower, 0, full_rows - window_rows)


def column_table(numer, flip, cols, out_cols):
    valid_cols = cols * numer // 14
    col_pos = jnp.arange(out_cols, dtype=jnp.int32)
    col_pos = jnp.where(flip == 1, out_cols - 1 - col_pos, col_pos)
    return resize_matrix(col_pos, out_cols, valid_cols, cols)


def shards(features, views, conv_first, bias_first, conv_second, bias_second, classify, class_bias):
    feat = features[0]
    rows_dev, cols = (feat.shape[1], feat.shape[2])
    spaces = lax.axis_size("space")
    full_rows = rows_dev * spaces
    place = lax.axis_index("space")
    member_index = lax.axis_index("member")
    members = views.shape[0]
    picked = jnp.arange(members, dtype=jnp.int32) == member_index
    code = jnp.sum(jnp.where(picked, views, 0))
    numer = code // 2
    valid_rows = full_rows * numer // 14
    valid_cols = cols * numer // 14
    count = lax.axis_size("space")
    halo = 2
    forward = [(i, i + 1) for i in range(count - 1)]
    backward = [(target, source) for source, target in forward]
    flat_feat = feat.reshape(feat.shape[0], rows_dev * cols)
    top_rows = lax.ppermute(flat_feat[:, (rows_dev - halo) * cols:], "space", forward)
    low_rows = lax.ppermute(flat_feat[:, : halo * cols], "space", backward)
    top = place * rows_dev
    limits = jnp.stack(
        [halo - top, valid_rows - top + halo, valid_cols, 1 - top, valid_rows - top + 1, -top, valid_rows - top]
    ).astype(jnp.int32)
    biases = jnp.concatenate([bias_first, bias_second, class_bias]).reshape(-1, 1)
    hidden = conv_first_layer(flat_feat, top_rows, low_rows, cols, conv_first, biases, limits)
    logits = conv_second_layer(hidden, cols, conv_second, biases, classify, limits)
    out_rows = UP * full_rows
    out_cols = UP * cols
    own_rows = out_rows // spaces
    part_rows = own_rows // members
    window_rows = (part_rows - 1) // UP + 3
    need = block_needs(spaces, members, rows_dev, LOW_CODE, HIGH_CODE)
    gathered = gather_rows(logits, "space", need)
    pieces = []
    for target in range(members):
        first_row = place * own_rows + target * part_rows
        begin = window_start(numer, first_row, full_rows, out_rows, window_rows)
        pieces.append(lax.dynamic_slice_in_dim(gathered, begin, window_rows, 1))
    outgoing = jnp.stack(pieces, 0)
    own_first = place * own_rows + member_index * part_rows
    positions = own_first + jnp.arange(part_rows, dtype=jnp.int32)
    result = jnp.zeros((part_rows, logits.shape[0], out_cols), jnp.float32)
    for shift in range(members):
        if shift == 0:
            arrived = lax.dynamic_index_in_dim(outgoing, member_index, 0, keepdims=False)
        else:
            send = lax.dynamic_index_in_dim(
                outgoing, (member_index + shift) % members, 0, keepdims=False
            )
            arrived = lax.ppermute(
                send, "member", [(i, (i + shift) % members) for i in range(members)]
            )
        source = (member_index - shift) % members
        source_code = jnp.sum(jnp.where(jnp.arange(members) == source, views, 0))
        source_numer = source_code // 2
        source_flip = source_code % 2
        source_valid = full_rows * source_numer // 14
        begin = window_start(source_numer, own_first, full_rows, out_rows, window_rows)
        source_cols = column_table(source_numer, source_flip, cols, out_cols)
        row_table = resize_matrix(positions, out_rows, source_valid, full_rows)
        row_part = lax.dynamic_slice_in_dim(row_table, begin, window_rows, 1)
        widened = jnp.einsum(
            "cyx,jx->cyj", arrived, source_cols, preferred_element_type=jnp.float32
        ).astype(jnp.bfloat16)
        result = result + jnp.einsum(
            "iy,cyj->icj", row_part, widened, preferred_element_type=jnp.float32
        )
    return result


def solution(mesh):
    placed = (
        P(("groups", "member"), None, "space", None),
        P("groups"),
        P(),
        P(),
        P(),
        P(),
        P(),
        P(),
    )
    return jax.shard_map(
        shards,
        mesh=mesh,
        in_specs=placed,
        out_specs=P(("groups", "space", "member"), None, None),
        check_vma=False,
    )
```

```python
import functools

import jax
import jax.numpy as jnp
from jax import lax
from jax.experimental import pallas as pl
from jax.experimental.pallas import tpu as pltpu
from jax.sharding import PartitionSpec as P

UP = 4
LOW_CODE = 8
HIGH_CODE = 29


def with_halo(block, sides, width):
    for axis, dim in sides:
        count = lax.axis_size(axis)
        forward = [(i, i + 1) for i in range(count - 1)]
        backward = [(target, source) for source, target in forward]
        low = lax.ppermute(
            lax.slice_in_dim(block, block.shape[dim] - width, None, axis=dim), axis, forward
        )
        high = lax.ppermute(lax.slice_in_dim(block, 0, width, axis=dim), axis, backward)
        block = jnp.concatenate([low, block, high], axis=dim)
    return block


def gather_rows(block, axis, need):
    count = lax.axis_size(axis)
    if count & (count - 1):
        return lax.all_gather(block, axis, axis=1, tiled=True)
    me = lax.axis_index(axis)
    lead, rows, rest = block.shape[0], block.shape[1], block.shape[2:]
    held = block[:, None]
    bit = count // 2
    while bit:
        span = 2 * bit
        routes = {}
        for p in range(held.shape[1]):
            pairs = []
            for i in range(count):
                j = i ^ bit
                wanted = set().union(*[need[g] for g in range(count) if g // bit == j // bit])
                if p * span + i % span in wanted:
                    pairs.append((i, j))
            routes.setdefault(tuple(pairs), []).append(p)
        if bit == 1 or len(routes) == 1:
            pairs = sorted(set().union(*[set(r) for r in routes]))
            other = lax.ppermute(held, axis, pairs)
        else:
            parts = [None] * held.shape[1]
            for pairs, places in routes.items():
                if pairs:
                    for p in places:
                        parts[p] = lax.ppermute(held[:, p:p + 1], axis, list(pairs))
            empty = jnp.zeros_like(held[:, :1])
            other = jnp.concatenate([empty if x is None else x for x in parts], 1)
        upper = (me & bit) != 0
        held = jnp.where(upper, jnp.stack([other, held], 2), jnp.stack([held, other], 2))
        held = held.reshape((lead, -1, rows) + rest)
        bit //= 2
    return held.reshape((lead, count * rows) + rest)


def block_needs(spaces, members, rows_dev, low_code, high_code):
    full_rows = rows_dev * spaces
    out_rows = UP * full_rows
    own_rows = out_rows // spaces
    part_rows = own_rows // members
    window_rows = (part_rows - 1) // UP + 3
    need = []
    for place in range(spaces):
        blocks = set()
        for numer in range(low_code // 2, high_code // 2 + 1):
            valid = full_rows * numer // 14
            for target in range(members):
                first_row = place * own_rows + target * part_rows
                pos = (2 * first_row + 1) * valid - out_rows
                lower = 0 if pos < 0 else pos // (2 * out_rows)
                lower = valid - 1 if lower >= valid - 1 else lower
                begin = min(max(lower, 0), full_rows - window_rows)
                blocks |= set(range(begin // rows_dev, (begin + window_rows - 1) // rows_dev + 1))
        need.append(blocks)
    return need


def resize_matrix(positions, out_len, valid, in_len):
    numer = (2 * positions + 1) * valid - out_len
    denom = 2 * out_len
    lower = numer // denom
    frac = (numer - lower * denom).astype(jnp.float32) / denom
    below = numer < 0
    frac = jnp.where(below, jnp.float32(0.0), frac)
    lower = jnp.where(below, 0, lower)
    top_index = valid - 1
    over = lower >= top_index
    frac = jnp.where(over, jnp.float32(0.0), frac)
    lower = jnp.where(over, top_index, lower)
    columns = jnp.arange(in_len, dtype=jnp.int32)
    first = jnp.where(columns[None, :] == lower[:, None], 1.0 - frac[:, None], jnp.float32(0.0))
    second = jnp.where(columns[None, :] == lower[:, None] + 1, frac[:, None], jnp.float32(0.0))
    return (first + second).astype(jnp.bfloat16)


def run_conv(x_ref, w_ref, bias, lo, hi, good_cols, o_ref, width, block, head=None):
    flat = block * width
    outs = w_ref.shape[2]
    place = lax.broadcasted_iota(jnp.int32, (1, flat), 1)
    col = place % width
    stacked = jnp.concatenate(
        [jnp.concatenate([w_ref[a, b] for a in range(3)], axis=1) for b in range(3)], axis=0
    )

    def step(i, carry):
        r0 = i * block
        rhs = jnp.concatenate(
            [x_ref[:, pl.ds(pl.multiple_of((r0 + a) * width, width), flat)] for a in range(3)],
            axis=0,
        )
        res = jnp.dot(stacked, rhs, preferred_element_type=jnp.float32)
        taps = [res[b * outs:(b + 1) * outs] for b in range(3)]
        left = jnp.where(col == 0, 0.0, pltpu.roll(taps[0], 1, 1))
        right = jnp.where(col == width - 1, 0.0, pltpu.roll(taps[2], flat - 1, 1))
        total = jnp.maximum(taps[1] + left + right + bias, 0.0)
        row = r0 + place // width
        keep = (row >= lo) & (row < hi) & (col < good_cols)
        out = jnp.where(keep, total, 0.0).astype(jnp.bfloat16)
        if head is not None:
            out = jnp.dot(head[0], out, preferred_element_type=jnp.float32) + head[1]
        o_ref[:, pl.ds(pl.multiple_of(r0 * width, width), flat)] = out.astype(o_ref.dtype)
        return carry

    lax.fori_loop(0, o_ref.shape[1] // flat, step, 0, unroll=True)


def first_body(main_ref, top_ref, low_ref, w_ref, b_ref, s_ref, o_ref, x_ref, *, width, block, halo):
    lo_in, hi_in, good_cols, lo, hi = s_ref[0], s_ref[1], s_ref[2], s_ref[3], s_ref[4]
    chans = main_ref.shape[0]
    rows_main = main_ref.shape[1] // width

    def put(src, offset, rows):
        place = lax.broadcasted_iota(jnp.int32, (1, rows * width), 1)
        row = offset + place // width
        keep = (row >= lo_in) & (row < hi_in) & (place % width < good_cols)
        x_ref[:, pl.ds(pl.multiple_of(offset * width, width), rows * width)] = jnp.where(
            keep, src, jnp.zeros_like(src)
        )

    put(top_ref[...], 0, halo)
    put(low_ref[...], halo + rows_main, halo)

    def chunk(i, carry):
        start = pl.multiple_of(i * 2 * width, width)
        put(main_ref[:, pl.ds(start, 2 * width)], halo + 2 * i, 2)
        return carry

    lax.fori_loop(0, rows_main // 2, chunk, 0)
    run_conv(x_ref, w_ref, b_ref[pl.ds(0, chans), :], lo, hi, good_cols, o_ref, width, block)


def second_body(x_ref, w_ref, b_ref, k_ref, s_ref, o_ref, *, width, block):
    chans = x_ref.shape[0]
    classes = k_ref.shape[0]
    head = (k_ref[...], b_ref[pl.ds(2 * chans, classes), :])
    lo, hi, good_cols = s_ref[5], s_ref[6], s_ref[2]
    run_conv(x_ref, w_ref, b_ref[pl.ds(chans, chans), :], lo, hi, good_cols, o_ref, width, block, head)


def pick_block(rows):
    return next(k for k in (4, 3, 2, 1) if rows % k == 0)


def conv_first_layer(feat, top, low, width, weights, biases, limits):
    chans = feat.shape[0]
    rows_main = feat.shape[1] // width
    halo = top.shape[1] // width
    rows_in = rows_main + 2 * halo
    rows_out = rows_in - 2
    outs = weights.shape[2]
    block = pick_block(rows_out)
    vmem = pl.BlockSpec(memory_space=pltpu.VMEM)
    cost = pl.CostEstimate(
        flops=2 * 9 * rows_out * width * chans * outs,
        bytes_accessed=2 * (chans * rows_in * width + weights.size + rows_out * width * outs),
        transcendentals=0,
    )
    out = pl.pallas_call(
        functools.partial(first_body, width=width, block=block, halo=halo),
        out_shape=jax.ShapeDtypeStruct((outs, rows_out * width), jnp.bfloat16),
        in_specs=[vmem] * 5 + [pl.BlockSpec(memory_space=pltpu.SMEM)],
        out_specs=vmem,
        scratch_shapes=[pltpu.VMEM((chans, rows_in * width), jnp.bfloat16)],
        cost_estimate=cost,
    )(
        feat,
        top,
        low,
        weights,
        biases,
        limits,
    )
    return out


def conv_second_layer(x, width, weights, biases, head, limits):
    chans, flat_in = x.shape
    rows_out = flat_in // width - 2
    outs = weights.shape[2]
    classes = head.shape[0]
    block = pick_block(rows_out)
    vmem = pl.BlockSpec(memory_space=pltpu.VMEM)
    cost = pl.CostEstimate(
        flops=2 * 9 * rows_out * width * chans * outs + 2 * rows_out * width * outs * classes,
        bytes_accessed=2 * (x.size + weights.size + rows_out * width * classes),
        transcendentals=0,
    )
    out = pl.pallas_call(
        functools.partial(second_body, width=width, block=block),
        out_shape=jax.ShapeDtypeStruct((classes, rows_out * width), jnp.bfloat16),
        in_specs=[vmem] * 4 + [pl.BlockSpec(memory_space=pltpu.SMEM)],
        out_specs=vmem,
        cost_estimate=cost,
    )(x, weights, biases, head, limits)
    return out.reshape(classes, rows_out, width)


def window_start(numer, first_row, full_rows, out_rows, window_rows):
    valid = full_rows * numer // 14
    numer_pos = (2 * first_row + 1) * valid - out_rows
    lower = numer_pos // (2 * out_rows)
    lower = jnp.where(numer_pos < 0, 0, lower)
    lower = jnp.where(lower >= valid - 1, valid - 1, lower)
    return jnp.clip(lower, 0, full_rows - window_rows)


def column_table(numer, flip, cols, out_cols):
    valid_cols = cols * numer // 14
    col_pos = jnp.arange(out_cols, dtype=jnp.int32)
    col_pos = jnp.where(flip == 1, out_cols - 1 - col_pos, col_pos)
    return resize_matrix(col_pos, out_cols, valid_cols, cols)


def shards(features, views, conv_first, bias_first, conv_second, bias_second, classify, class_bias):
    feat = features[0]
    rows_dev, cols = (feat.shape[1], feat.shape[2])
    spaces = lax.axis_size("space")
    full_rows = rows_dev * spaces
    place = lax.axis_index("space")
    member_index = lax.axis_index("member")
    members = views.shape[0]
    picked = jnp.arange(members, dtype=jnp.int32) == member_index
    code = jnp.sum(jnp.where(picked, views, 0))
    numer = code // 2
    valid_rows = full_rows * numer // 14
    valid_cols = cols * numer // 14
    count = lax.axis_size("space")
    halo = 2
    forward = [(i, i + 1) for i in range(count - 1)]
    backward = [(target, source) for source, target in forward]
    flat_feat = feat.reshape(feat.shape[0], rows_dev * cols)
    top_rows = lax.ppermute(flat_feat[:, (rows_dev - halo) * cols:], "space", forward)
    low_rows = lax.ppermute(flat_feat[:, : halo * cols], "space", backward)
    top = place * rows_dev
    limits = jnp.stack(
        [halo - top, valid_rows - top + halo, valid_cols, 1 - top, valid_rows - top + 1, -top, valid_rows - top]
    ).astype(jnp.int32)
    biases = jnp.concatenate([bias_first, bias_second, class_bias]).reshape(-1, 1)
    hidden = conv_first_layer(flat_feat, top_rows, low_rows, cols, conv_first, biases, limits)
    logits = conv_second_layer(hidden, cols, conv_second, biases, classify, limits)
    out_rows = UP * full_rows
    out_cols = UP * cols
    own_rows = out_rows // spaces
    part_rows = own_rows // members
    window_rows = (part_rows - 1) // UP + 3
    need = block_needs(spaces, members, rows_dev, LOW_CODE, HIGH_CODE)
    gathered = gather_rows(logits, "space", need)
    pieces = []
    for target in range(members):
        first_row = place * own_rows + target * part_rows
        begin = window_start(numer, first_row, full_rows, out_rows, window_rows)
        pieces.append(lax.dynamic_slice_in_dim(gathered, begin, window_rows, 1))
    outgoing = jnp.stack(pieces, 0)
    own_first = place * own_rows + member_index * part_rows
    positions = own_first + jnp.arange(part_rows, dtype=jnp.int32)
    result = jnp.zeros((part_rows, logits.shape[0], out_cols), jnp.float32)
    for shift in range(members):
        if shift == 0:
            arrived = lax.dynamic_index_in_dim(outgoing, member_index, 0, keepdims=False)
        else:
            send = lax.dynamic_index_in_dim(
                outgoing, (member_index + shift) % members, 0, keepdims=False
            )
            arrived = lax.ppermute(
                send, "member", [(i, (i + shift) % members) for i in range(members)]
            )
        source = (member_index - shift) % members
        source_code = jnp.sum(jnp.where(jnp.arange(members) == source, views, 0))
        source_numer = source_code // 2
        source_flip = source_code % 2
        source_valid = full_rows * source_numer // 14
        begin = window_start(source_numer, own_first, full_rows, out_rows, window_rows)
        source_cols = column_table(source_numer, source_flip, cols, out_cols)
        row_table = resize_matrix(positions, out_rows, source_valid, full_rows)
        row_part = lax.dynamic_slice_in_dim(row_table, begin, window_rows, 1)
        widened = jnp.einsum(
            "cyx,jx->cyj", arrived, source_cols, preferred_element_type=jnp.float32
        ).astype(jnp.bfloat16)
        result = result + jnp.einsum(
            "iy,cyj->icj", row_part, widened, preferred_element_type=jnp.float32
        )
    return result


def solution(mesh):
    placed = (
        P(("groups", "member"), None, "space", None),
        P("groups"),
        P(),
        P(),
        P(),
        P(),
        P(),
        P(),
    )
    return jax.shard_map(
        shards,
        mesh=mesh,
        in_specs=placed,
        out_specs=P(("groups", "space", "member"), None, None),
        check_vma=False,
    )
```

```python
import functools

import jax
import jax.numpy as jnp
from jax import lax
from jax.experimental import pallas as pl
from jax.experimental.pallas import tpu as pltpu
from jax.sharding import PartitionSpec as P

UP = 4
LOW_CODE = 8
HIGH_CODE = 29


def with_halo(block, sides, width):
    for axis, dim in sides:
        count = lax.axis_size(axis)
        forward = [(i, i + 1) for i in range(count - 1)]
        backward = [(target, source) for source, target in forward]
        low = lax.ppermute(
            lax.slice_in_dim(block, block.shape[dim] - width, None, axis=dim), axis, forward
        )
        high = lax.ppermute(lax.slice_in_dim(block, 0, width, axis=dim), axis, backward)
        block = jnp.concatenate([low, block, high], axis=dim)
    return block


def gather_rows(block, axis, need):
    count = lax.axis_size(axis)
    if count & (count - 1):
        return lax.all_gather(block, axis, axis=1, tiled=True)
    me = lax.axis_index(axis)
    lead, rows, rest = block.shape[0], block.shape[1], block.shape[2:]
    held = block[:, None]
    bit = count // 2
    while bit:
        span = 2 * bit
        routes = {}
        for p in range(held.shape[1]):
            pairs = []
            for i in range(count):
                j = i ^ bit
                wanted = set().union(*[need[g] for g in range(count) if g // bit == j // bit])
                if p * span + i % span in wanted:
                    pairs.append((i, j))
            routes.setdefault(tuple(pairs), []).append(p)
        if bit == 1 or len(routes) == 1:
            pairs = sorted(set().union(*[set(r) for r in routes]))
            other = lax.ppermute(held, axis, pairs)
        else:
            parts = [None] * held.shape[1]
            for pairs, places in routes.items():
                if pairs:
                    for p in places:
                        parts[p] = lax.ppermute(held[:, p:p + 1], axis, list(pairs))
            empty = jnp.zeros_like(held[:, :1])
            other = jnp.concatenate([empty if x is None else x for x in parts], 1)
        upper = (me & bit) != 0
        held = jnp.where(upper, jnp.stack([other, held], 2), jnp.stack([held, other], 2))
        held = held.reshape((lead, -1, rows) + rest)
        bit //= 2
    return held.reshape((lead, count * rows) + rest)


def block_needs(spaces, members, rows_dev, low_code, high_code):
    full_rows = rows_dev * spaces
    out_rows = UP * full_rows
    own_rows = out_rows // spaces
    part_rows = own_rows // members
    window_rows = (part_rows - 1) // UP + 3
    need = []
    for place in range(spaces):
        blocks = set()
        for numer in range(low_code // 2, high_code // 2 + 1):
            valid = full_rows * numer // 14
            for target in range(members):
                first_row = place * own_rows + target * part_rows
                pos = (2 * first_row + 1) * valid - out_rows
                lower = 0 if pos < 0 else pos // (2 * out_rows)
                lower = valid - 1 if lower >= valid - 1 else lower
                begin = min(max(lower, 0), full_rows - window_rows)
                blocks |= set(range(begin // rows_dev, (begin + window_rows - 1) // rows_dev + 1))
        need.append(blocks)
    return need


def resize_matrix(positions, out_len, valid, in_len):
    numer = (2 * positions + 1) * valid - out_len
    denom = 2 * out_len
    lower = numer // denom
    frac = (numer - lower * denom).astype(jnp.float32) / denom
    below = numer < 0
    frac = jnp.where(below, jnp.float32(0.0), frac)
    lower = jnp.where(below, 0, lower)
    top_index = valid - 1
    over = lower >= top_index
    frac = jnp.where(over, jnp.float32(0.0), frac)
    lower = jnp.where(over, top_index, lower)
    columns = jnp.arange(in_len, dtype=jnp.int32)
    first = jnp.where(columns[None, :] == lower[:, None], 1.0 - frac[:, None], jnp.float32(0.0))
    second = jnp.where(columns[None, :] == lower[:, None] + 1, frac[:, None], jnp.float32(0.0))
    return (first + second).astype(jnp.bfloat16)


def run_conv(x_ref, w_ref, bias, lo, hi, good_cols, o_ref, width, block, head=None):
    flat = block * width
    outs = w_ref.shape[2]
    place = lax.broadcasted_iota(jnp.int32, (1, flat), 1)
    col = place % width
    stacked = jnp.concatenate(
        [jnp.concatenate([w_ref[a, b] for a in range(3)], axis=1) for b in range(3)], axis=0
    )

    def step(i, carry):
        r0 = i * block
        rhs = jnp.concatenate(
            [x_ref[:, pl.ds(pl.multiple_of((r0 + a) * width, width), flat)] for a in range(3)],
            axis=0,
        )
        res = jnp.dot(stacked, rhs, preferred_element_type=jnp.float32)
        taps = [res[b * outs:(b + 1) * outs] for b in range(3)]
        left = jnp.where(col == 0, 0.0, pltpu.roll(taps[0], 1, 1))
        right = jnp.where(col == width - 1, 0.0, pltpu.roll(taps[2], flat - 1, 1))
        total = jnp.maximum(taps[1] + left + right + bias, 0.0)
        row = r0 + place // width
        keep = (row >= lo) & (row < hi) & (col < good_cols)
        out = jnp.where(keep, total, 0.0).astype(jnp.bfloat16)
        if head is None:
            o_ref[:, pl.ds(r0 * width, flat)] = out.astype(o_ref.dtype)
        else:
            out = jnp.dot(head[0], out, preferred_element_type=jnp.float32) + head[1]
            out = out.astype(o_ref.dtype)
            for r in range(block):
                o_ref[:, r0 + r, :] = out[:, r * width:(r + 1) * width]
        return carry

    rows_out = o_ref.shape[1] // width if head is None else o_ref.shape[1]
    for i in range(rows_out // block):
        step(i, 0)


def first_body(main_ref, top_ref, low_ref, w_ref, b_ref, s_ref, o_ref, x_ref, *, width, block, halo):
    lo_in, hi_in, good_cols, lo, hi = s_ref[0], s_ref[1], s_ref[2], s_ref[3], s_ref[4]
    chans = main_ref.shape[0]
    rows_main = main_ref.shape[1] // width

    def put(src, offset, rows):
        place = lax.broadcasted_iota(jnp.int32, (1, rows * width), 1)
        row = offset + place // width
        keep = (row >= lo_in) & (row < hi_in) & (place % width < good_cols)
        x_ref[:, pl.ds(pl.multiple_of(offset * width, width), rows * width)] = jnp.where(
            keep, src, jnp.zeros_like(src)
        )

    put(top_ref[...], 0, halo)
    put(low_ref[...], halo + rows_main, halo)

    def chunk(i, carry):
        start = pl.multiple_of(i * 2 * width, width)
        put(main_ref[:, pl.ds(start, 2 * width)], halo + 2 * i, 2)
        return carry

    lax.fori_loop(0, rows_main // 2, chunk, 0)
    run_conv(x_ref, w_ref, b_ref[pl.ds(0, chans), :], lo, hi, good_cols, o_ref, width, block)


def second_body(x_ref, w_ref, b_ref, k_ref, s_ref, o_ref, *, width, block):
    chans = x_ref.shape[0]
    classes = k_ref.shape[0]
    head = (k_ref[...], b_ref[pl.ds(2 * chans, classes), :])
    lo, hi, good_cols = s_ref[5], s_ref[6], s_ref[2]
    run_conv(x_ref, w_ref, b_ref[pl.ds(chans, chans), :], lo, hi, good_cols, o_ref, width, block, head)


def pick_block(rows):
    return next(k for k in (4, 3, 2, 1) if rows % k == 0)


def conv_first_layer(feat, top, low, width, weights, biases, limits):
    chans = feat.shape[0]
    rows_main = feat.shape[1] // width
    halo = top.shape[1] // width
    rows_in = rows_main + 2 * halo
    rows_out = rows_in - 2
    outs = weights.shape[2]
    block = pick_block(rows_out)
    vmem = pl.BlockSpec(memory_space=pltpu.VMEM)
    cost = pl.CostEstimate(
        flops=2 * 9 * rows_out * width * chans * outs,
        bytes_accessed=2 * (chans * rows_in * width + weights.size + rows_out * width * outs),
        transcendentals=0,
    )
    out = pl.pallas_call(
        functools.partial(first_body, width=width, block=block, halo=halo),
        out_shape=jax.ShapeDtypeStruct((outs, rows_out * width), jnp.bfloat16),
        in_specs=[vmem] * 5 + [pl.BlockSpec(memory_space=pltpu.SMEM)],
        out_specs=vmem,
        scratch_shapes=[pltpu.VMEM((chans, rows_in * width), jnp.bfloat16)],
        cost_estimate=cost,
    )(
        feat,
        top,
        low,
        weights,
        biases,
        limits,
    )
    return out


def conv_second_layer(x, width, weights, biases, head, limits):
    chans, flat_in = x.shape
    rows_out = flat_in // width - 2
    outs = weights.shape[2]
    classes = head.shape[0]
    block = pick_block(rows_out)
    vmem = pl.BlockSpec(memory_space=pltpu.VMEM)
    cost = pl.CostEstimate(
        flops=2 * 9 * rows_out * width * chans * outs + 2 * rows_out * width * outs * classes,
        bytes_accessed=2 * (x.size + weights.size + rows_out * width * classes),
        transcendentals=0,
    )
    out = pl.pallas_call(
        functools.partial(second_body, width=width, block=block),
        out_shape=jax.ShapeDtypeStruct((classes, rows_out, width), jnp.bfloat16),
        in_specs=[vmem] * 4 + [pl.BlockSpec(memory_space=pltpu.SMEM)],
        out_specs=vmem,
        cost_estimate=cost,
    )(x, weights, biases, head, limits)
    return out


def window_start(numer, first_row, full_rows, out_rows, window_rows):
    valid = full_rows * numer // 14
    numer_pos = (2 * first_row + 1) * valid - out_rows
    lower = numer_pos // (2 * out_rows)
    lower = jnp.where(numer_pos < 0, 0, lower)
    lower = jnp.where(lower >= valid - 1, valid - 1, lower)
    return jnp.clip(lower, 0, full_rows - window_rows)


def column_table(numer, flip, cols, out_cols):
    valid_cols = cols * numer // 14
    col_pos = jnp.arange(out_cols, dtype=jnp.int32)
    col_pos = jnp.where(flip == 1, out_cols - 1 - col_pos, col_pos)
    return resize_matrix(col_pos, out_cols, valid_cols, cols)


def shards(features, views, conv_first, bias_first, conv_second, bias_second, classify, class_bias):
    feat = features[0]
    rows_dev, cols = (feat.shape[1], feat.shape[2])
    spaces = lax.axis_size("space")
    full_rows = rows_dev * spaces
    place = lax.axis_index("space")
    member_index = lax.axis_index("member")
    members = views.shape[0]
    picked = jnp.arange(members, dtype=jnp.int32) == member_index
    code = jnp.sum(jnp.where(picked, views, 0))
    numer = code // 2
    valid_rows = full_rows * numer // 14
    valid_cols = cols * numer // 14
    count = lax.axis_size("space")
    halo = 2
    forward = [(i, i + 1) for i in range(count - 1)]
    backward = [(target, source) for source, target in forward]
    flat_feat = feat.reshape(feat.shape[0], rows_dev * cols)
    top_rows = lax.ppermute(flat_feat[:, (rows_dev - halo) * cols:], "space", forward)
    low_rows = lax.ppermute(flat_feat[:, : halo * cols], "space", backward)
    top = place * rows_dev
    limits = jnp.stack(
        [halo - top, valid_rows - top + halo, valid_cols, 1 - top, valid_rows - top + 1, -top, valid_rows - top]
    ).astype(jnp.int32)
    biases = jnp.concatenate([bias_first, bias_second, class_bias]).reshape(-1, 1)
    hidden = conv_first_layer(flat_feat, top_rows, low_rows, cols, conv_first, biases, limits)
    logits = conv_second_layer(hidden, cols, conv_second, biases, classify, limits)
    out_rows = UP * full_rows
    out_cols = UP * cols
    own_rows = out_rows // spaces
    part_rows = own_rows // members
    window_rows = (part_rows - 1) // UP + 3
    need = block_needs(spaces, members, rows_dev, LOW_CODE, HIGH_CODE)
    gathered = gather_rows(logits, "space", need)
    pieces = []
    for target in range(members):
        first_row = place * own_rows + target * part_rows
        begin = window_start(numer, first_row, full_rows, out_rows, window_rows)
        pieces.append(lax.dynamic_slice_in_dim(gathered, begin, window_rows, 1))
    outgoing = jnp.stack(pieces, 0)
    own_first = place * own_rows + member_index * part_rows
    positions = own_first + jnp.arange(part_rows, dtype=jnp.int32)
    result = jnp.zeros((part_rows, logits.shape[0], out_cols), jnp.float32)
    for shift in range(members):
        if shift == 0:
            arrived = lax.dynamic_index_in_dim(outgoing, member_index, 0, keepdims=False)
        else:
            send = lax.dynamic_index_in_dim(
                outgoing, (member_index + shift) % members, 0, keepdims=False
            )
            arrived = lax.ppermute(
                send, "member", [(i, (i + shift) % members) for i in range(members)]
            )
        source = (member_index - shift) % members
        source_code = jnp.sum(jnp.where(jnp.arange(members) == source, views, 0))
        source_numer = source_code // 2
        source_flip = source_code % 2
        source_valid = full_rows * source_numer // 14
        begin = window_start(source_numer, own_first, full_rows, out_rows, window_rows)
        source_cols = column_table(source_numer, source_flip, cols, out_cols)
        row_table = resize_matrix(positions, out_rows, source_valid, full_rows)
        row_part = lax.dynamic_slice_in_dim(row_table, begin, window_rows, 1)
        widened = jnp.einsum(
            "cyx,jx->cyj", arrived, source_cols, preferred_element_type=jnp.float32
        ).astype(jnp.bfloat16)
        result = result + jnp.einsum(
            "iy,cyj->icj", row_part, widened, preferred_element_type=jnp.float32
        )
    return result


def solution(mesh):
    placed = (
        P(("groups", "member"), None, "space", None),
        P("groups"),
        P(),
        P(),
        P(),
        P(),
        P(),
        P(),
    )
    return jax.shard_map(
        shards,
        mesh=mesh,
        in_specs=placed,
        out_specs=P(("groups", "space", "member"), None, None),
        check_vma=False,
    )
```

```python
import functools

import jax
import jax.numpy as jnp
from jax import lax
from jax.experimental import pallas as pl
from jax.experimental.pallas import tpu as pltpu
from jax.sharding import PartitionSpec as P

UP = 4
LOW_CODE = 8
HIGH_CODE = 29


def with_halo(block, sides, width):
    for axis, dim in sides:
        count = lax.axis_size(axis)
        forward = [(i, i + 1) for i in range(count - 1)]
        backward = [(target, source) for source, target in forward]
        low = lax.ppermute(
            lax.slice_in_dim(block, block.shape[dim] - width, None, axis=dim), axis, forward
        )
        high = lax.ppermute(lax.slice_in_dim(block, 0, width, axis=dim), axis, backward)
        block = jnp.concatenate([low, block, high], axis=dim)
    return block


def gather_rows(block, axis, need):
    count = lax.axis_size(axis)
    if count & (count - 1):
        return lax.all_gather(block, axis, axis=1, tiled=True)
    me = lax.axis_index(axis)
    lead, rows, rest = block.shape[0], block.shape[1], block.shape[2:]
    held = block[:, None]
    bit = count // 2
    while bit:
        span = 2 * bit
        routes = {}
        for p in range(held.shape[1]):
            pairs = []
            for i in range(count):
                j = i ^ bit
                wanted = set().union(*[need[g] for g in range(count) if g // bit == j // bit])
                if p * span + i % span in wanted:
                    pairs.append((i, j))
            routes.setdefault(tuple(pairs), []).append(p)
        if bit == 1 or len(routes) == 1:
            pairs = sorted(set().union(*[set(r) for r in routes]))
            other = lax.ppermute(held, axis, pairs)
        else:
            parts = [None] * held.shape[1]
            for pairs, places in routes.items():
                if pairs:
                    for p in places:
                        parts[p] = lax.ppermute(held[:, p:p + 1], axis, list(pairs))
            empty = jnp.zeros_like(held[:, :1])
            other = jnp.concatenate([empty if x is None else x for x in parts], 1)
        upper = (me & bit) != 0
        held = jnp.where(upper, jnp.stack([other, held], 2), jnp.stack([held, other], 2))
        held = held.reshape((lead, -1, rows) + rest)
        bit //= 2
    return held.reshape((lead, count * rows) + rest)


def block_needs(spaces, members, rows_dev, low_code, high_code):
    full_rows = rows_dev * spaces
    out_rows = UP * full_rows
    own_rows = out_rows // spaces
    part_rows = own_rows // members
    window_rows = (part_rows - 1) // UP + 3
    need = []
    for place in range(spaces):
        blocks = set()
        for numer in range(low_code // 2, high_code // 2 + 1):
            valid = full_rows * numer // 14
            for target in range(members):
                first_row = place * own_rows + target * part_rows
                pos = (2 * first_row + 1) * valid - out_rows
                lower = 0 if pos < 0 else pos // (2 * out_rows)
                lower = valid - 1 if lower >= valid - 1 else lower
                begin = min(max(lower, 0), full_rows - window_rows)
                blocks |= set(range(begin // rows_dev, (begin + window_rows - 1) // rows_dev + 1))
        need.append(blocks)
    return need


def resize_matrix(positions, out_len, valid, in_len):
    numer = (2 * positions + 1) * valid - out_len
    denom = 2 * out_len
    lower = numer // denom
    frac = (numer - lower * denom).astype(jnp.float32) / denom
    below = numer < 0
    frac = jnp.where(below, jnp.float32(0.0), frac)
    lower = jnp.where(below, 0, lower)
    top_index = valid - 1
    over = lower >= top_index
    frac = jnp.where(over, jnp.float32(0.0), frac)
    lower = jnp.where(over, top_index, lower)
    columns = jnp.arange(in_len, dtype=jnp.int32)
    first = jnp.where(columns[None, :] == lower[:, None], 1.0 - frac[:, None], jnp.float32(0.0))
    second = jnp.where(columns[None, :] == lower[:, None] + 1, frac[:, None], jnp.float32(0.0))
    return (first + second).astype(jnp.bfloat16)


def run_conv(x_ref, w_ref, bias, lo, hi, good_cols, o_ref, width, block, head=None):
    flat = block * width
    outs = w_ref.shape[2]
    place = lax.broadcasted_iota(jnp.int32, (1, flat), 1)
    col = place % width
    stacked = jnp.concatenate(
        [jnp.concatenate([w_ref[a, b] for a in range(3)], axis=1) for b in range(3)], axis=0
    )

    def step(i, carry):
        r0 = i * block
        rhs = jnp.concatenate(
            [x_ref[:, pl.ds(pl.multiple_of((r0 + a) * width, width), flat)] for a in range(3)],
            axis=0,
        )
        res = jnp.dot(stacked, rhs, preferred_element_type=jnp.float32)
        taps = [res[b * outs:(b + 1) * outs] for b in range(3)]
        left = jnp.where(col == 0, 0.0, pltpu.roll(taps[0], 1, 1))
        right = jnp.where(col == width - 1, 0.0, pltpu.roll(taps[2], flat - 1, 1))
        total = jnp.maximum(taps[1] + left + right + bias, 0.0)
        row = r0 + place // width
        keep = (row >= lo) & (row < hi) & (col < good_cols)
        out = jnp.where(keep, total, 0.0).astype(jnp.bfloat16)
        if head is not None:
            out = jnp.dot(head[0], out, preferred_element_type=jnp.float32) + head[1]
        o_ref[:, pl.ds(pl.multiple_of(r0 * width, width), flat)] = out.astype(o_ref.dtype)
        return carry

    lax.fori_loop(0, o_ref.shape[1] // flat, step, 0, unroll=True)


def first_body(main_ref, top_ref, low_ref, w_ref, b_ref, s_ref, o_ref, x_ref, *, width, block, halo):
    lo_in, hi_in, good_cols, lo, hi = s_ref[0], s_ref[1], s_ref[2], s_ref[3], s_ref[4]
    chans = main_ref.shape[0]
    rows_main = main_ref.shape[1] // width

    def put(src, offset, rows):
        place = lax.broadcasted_iota(jnp.int32, (1, rows * width), 1)
        row = offset + place // width
        keep = (row >= lo_in) & (row < hi_in) & (place % width < good_cols)
        x_ref[:, pl.ds(pl.multiple_of(offset * width, width), rows * width)] = jnp.where(
            keep, src, jnp.zeros_like(src)
        )

    put(top_ref[...], 0, halo)
    put(low_ref[...], halo + rows_main, halo)

    def chunk(i, carry):
        start = pl.multiple_of(i * 2 * width, width)
        put(main_ref[:, pl.ds(start, 2 * width)], halo + 2 * i, 2)
        return carry

    lax.fori_loop(0, rows_main // 2, chunk, 0)
    run_conv(x_ref, w_ref, b_ref[pl.ds(0, chans), :], lo, hi, good_cols, o_ref, width, block)


def second_body(x_ref, w_ref, b_ref, k_ref, s_ref, o_ref, *, width, block):
    chans = x_ref.shape[0]
    classes = k_ref.shape[0]
    head = (k_ref[...], b_ref[pl.ds(2 * chans, classes), :])
    lo, hi, good_cols = s_ref[5], s_ref[6], s_ref[2]
    run_conv(x_ref, w_ref, b_ref[pl.ds(chans, chans), :], lo, hi, good_cols, o_ref, width, block, head)


def pick_block(rows):
    return next(k for k in (2, 1) if rows % k == 0)


def conv_first_layer(feat, top, low, width, weights, biases, limits):
    chans = feat.shape[0]
    rows_main = feat.shape[1] // width
    halo = top.shape[1] // width
    rows_in = rows_main + 2 * halo
    rows_out = rows_in - 2
    outs = weights.shape[2]
    block = pick_block(rows_out)
    vmem = pl.BlockSpec(memory_space=pltpu.VMEM)
    cost = pl.CostEstimate(
        flops=2 * 9 * rows_out * width * chans * outs,
        bytes_accessed=2 * (chans * rows_in * width + weights.size + rows_out * width * outs),
        transcendentals=0,
    )
    out = pl.pallas_call(
        functools.partial(first_body, width=width, block=block, halo=halo),
        out_shape=jax.ShapeDtypeStruct((outs, rows_out * width), jnp.bfloat16),
        in_specs=[vmem] * 5 + [pl.BlockSpec(memory_space=pltpu.SMEM)],
        out_specs=vmem,
        scratch_shapes=[pltpu.VMEM((chans, rows_in * width), jnp.bfloat16)],
        cost_estimate=cost,
    )(
        feat,
        top,
        low,
        weights,
        biases,
        limits,
    )
    return out


def conv_second_layer(x, width, weights, biases, head, limits):
    chans, flat_in = x.shape
    rows_out = flat_in // width - 2
    outs = weights.shape[2]
    classes = head.shape[0]
    block = pick_block(rows_out)
    vmem = pl.BlockSpec(memory_space=pltpu.VMEM)
    cost = pl.CostEstimate(
        flops=2 * 9 * rows_out * width * chans * outs + 2 * rows_out * width * outs * classes,
        bytes_accessed=2 * (x.size + weights.size + rows_out * width * classes),
        transcendentals=0,
    )
    out = pl.pallas_call(
        functools.partial(second_body, width=width, block=block),
        out_shape=jax.ShapeDtypeStruct((classes, rows_out * width), jnp.bfloat16),
        in_specs=[vmem] * 4 + [pl.BlockSpec(memory_space=pltpu.SMEM)],
        out_specs=vmem,
        cost_estimate=cost,
    )(x, weights, biases, head, limits)
    return out.reshape(classes, rows_out, width)


def window_start(numer, first_row, full_rows, out_rows, window_rows):
    valid = full_rows * numer // 14
    numer_pos = (2 * first_row + 1) * valid - out_rows
    lower = numer_pos // (2 * out_rows)
    lower = jnp.where(numer_pos < 0, 0, lower)
    lower = jnp.where(lower >= valid - 1, valid - 1, lower)
    return jnp.clip(lower, 0, full_rows - window_rows)


def column_table(numer, flip, cols, out_cols):
    valid_cols = cols * numer // 14
    col_pos = jnp.arange(out_cols, dtype=jnp.int32)
    col_pos = jnp.where(flip == 1, out_cols - 1 - col_pos, col_pos)
    return resize_matrix(col_pos, out_cols, valid_cols, cols)


def shards(features, views, conv_first, bias_first, conv_second, bias_second, classify, class_bias):
    feat = features[0]
    rows_dev, cols = (feat.shape[1], feat.shape[2])
    spaces = lax.axis_size("space")
    full_rows = rows_dev * spaces
    place = lax.axis_index("space")
    member_index = lax.axis_index("member")
    members = views.shape[0]
    picked = jnp.arange(members, dtype=jnp.int32) == member_index
    code = jnp.sum(jnp.where(picked, views, 0))
    numer = code // 2
    valid_rows = full_rows * numer // 14
    valid_cols = cols * numer // 14
    count = lax.axis_size("space")
    halo = 2
    forward = [(i, i + 1) for i in range(count - 1)]
    backward = [(target, source) for source, target in forward]
    flat_feat = feat.reshape(feat.shape[0], rows_dev * cols)
    top_rows = lax.ppermute(flat_feat[:, (rows_dev - halo) * cols:], "space", forward)
    low_rows = lax.ppermute(flat_feat[:, : halo * cols], "space", backward)
    top = place * rows_dev
    limits = jnp.stack(
        [halo - top, valid_rows - top + halo, valid_cols, 1 - top, valid_rows - top + 1, -top, valid_rows - top]
    ).astype(jnp.int32)
    biases = jnp.concatenate([bias_first, bias_second, class_bias]).reshape(-1, 1)
    hidden = conv_first_layer(flat_feat, top_rows, low_rows, cols, conv_first, biases, limits)
    logits = conv_second_layer(hidden, cols, conv_second, biases, classify, limits)
    out_rows = UP * full_rows
    out_cols = UP * cols
    own_rows = out_rows // spaces
    part_rows = own_rows // members
    window_rows = (part_rows - 1) // UP + 3
    need = block_needs(spaces, members, rows_dev, LOW_CODE, HIGH_CODE)
    gathered = gather_rows(logits, "space", need)
    pieces = []
    for target in range(members):
        first_row = place * own_rows + target * part_rows
        begin = window_start(numer, first_row, full_rows, out_rows, window_rows)
        pieces.append(lax.dynamic_slice_in_dim(gathered, begin, window_rows, 1))
    outgoing = jnp.stack(pieces, 0)
    own_first = place * own_rows + member_index * part_rows
    positions = own_first + jnp.arange(part_rows, dtype=jnp.int32)
    result = jnp.zeros((part_rows, logits.shape[0], out_cols), jnp.float32)
    for shift in range(members):
        if shift == 0:
            arrived = lax.dynamic_index_in_dim(outgoing, member_index, 0, keepdims=False)
        else:
            send = lax.dynamic_index_in_dim(
                outgoing, (member_index + shift) % members, 0, keepdims=False
            )
            arrived = lax.ppermute(
                send, "member", [(i, (i + shift) % members) for i in range(members)]
            )
        source = (member_index - shift) % members
        source_code = jnp.sum(jnp.where(jnp.arange(members) == source, views, 0))
        source_numer = source_code // 2
        source_flip = source_code % 2
        source_valid = full_rows * source_numer // 14
        begin = window_start(source_numer, own_first, full_rows, out_rows, window_rows)
        source_cols = column_table(source_numer, source_flip, cols, out_cols)
        row_table = resize_matrix(positions, out_rows, source_valid, full_rows)
        row_part = lax.dynamic_slice_in_dim(row_table, begin, window_rows, 1)
        widened = jnp.einsum(
            "cyx,jx->cyj", arrived, source_cols, preferred_element_type=jnp.float32
        ).astype(jnp.bfloat16)
        result = result + jnp.einsum(
            "iy,cyj->icj", row_part, widened, preferred_element_type=jnp.float32
        )
    return result


def solution(mesh):
    placed = (
        P(("groups", "member"), None, "space", None),
        P("groups"),
        P(),
        P(),
        P(),
        P(),
        P(),
        P(),
    )
    return jax.shard_map(
        shards,
        mesh=mesh,
        in_specs=placed,
        out_specs=P(("groups", "space", "member"), None, None),
        check_vma=False,
    )
```

```python
import functools

import jax
import jax.numpy as jnp
from jax import lax
from jax.experimental import pallas as pl
from jax.experimental.pallas import tpu as pltpu
from jax.sharding import PartitionSpec as P

UP = 4
LOW_CODE = 8
HIGH_CODE = 29


def with_halo(block, sides, width):
    for axis, dim in sides:
        count = lax.axis_size(axis)
        forward = [(i, i + 1) for i in range(count - 1)]
        backward = [(target, source) for source, target in forward]
        low = lax.ppermute(
            lax.slice_in_dim(block, block.shape[dim] - width, None, axis=dim), axis, forward
        )
        high = lax.ppermute(lax.slice_in_dim(block, 0, width, axis=dim), axis, backward)
        block = jnp.concatenate([low, block, high], axis=dim)
    return block


def gather_rows(block, axis, need):
    count = lax.axis_size(axis)
    if count & (count - 1):
        return lax.all_gather(block, axis, axis=1, tiled=True)
    me = lax.axis_index(axis)
    lead, rows, rest = block.shape[0], block.shape[1], block.shape[2:]
    held = block[:, None]
    bit = count // 2
    while bit:
        span = 2 * bit
        routes = {}
        for p in range(held.shape[1]):
            pairs = []
            for i in range(count):
                j = i ^ bit
                wanted = set().union(*[need[g] for g in range(count) if g // bit == j // bit])
                if p * span + i % span in wanted:
                    pairs.append((i, j))
            routes.setdefault(tuple(pairs), []).append(p)
        if bit == 1 or len(routes) == 1:
            pairs = sorted(set().union(*[set(r) for r in routes]))
            other = lax.ppermute(held, axis, pairs)
        else:
            parts = [None] * held.shape[1]
            for pairs, places in routes.items():
                if pairs:
                    for p in places:
                        parts[p] = lax.ppermute(held[:, p:p + 1], axis, list(pairs))
            empty = jnp.zeros_like(held[:, :1])
            other = jnp.concatenate([empty if x is None else x for x in parts], 1)
        upper = (me & bit) != 0
        held = jnp.where(upper, jnp.stack([other, held], 2), jnp.stack([held, other], 2))
        held = held.reshape((lead, -1, rows) + rest)
        bit //= 2
    return held.reshape((lead, count * rows) + rest)


def block_needs(spaces, members, rows_dev, low_code, high_code):
    full_rows = rows_dev * spaces
    out_rows = UP * full_rows
    own_rows = out_rows // spaces
    part_rows = own_rows // members
    window_rows = (part_rows - 1) // UP + 3
    need = []
    for place in range(spaces):
        blocks = set()
        for numer in range(low_code // 2, high_code // 2 + 1):
            valid = full_rows * numer // 14
            for target in range(members):
                first_row = place * own_rows + target * part_rows
                pos = (2 * first_row + 1) * valid - out_rows
                lower = 0 if pos < 0 else pos // (2 * out_rows)
                lower = valid - 1 if lower >= valid - 1 else lower
                begin = min(max(lower, 0), full_rows - window_rows)
                blocks |= set(range(begin // rows_dev, (begin + window_rows - 1) // rows_dev + 1))
        need.append(blocks)
    return need


def resize_matrix(positions, out_len, valid, in_len):
    numer = (2 * positions + 1) * valid - out_len
    denom = 2 * out_len
    lower = numer // denom
    frac = (numer - lower * denom).astype(jnp.float32) / denom
    below = numer < 0
    frac = jnp.where(below, jnp.float32(0.0), frac)
    lower = jnp.where(below, 0, lower)
    top_index = valid - 1
    over = lower >= top_index
    frac = jnp.where(over, jnp.float32(0.0), frac)
    lower = jnp.where(over, top_index, lower)
    columns = jnp.arange(in_len, dtype=jnp.int32)
    first = jnp.where(columns[None, :] == lower[:, None], 1.0 - frac[:, None], jnp.float32(0.0))
    second = jnp.where(columns[None, :] == lower[:, None] + 1, frac[:, None], jnp.float32(0.0))
    return (first + second).astype(jnp.bfloat16)


def run_conv(x_ref, w_ref, bias, lo, hi, good_cols, o_ref, width, block, head=None, skip=0):
    flat = block * width
    outs = w_ref.shape[2]
    place = lax.broadcasted_iota(jnp.int32, (1, flat), 1)
    col = place % width
    stacked = jnp.concatenate(
        [jnp.concatenate([w_ref[a, b] for a in range(3)], axis=1) for b in range(3)], axis=0
    )

    def step(i, carry):
        r0 = i * block
        rhs = jnp.concatenate(
            [x_ref[:, pl.ds(pl.multiple_of((skip + r0 + a) * width, width), flat)] for a in range(3)],
            axis=0,
        )
        res = jnp.dot(stacked, rhs, preferred_element_type=jnp.float32)
        taps = [res[b * outs:(b + 1) * outs] for b in range(3)]
        left = jnp.where(col == 0, 0.0, pltpu.roll(taps[0], 1, 1))
        right = jnp.where(col == width - 1, 0.0, pltpu.roll(taps[2], flat - 1, 1))
        total = jnp.maximum(taps[1] + left + right + bias, 0.0)
        row = skip + r0 + place // width
        keep = (row >= lo) & (row < hi) & (col < good_cols)
        out = jnp.where(keep, total, 0.0).astype(jnp.bfloat16)
        if head is not None:
            out = jnp.dot(head[0], out, preferred_element_type=jnp.float32) + head[1]
        o_ref[:, pl.ds(pl.multiple_of(r0 * width, width), flat)] = out.astype(o_ref.dtype)
        return carry

    lax.fori_loop(0, o_ref.shape[1] // flat, step, 0, unroll=True)


def first_body(main_ref, top_ref, low_ref, w_ref, b_ref, s_ref, o_ref, x_ref, *, width, block, halo):
    lo_in, hi_in, good_cols, lo, hi = s_ref[0], s_ref[1], s_ref[2], s_ref[3], s_ref[4]
    chans = main_ref.shape[0]
    rows_main = main_ref.shape[1] // width

    def put(src, offset, rows):
        place = lax.broadcasted_iota(jnp.int32, (1, rows * width), 1)
        row = offset + place // width
        keep = (row >= lo_in) & (row < hi_in) & (place % width < good_cols)
        x_ref[:, pl.ds(pl.multiple_of(offset * width, width), rows * width)] = jnp.where(
            keep, src, jnp.zeros_like(src)
        )

    put(top_ref[...], 0, halo)
    put(low_ref[...], halo + rows_main, halo)

    def chunk(i, carry):
        start = pl.multiple_of(i * 2 * width, width)
        put(main_ref[:, pl.ds(start, 2 * width)], halo + 2 * i, 2)
        return carry

    lax.fori_loop(0, rows_main // 2, chunk, 0)
    run_conv(x_ref, w_ref, b_ref[pl.ds(0, chans), :], lo, hi, good_cols, o_ref, width, block)


def second_body(x_ref, w_ref, b_ref, k_ref, s_ref, o_ref, *, width, block, skip):
    chans = x_ref.shape[0]
    classes = k_ref.shape[0]
    head = (k_ref[...], b_ref[pl.ds(2 * chans, classes), :])
    lo, hi, good_cols = s_ref[5], s_ref[6], s_ref[2]
    run_conv(x_ref, w_ref, b_ref[pl.ds(chans, chans), :], lo, hi, good_cols, o_ref, width, block, head, skip)


def pick_block(rows):
    return next(k for k in (4, 3, 2, 1) if rows % k == 0)


def conv_first_layer(feat, top, low, width, weights, biases, limits):
    chans = feat.shape[0]
    rows_main = feat.shape[1] // width
    halo = top.shape[1] // width
    rows_in = rows_main + 2 * halo
    rows_out = rows_in - 2
    outs = weights.shape[2]
    block = pick_block(rows_out)
    vmem = pl.BlockSpec(memory_space=pltpu.VMEM)
    cost = pl.CostEstimate(
        flops=2 * 9 * rows_out * width * chans * outs,
        bytes_accessed=2 * (chans * rows_in * width + weights.size + rows_out * width * outs),
        transcendentals=0,
    )
    out = pl.pallas_call(
        functools.partial(first_body, width=width, block=block, halo=halo),
        out_shape=jax.ShapeDtypeStruct((outs, rows_out * width), jnp.bfloat16),
        in_specs=[vmem] * 5 + [pl.BlockSpec(memory_space=pltpu.SMEM)],
        out_specs=vmem,
        scratch_shapes=[pltpu.VMEM((chans, rows_in * width), jnp.bfloat16)],
        cost_estimate=cost,
    )(
        feat,
        top,
        low,
        weights,
        biases,
        limits,
    )
    return out


def conv_second_layer(x, width, weights, biases, head, limits, skip, rows_out):
    chans, flat_in = x.shape
    outs = weights.shape[2]
    classes = head.shape[0]
    block = pick_block(rows_out)
    vmem = pl.BlockSpec(memory_space=pltpu.VMEM)
    cost = pl.CostEstimate(
        flops=2 * 9 * rows_out * width * chans * outs + 2 * rows_out * width * outs * classes,
        bytes_accessed=2 * (x.size + weights.size + rows_out * width * classes),
        transcendentals=0,
    )
    out = pl.pallas_call(
        functools.partial(second_body, width=width, block=block, skip=skip),
        out_shape=jax.ShapeDtypeStruct((classes, rows_out * width), jnp.bfloat16),
        in_specs=[vmem] * 4 + [pl.BlockSpec(memory_space=pltpu.SMEM)],
        out_specs=vmem,
        cost_estimate=cost,
    )(x, weights, biases, head, limits)
    return out.reshape(classes, rows_out, width)


def window_start(numer, first_row, full_rows, out_rows, window_rows):
    valid = full_rows * numer // 14
    numer_pos = (2 * first_row + 1) * valid - out_rows
    lower = numer_pos // (2 * out_rows)
    lower = jnp.where(numer_pos < 0, 0, lower)
    lower = jnp.where(lower >= valid - 1, valid - 1, lower)
    return jnp.clip(lower, 0, full_rows - window_rows)


def column_table(numer, flip, cols, out_cols):
    valid_cols = cols * numer // 14
    col_pos = jnp.arange(out_cols, dtype=jnp.int32)
    col_pos = jnp.where(flip == 1, out_cols - 1 - col_pos, col_pos)
    return resize_matrix(col_pos, out_cols, valid_cols, cols)


def shards(features, views, conv_first, bias_first, conv_second, bias_second, classify, class_bias):
    feat = features[0]
    rows_dev, cols = (feat.shape[1], feat.shape[2])
    spaces = lax.axis_size("space")
    full_rows = rows_dev * spaces
    place = lax.axis_index("space")
    member_index = lax.axis_index("member")
    members = views.shape[0]
    picked = jnp.arange(members, dtype=jnp.int32) == member_index
    code = jnp.sum(jnp.where(picked, views, 0))
    numer = code // 2
    valid_rows = full_rows * numer // 14
    valid_cols = cols * numer // 14
    count = lax.axis_size("space")
    halo = 2
    forward = [(i, i + 1) for i in range(count - 1)]
    backward = [(target, source) for source, target in forward]
    flat_feat = feat.reshape(feat.shape[0], rows_dev * cols)
    top_rows = lax.ppermute(flat_feat[:, (rows_dev - halo) * cols:], "space", forward)
    low_rows = lax.ppermute(flat_feat[:, : halo * cols], "space", backward)
    top = place * rows_dev
    limits = jnp.stack(
        [halo - top, valid_rows - top + halo, valid_cols, 1 - top, valid_rows - top + 1, -top, valid_rows - top]
    ).astype(jnp.int32)
    biases = jnp.concatenate([bias_first, bias_second, class_bias]).reshape(-1, 1)
    hidden = conv_first_layer(flat_feat, top_rows, low_rows, cols, conv_first, biases, limits)
    half = rows_dev // 2 if rows_dev % 4 == 0 else rows_dev
    logit_parts = [
        conv_second_layer(hidden, cols, conv_second, biases, classify, limits, skip, half)
        for skip in range(0, rows_dev, half)
    ]
    out_rows = UP * full_rows
    out_cols = UP * cols
    own_rows = out_rows // spaces
    part_rows = own_rows // members
    window_rows = (part_rows - 1) // UP + 3
    need = block_needs(spaces, members, rows_dev, LOW_CODE, HIGH_CODE)
    gathered = jnp.stack(
        [gather_rows(x, "space", need).reshape(x.shape[0], spaces, half, cols) for x in logit_parts], 2
    ).reshape(classify.shape[0], full_rows, cols)
    pieces = []
    for target in range(members):
        first_row = place * own_rows + target * part_rows
        begin = window_start(numer, first_row, full_rows, out_rows, window_rows)
        pieces.append(lax.dynamic_slice_in_dim(gathered, begin, window_rows, 1))
    outgoing = jnp.stack(pieces, 0)
    own_first = place * own_rows + member_index * part_rows
    positions = own_first + jnp.arange(part_rows, dtype=jnp.int32)
    result = jnp.zeros((part_rows, classify.shape[0], out_cols), jnp.float32)
    for shift in range(members):
        if shift == 0:
            arrived = lax.dynamic_index_in_dim(outgoing, member_index, 0, keepdims=False)
        else:
            send = lax.dynamic_index_in_dim(
                outgoing, (member_index + shift) % members, 0, keepdims=False
            )
            arrived = lax.ppermute(
                send, "member", [(i, (i + shift) % members) for i in range(members)]
            )
        source = (member_index - shift) % members
        source_code = jnp.sum(jnp.where(jnp.arange(members) == source, views, 0))
        source_numer = source_code // 2
        source_flip = source_code % 2
        source_valid = full_rows * source_numer // 14
        begin = window_start(source_numer, own_first, full_rows, out_rows, window_rows)
        source_cols = column_table(source_numer, source_flip, cols, out_cols)
        row_table = resize_matrix(positions, out_rows, source_valid, full_rows)
        row_part = lax.dynamic_slice_in_dim(row_table, begin, window_rows, 1)
        widened = jnp.einsum(
            "cyx,jx->cyj", arrived, source_cols, preferred_element_type=jnp.float32
        ).astype(jnp.bfloat16)
        result = result + jnp.einsum(
            "iy,cyj->icj", row_part, widened, preferred_element_type=jnp.float32
        )
    return result


def solution(mesh):
    placed = (
        P(("groups", "member"), None, "space", None),
        P("groups"),
        P(),
        P(),
        P(),
        P(),
        P(),
        P(),
    )
    return jax.shard_map(
        shards,
        mesh=mesh,
        in_specs=placed,
        out_specs=P(("groups", "space", "member"), None, None),
        check_vma=False,
    )
```

```python
import functools

import jax
import jax.numpy as jnp
from jax import lax
from jax.experimental import pallas as pl
from jax.experimental.pallas import tpu as pltpu
from jax.sharding import PartitionSpec as P

UP = 4
LOW_CODE = 8
HIGH_CODE = 29


def with_halo(block, sides, width):
    for axis, dim in sides:
        count = lax.axis_size(axis)
        forward = [(i, i + 1) for i in range(count - 1)]
        backward = [(target, source) for source, target in forward]
        low = lax.ppermute(
            lax.slice_in_dim(block, block.shape[dim] - width, None, axis=dim), axis, forward
        )
        high = lax.ppermute(lax.slice_in_dim(block, 0, width, axis=dim), axis, backward)
        block = jnp.concatenate([low, block, high], axis=dim)
    return block


def gather_rows(block, axis, need):
    count = lax.axis_size(axis)
    if count & (count - 1):
        return lax.all_gather(block, axis, axis=1, tiled=True)
    me = lax.axis_index(axis)
    lead, rows, rest = block.shape[0], block.shape[1], block.shape[2:]
    held = block[:, None]
    bit = count // 2
    while bit:
        span = 2 * bit
        routes = {}
        for p in range(held.shape[1]):
            pairs = []
            for i in range(count):
                j = i ^ bit
                wanted = set().union(*[need[g] for g in range(count) if g // bit == j // bit])
                if p * span + i % span in wanted:
                    pairs.append((i, j))
            routes.setdefault(tuple(pairs), []).append(p)
        if bit == 1 or len(routes) == 1:
            pairs = sorted(set().union(*[set(r) for r in routes]))
            other = lax.ppermute(held, axis, pairs)
        else:
            parts = [None] * held.shape[1]
            for pairs, places in routes.items():
                if pairs:
                    for p in places:
                        parts[p] = lax.ppermute(held[:, p:p + 1], axis, list(pairs))
            empty = jnp.zeros_like(held[:, :1])
            other = jnp.concatenate([empty if x is None else x for x in parts], 1)
        upper = (me & bit) != 0
        held = jnp.where(upper, jnp.stack([other, held], 2), jnp.stack([held, other], 2))
        held = held.reshape((lead, -1, rows) + rest)
        bit //= 2
    return held.reshape((lead, count * rows) + rest)


def block_needs(spaces, members, rows_dev, low_code, high_code):
    full_rows = rows_dev * spaces
    out_rows = UP * full_rows
    own_rows = out_rows // spaces
    part_rows = own_rows // members
    window_rows = (part_rows - 1) // UP + 3
    need = []
    for place in range(spaces):
        blocks = set()
        for numer in range(low_code // 2, high_code // 2 + 1):
            valid = full_rows * numer // 14
            for target in range(members):
                first_row = place * own_rows + target * part_rows
                pos = (2 * first_row + 1) * valid - out_rows
                lower = 0 if pos < 0 else pos // (2 * out_rows)
                lower = valid - 1 if lower >= valid - 1 else lower
                begin = min(max(lower, 0), full_rows - window_rows)
                blocks |= set(range(begin // rows_dev, (begin + window_rows - 1) // rows_dev + 1))
        need.append(blocks)
    return need


def resize_matrix(positions, out_len, valid, in_len):
    numer = (2 * positions + 1) * valid - out_len
    denom = 2 * out_len
    lower = numer // denom
    frac = (numer - lower * denom).astype(jnp.float32) / denom
    below = numer < 0
    frac = jnp.where(below, jnp.float32(0.0), frac)
    lower = jnp.where(below, 0, lower)
    top_index = valid - 1
    over = lower >= top_index
    frac = jnp.where(over, jnp.float32(0.0), frac)
    lower = jnp.where(over, top_index, lower)
    columns = jnp.arange(in_len, dtype=jnp.int32)
    first = jnp.where(columns[None, :] == lower[:, None], 1.0 - frac[:, None], jnp.float32(0.0))
    second = jnp.where(columns[None, :] == lower[:, None] + 1, frac[:, None], jnp.float32(0.0))
    return (first + second).astype(jnp.bfloat16)


def run_conv(x_ref, w_ref, bias, lo, hi, good_cols, o_ref, width, block, head=None):
    flat = block * width
    outs = w_ref.shape[2]
    place = lax.broadcasted_iota(jnp.int32, (1, flat), 1)
    col = place % width
    stacked = jnp.concatenate(
        [jnp.concatenate([w_ref[a, b] for a in range(3)], axis=1) for b in range(3)], axis=0
    )

    def step(i, carry):
        r0 = i * block
        rhs = jnp.concatenate(
            [x_ref[:, pl.ds(pl.multiple_of((r0 + a) * width, width), flat)] for a in range(3)],
            axis=0,
        )
        res = jnp.dot(stacked, rhs, preferred_element_type=jnp.float32)
        taps = [res[b * outs:(b + 1) * outs] for b in range(3)]
        left = jnp.where(col == 0, 0.0, pltpu.roll(taps[0], 1, 1))
        right = jnp.where(col == width - 1, 0.0, pltpu.roll(taps[2], flat - 1, 1))
        total = jnp.maximum(taps[1] + left + right + bias, 0.0)
        row = r0 + place // width
        keep = (row >= lo) & (row < hi) & (col < good_cols)
        out = jnp.where(keep, total, 0.0).astype(jnp.bfloat16)
        if head is not None:
            out = jnp.dot(head[0], out, preferred_element_type=jnp.float32) + head[1]
        o_ref[:, pl.ds(pl.multiple_of(r0 * width, width), flat)] = out.astype(o_ref.dtype)
        return carry

    lax.fori_loop(0, o_ref.shape[1] // flat, step, 0, unroll=True)


def first_body(
    main_ref, top_ref, low_ref, w_ref, b_ref, s_ref, o_ref, x_ref, top_buf, low_buf, sems, *, width, block, halo
):
    lo_in, hi_in, good_cols, lo, hi = s_ref[0], s_ref[1], s_ref[2], s_ref[3], s_ref[4]
    chans = main_ref.shape[0]
    rows_main = main_ref.shape[1] // width

    def put(src, offset, rows):
        place = lax.broadcasted_iota(jnp.int32, (1, rows * width), 1)
        row = offset + place // width
        keep = (row >= lo_in) & (row < hi_in) & (place % width < good_cols)
        x_ref[:, pl.ds(pl.multiple_of(offset * width, width), rows * width)] = jnp.where(
            keep, src, jnp.zeros_like(src)
        )

    fetch_top = pltpu.make_async_copy(top_ref, top_buf, sems.at[0])
    fetch_low = pltpu.make_async_copy(low_ref, low_buf, sems.at[1])
    fetch_top.start()
    fetch_low.start()

    def chunk(i, carry):
        start = pl.multiple_of(i * 2 * width, width)
        put(main_ref[:, pl.ds(start, 2 * width)], halo + 2 * i, 2)
        return carry

    lax.fori_loop(0, rows_main // 2, chunk, 0)
    fetch_top.wait()
    fetch_low.wait()
    put(top_buf[...], 0, halo)
    put(low_buf[...], halo + rows_main, halo)
    run_conv(x_ref, w_ref, b_ref[pl.ds(0, chans), :], lo, hi, good_cols, o_ref, width, block)


def second_body(x_ref, w_ref, b_ref, k_ref, s_ref, o_ref, *, width, block):
    chans = x_ref.shape[0]
    classes = k_ref.shape[0]
    head = (k_ref[...], b_ref[pl.ds(2 * chans, classes), :])
    lo, hi, good_cols = s_ref[5], s_ref[6], s_ref[2]
    run_conv(x_ref, w_ref, b_ref[pl.ds(chans, chans), :], lo, hi, good_cols, o_ref, width, block, head)


def pick_block(rows):
    return next(k for k in (4, 3, 2, 1) if rows % k == 0)


def conv_first_layer(feat, top, low, width, weights, biases, limits):
    chans = feat.shape[0]
    rows_main = feat.shape[1] // width
    halo = top.shape[1] // width
    rows_in = rows_main + 2 * halo
    rows_out = rows_in - 2
    outs = weights.shape[2]
    block = pick_block(rows_out)
    vmem = pl.BlockSpec(memory_space=pltpu.VMEM)
    anywhere = pl.BlockSpec(memory_space=pl.ANY)
    cost = pl.CostEstimate(
        flops=2 * 9 * rows_out * width * chans * outs,
        bytes_accessed=2 * (chans * rows_in * width + weights.size + rows_out * width * outs),
        transcendentals=0,
    )
    out = pl.pallas_call(
        functools.partial(first_body, width=width, block=block, halo=halo),
        out_shape=jax.ShapeDtypeStruct((outs, rows_out * width), jnp.bfloat16),
        in_specs=[vmem, anywhere, anywhere, vmem, vmem, pl.BlockSpec(memory_space=pltpu.SMEM)],
        out_specs=vmem,
        scratch_shapes=[
            pltpu.VMEM((chans, rows_in * width), jnp.bfloat16),
            pltpu.VMEM((chans, halo * width), jnp.bfloat16),
            pltpu.VMEM((chans, halo * width), jnp.bfloat16),
            pltpu.SemaphoreType.DMA((2,)),
        ],
        cost_estimate=cost,
    )(
        feat,
        top,
        low,
        weights,
        biases,
        limits,
    )
    return out


def conv_second_layer(x, width, weights, biases, head, limits):
    chans, flat_in = x.shape
    rows_out = flat_in // width - 2
    outs = weights.shape[2]
    classes = head.shape[0]
    block = pick_block(rows_out)
    vmem = pl.BlockSpec(memory_space=pltpu.VMEM)
    cost = pl.CostEstimate(
        flops=2 * 9 * rows_out * width * chans * outs + 2 * rows_out * width * outs * classes,
        bytes_accessed=2 * (x.size + weights.size + rows_out * width * classes),
        transcendentals=0,
    )
    out = pl.pallas_call(
        functools.partial(second_body, width=width, block=block),
        out_shape=jax.ShapeDtypeStruct((classes, rows_out * width), jnp.bfloat16),
        in_specs=[vmem] * 4 + [pl.BlockSpec(memory_space=pltpu.SMEM)],
        out_specs=vmem,
        cost_estimate=cost,
    )(x, weights, biases, head, limits)
    return out.reshape(classes, rows_out, width)


def window_start(numer, first_row, full_rows, out_rows, window_rows):
    valid = full_rows * numer // 14
    numer_pos = (2 * first_row + 1) * valid - out_rows
    lower = numer_pos // (2 * out_rows)
    lower = jnp.where(numer_pos < 0, 0, lower)
    lower = jnp.where(lower >= valid - 1, valid - 1, lower)
    return jnp.clip(lower, 0, full_rows - window_rows)


def column_table(numer, flip, cols, out_cols):
    valid_cols = cols * numer // 14
    col_pos = jnp.arange(out_cols, dtype=jnp.int32)
    col_pos = jnp.where(flip == 1, out_cols - 1 - col_pos, col_pos)
    return resize_matrix(col_pos, out_cols, valid_cols, cols)


def shards(features, views, conv_first, bias_first, conv_second, bias_second, classify, class_bias):
    feat = features[0]
    rows_dev, cols = (feat.shape[1], feat.shape[2])
    spaces = lax.axis_size("space")
    full_rows = rows_dev * spaces
    place = lax.axis_index("space")
    member_index = lax.axis_index("member")
    members = views.shape[0]
    picked = jnp.arange(members, dtype=jnp.int32) == member_index
    code = jnp.sum(jnp.where(picked, views, 0))
    numer = code // 2
    valid_rows = full_rows * numer // 14
    valid_cols = cols * numer // 14
    count = lax.axis_size("space")
    halo = 2
    forward = [(i, i + 1) for i in range(count - 1)]
    backward = [(target, source) for source, target in forward]
    flat_feat = feat.reshape(feat.shape[0], rows_dev * cols)
    top_rows = lax.ppermute(flat_feat[:, (rows_dev - halo) * cols:], "space", forward)
    low_rows = lax.ppermute(flat_feat[:, : halo * cols], "space", backward)
    top = place * rows_dev
    limits = jnp.stack(
        [halo - top, valid_rows - top + halo, valid_cols, 1 - top, valid_rows - top + 1, -top, valid_rows - top]
    ).astype(jnp.int32)
    biases = jnp.concatenate([bias_first, bias_second, class_bias]).reshape(-1, 1)
    hidden = conv_first_layer(flat_feat, top_rows, low_rows, cols, conv_first, biases, limits)
    logits = conv_second_layer(hidden, cols, conv_second, biases, classify, limits)
    out_rows = UP * full_rows
    out_cols = UP * cols
    own_rows = out_rows // spaces
    part_rows = own_rows // members
    window_rows = (part_rows - 1) // UP + 3
    need = block_needs(spaces, members, rows_dev, LOW_CODE, HIGH_CODE)
    gathered = gather_rows(logits, "space", need)
    pieces = []
    for target in range(members):
        first_row = place * own_rows + target * part_rows
        begin = window_start(numer, first_row, full_rows, out_rows, window_rows)
        pieces.append(lax.dynamic_slice_in_dim(gathered, begin, window_rows, 1))
    outgoing = jnp.stack(pieces, 0)
    own_first = place * own_rows + member_index * part_rows
    positions = own_first + jnp.arange(part_rows, dtype=jnp.int32)
    result = jnp.zeros((part_rows, logits.shape[0], out_cols), jnp.float32)
    for shift in range(members):
        if shift == 0:
            arrived = lax.dynamic_index_in_dim(outgoing, member_index, 0, keepdims=False)
        else:
            send = lax.dynamic_index_in_dim(
                outgoing, (member_index + shift) % members, 0, keepdims=False
            )
            arrived = lax.ppermute(
                send, "member", [(i, (i + shift) % members) for i in range(members)]
            )
        source = (member_index - shift) % members
        source_code = jnp.sum(jnp.where(jnp.arange(members) == source, views, 0))
        source_numer = source_code // 2
        source_flip = source_code % 2
        source_valid = full_rows * source_numer // 14
        begin = window_start(source_numer, own_first, full_rows, out_rows, window_rows)
        source_cols = column_table(source_numer, source_flip, cols, out_cols)
        row_table = resize_matrix(positions, out_rows, source_valid, full_rows)
        row_part = lax.dynamic_slice_in_dim(row_table, begin, window_rows, 1)
        widened = jnp.einsum(
            "cyx,jx->cyj", arrived, source_cols, preferred_element_type=jnp.float32
        ).astype(jnp.bfloat16)
        result = result + jnp.einsum(
            "iy,cyj->icj", row_part, widened, preferred_element_type=jnp.float32
        )
    return result


def solution(mesh):
    placed = (
        P(("groups", "member"), None, "space", None),
        P("groups"),
        P(),
        P(),
        P(),
        P(),
        P(),
        P(),
    )
    return jax.shard_map(
        shards,
        mesh=mesh,
        in_specs=placed,
        out_specs=P(("groups", "space", "member"), None, None),
        check_vma=False,
    )
```

```python
import functools

import jax
import jax.numpy as jnp
from jax import lax
from jax.experimental import pallas as pl
from jax.experimental.pallas import tpu as pltpu
from jax.sharding import PartitionSpec as P

UP = 4
LOW_CODE = 8
HIGH_CODE = 29


def with_halo(block, sides, width):
    for axis, dim in sides:
        count = lax.axis_size(axis)
        forward = [(i, i + 1) for i in range(count - 1)]
        backward = [(target, source) for source, target in forward]
        low = lax.ppermute(
            lax.slice_in_dim(block, block.shape[dim] - width, None, axis=dim), axis, forward
        )
        high = lax.ppermute(lax.slice_in_dim(block, 0, width, axis=dim), axis, backward)
        block = jnp.concatenate([low, block, high], axis=dim)
    return block


def gather_rows(block, axis, need):
    count = lax.axis_size(axis)
    if count & (count - 1):
        return lax.all_gather(block, axis, axis=1, tiled=True)
    me = lax.axis_index(axis)
    lead, rows, rest = block.shape[0], block.shape[1], block.shape[2:]
    held = block[:, None]
    bit = count // 2
    while bit:
        span = 2 * bit
        routes = {}
        for p in range(held.shape[1]):
            pairs = []
            for i in range(count):
                j = i ^ bit
                wanted = set().union(*[need[g] for g in range(count) if g // bit == j // bit])
                if p * span + i % span in wanted:
                    pairs.append((i, j))
            routes.setdefault(tuple(pairs), []).append(p)
        if bit == 1 or len(routes) == 1:
            pairs = sorted(set().union(*[set(r) for r in routes]))
            other = lax.ppermute(held, axis, pairs)
        else:
            parts = [None] * held.shape[1]
            for pairs, places in routes.items():
                if pairs:
                    for p in places:
                        parts[p] = lax.ppermute(held[:, p:p + 1], axis, list(pairs))
            empty = jnp.zeros_like(held[:, :1])
            other = jnp.concatenate([empty if x is None else x for x in parts], 1)
        upper = (me & bit) != 0
        held = jnp.where(upper, jnp.stack([other, held], 2), jnp.stack([held, other], 2))
        held = held.reshape((lead, -1, rows) + rest)
        bit //= 2
    return held.reshape((lead, count * rows) + rest)


def block_needs(spaces, members, rows_dev, low_code, high_code):
    full_rows = rows_dev * spaces
    out_rows = UP * full_rows
    own_rows = out_rows // spaces
    part_rows = own_rows // members
    window_rows = (part_rows - 1) // UP + 3
    need = []
    for place in range(spaces):
        blocks = set()
        for numer in range(low_code // 2, high_code // 2 + 1):
            valid = full_rows * numer // 14
            for target in range(members):
                first_row = place * own_rows + target * part_rows
                pos = (2 * first_row + 1) * valid - out_rows
                lower = 0 if pos < 0 else pos // (2 * out_rows)
                lower = valid - 1 if lower >= valid - 1 else lower
                begin = min(max(lower, 0), full_rows - window_rows)
                blocks |= set(range(begin // rows_dev, (begin + window_rows - 1) // rows_dev + 1))
        need.append(blocks)
    return need


def resize_matrix(positions, out_len, valid, in_len):
    numer = (2 * positions + 1) * valid - out_len
    denom = 2 * out_len
    lower = numer // denom
    frac = (numer - lower * denom).astype(jnp.float32) / denom
    below = numer < 0
    frac = jnp.where(below, jnp.float32(0.0), frac)
    lower = jnp.where(below, 0, lower)
    top_index = valid - 1
    over = lower >= top_index
    frac = jnp.where(over, jnp.float32(0.0), frac)
    lower = jnp.where(over, top_index, lower)
    columns = jnp.arange(in_len, dtype=jnp.int32)
    first = jnp.where(columns[None, :] == lower[:, None], 1.0 - frac[:, None], jnp.float32(0.0))
    second = jnp.where(columns[None, :] == lower[:, None] + 1, frac[:, None], jnp.float32(0.0))
    return (first + second).astype(jnp.bfloat16)


def run_conv(x_ref, w_ref, bias, lo, hi, good_cols, o_ref, width, block, head=None):
    flat = block * width
    outs = w_ref.shape[2]
    place = lax.broadcasted_iota(jnp.int32, (1, flat), 1)
    col = place % width
    stacked = jnp.concatenate(
        [jnp.concatenate([w_ref[a, b] for a in range(3)], axis=1) for b in range(3)], axis=0
    )

    def step(i, carry):
        r0 = i * block
        rhs = jnp.concatenate(
            [x_ref[:, pl.ds(pl.multiple_of((r0 + a) * width, width), flat)] for a in range(3)],
            axis=0,
        )
        res = jnp.dot(stacked, rhs, preferred_element_type=jnp.float32)
        taps = [res[b * outs:(b + 1) * outs] for b in range(3)]
        left = jnp.where(col == 0, 0.0, pltpu.roll(taps[0], 1, 1))
        right = jnp.where(col == width - 1, 0.0, pltpu.roll(taps[2], flat - 1, 1))
        total = jnp.maximum(taps[1] + left + right + bias, 0.0)
        row = r0 + place // width
        keep = (row >= lo) & (row < hi) & (col < good_cols)
        out = jnp.where(keep, total, 0.0).astype(jnp.bfloat16)
        if head is not None:
            out = jnp.dot(head[0], out, preferred_element_type=jnp.float32) + head[1]
        o_ref[:, pl.ds(pl.multiple_of(r0 * width, width), flat)] = out.astype(o_ref.dtype)
        return carry

    lax.fori_loop(0, o_ref.shape[1] // flat, step, 0, unroll=True)


def first_body(main_ref, top_ref, low_ref, w_ref, b_ref, s_ref, o_ref, x_ref, *, width, block, halo):
    lo_in, hi_in, good_cols, lo, hi = s_ref[0], s_ref[1], s_ref[2], s_ref[3], s_ref[4]
    chans = main_ref.shape[0]
    rows_main = main_ref.shape[1] // width

    def put(src, offset, rows):
        place = lax.broadcasted_iota(jnp.int32, (1, rows * width), 1)
        row = offset + place // width
        keep = (row >= lo_in) & (row < hi_in) & (place % width < good_cols)
        x_ref[:, pl.ds(pl.multiple_of(offset * width, width), rows * width)] = jnp.where(
            keep, src, jnp.zeros_like(src)
        )

    put(top_ref[...], 0, halo)
    put(low_ref[...], halo + rows_main, halo)

    def chunk(i, carry):
        start = pl.multiple_of(i * 2 * width, width)
        put(main_ref[:, pl.ds(start, 2 * width)], halo + 2 * i, 2)
        return carry

    lax.fori_loop(0, rows_main // 2, chunk, 0)
    run_conv(x_ref, w_ref, b_ref[pl.ds(0, chans), 0:1], lo, hi, good_cols, o_ref, width, block)


def second_body(x_ref, w_ref, b_ref, k_ref, s_ref, o_ref, *, width, block):
    chans = x_ref.shape[0]
    classes = k_ref.shape[0]
    head = (k_ref[...], b_ref[pl.ds(2 * chans, classes), 0:1])
    lo, hi, good_cols = s_ref[5], s_ref[6], s_ref[2]
    run_conv(x_ref, w_ref, b_ref[pl.ds(chans, chans), 0:1], lo, hi, good_cols, o_ref, width, block, head)


def pick_block(rows):
    return next(k for k in (4, 3, 2, 1) if rows % k == 0)


def conv_first_layer(feat, top, low, width, weights, biases, limits):
    chans = feat.shape[0]
    rows_main = feat.shape[1] // width
    halo = top.shape[1] // width
    rows_in = rows_main + 2 * halo
    rows_out = rows_in - 2
    outs = weights.shape[2]
    block = pick_block(rows_out)
    vmem = pl.BlockSpec(memory_space=pltpu.VMEM)
    cost = pl.CostEstimate(
        flops=2 * 9 * rows_out * width * chans * outs,
        bytes_accessed=2 * (chans * rows_in * width + weights.size + rows_out * width * outs),
        transcendentals=0,
    )
    out = pl.pallas_call(
        functools.partial(first_body, width=width, block=block, halo=halo),
        out_shape=jax.ShapeDtypeStruct((outs, rows_out * width), jnp.bfloat16),
        in_specs=[vmem] * 5 + [pl.BlockSpec(memory_space=pltpu.SMEM)],
        out_specs=vmem,
        scratch_shapes=[pltpu.VMEM((chans, rows_in * width), jnp.bfloat16)],
        cost_estimate=cost,
    )(
        feat,
        top,
        low,
        weights,
        biases,
        limits,
    )
    return out


def conv_second_layer(x, width, weights, biases, head, limits):
    chans, flat_in = x.shape
    rows_out = flat_in // width - 2
    outs = weights.shape[2]
    classes = head.shape[0]
    block = pick_block(rows_out)
    vmem = pl.BlockSpec(memory_space=pltpu.VMEM)
    cost = pl.CostEstimate(
        flops=2 * 9 * rows_out * width * chans * outs + 2 * rows_out * width * outs * classes,
        bytes_accessed=2 * (x.size + weights.size + rows_out * width * classes),
        transcendentals=0,
    )
    out = pl.pallas_call(
        functools.partial(second_body, width=width, block=block),
        out_shape=jax.ShapeDtypeStruct((classes, rows_out * width), jnp.bfloat16),
        in_specs=[vmem] * 4 + [pl.BlockSpec(memory_space=pltpu.SMEM)],
        out_specs=vmem,
        cost_estimate=cost,
    )(x, weights, biases, head, limits)
    return out.reshape(classes, rows_out, width)


def window_start(numer, first_row, full_rows, out_rows, window_rows):
    valid = full_rows * numer // 14
    numer_pos = (2 * first_row + 1) * valid - out_rows
    lower = numer_pos // (2 * out_rows)
    lower = jnp.where(numer_pos < 0, 0, lower)
    lower = jnp.where(lower >= valid - 1, valid - 1, lower)
    return jnp.clip(lower, 0, full_rows - window_rows)


def column_table(numer, flip, cols, out_cols):
    valid_cols = cols * numer // 14
    col_pos = jnp.arange(out_cols, dtype=jnp.int32)
    col_pos = jnp.where(flip == 1, out_cols - 1 - col_pos, col_pos)
    return resize_matrix(col_pos, out_cols, valid_cols, cols)


def shards(features, views, conv_first, bias_first, conv_second, bias_second, classify, class_bias):
    feat = features[0]
    rows_dev, cols = (feat.shape[1], feat.shape[2])
    spaces = lax.axis_size("space")
    full_rows = rows_dev * spaces
    place = lax.axis_index("space")
    member_index = lax.axis_index("member")
    members = views.shape[0]
    picked = jnp.arange(members, dtype=jnp.int32) == member_index
    code = jnp.sum(jnp.where(picked, views, 0))
    numer = code // 2
    valid_rows = full_rows * numer // 14
    valid_cols = cols * numer // 14
    count = lax.axis_size("space")
    halo = 2
    forward = [(i, i + 1) for i in range(count - 1)]
    backward = [(target, source) for source, target in forward]
    flat_feat = feat.reshape(feat.shape[0], rows_dev * cols)
    top_rows = lax.ppermute(flat_feat[:, (rows_dev - halo) * cols:], "space", forward)
    low_rows = lax.ppermute(flat_feat[:, : halo * cols], "space", backward)
    top = place * rows_dev
    offsets = jnp.array([halo, halo, 0, 1, 1, 0, 0], jnp.int32)
    of_top = jnp.array([-1, -1, 0, -1, -1, -1, -1], jnp.int32)
    of_rows = jnp.array([0, 1, 0, 0, 1, 0, 1], jnp.int32)
    of_cols = jnp.array([0, 0, 1, 0, 0, 0, 0], jnp.int32)
    limits = offsets + of_top * top + of_rows * valid_rows + of_cols * valid_cols
    biases = jnp.concatenate([bias_first, bias_second, class_bias])
    biases = jnp.broadcast_to(biases[:, None], (biases.shape[0], 128))
    hidden = conv_first_layer(flat_feat, top_rows, low_rows, cols, conv_first, biases, limits)
    logits = conv_second_layer(hidden, cols, conv_second, biases, classify, limits)
    out_rows = UP * full_rows
    out_cols = UP * cols
    own_rows = out_rows // spaces
    part_rows = own_rows // members
    window_rows = (part_rows - 1) // UP + 3
    need = block_needs(spaces, members, rows_dev, LOW_CODE, HIGH_CODE)
    gathered = gather_rows(logits, "space", need)
    pieces = []
    for target in range(members):
        first_row = place * own_rows + target * part_rows
        begin = window_start(numer, first_row, full_rows, out_rows, window_rows)
        pieces.append(lax.dynamic_slice_in_dim(gathered, begin, window_rows, 1))
    outgoing = jnp.stack(pieces, 0)
    own_first = place * own_rows + member_index * part_rows
    positions = own_first + jnp.arange(part_rows, dtype=jnp.int32)
    result = jnp.zeros((part_rows, logits.shape[0], out_cols), jnp.float32)
    for shift in range(members):
        if shift == 0:
            arrived = lax.dynamic_index_in_dim(outgoing, member_index, 0, keepdims=False)
        else:
            send = lax.dynamic_index_in_dim(
                outgoing, (member_index + shift) % members, 0, keepdims=False
            )
            arrived = lax.ppermute(
                send, "member", [(i, (i + shift) % members) for i in range(members)]
            )
        source = (member_index - shift) % members
        source_code = jnp.sum(jnp.where(jnp.arange(members) == source, views, 0))
        source_numer = source_code // 2
        source_flip = source_code % 2
        source_valid = full_rows * source_numer // 14
        begin = window_start(source_numer, own_first, full_rows, out_rows, window_rows)
        source_cols = column_table(source_numer, source_flip, cols, out_cols)
        row_table = resize_matrix(positions, out_rows, source_valid, full_rows)
        row_part = lax.dynamic_slice_in_dim(row_table, begin, window_rows, 1)
        widened = jnp.einsum(
            "cyx,jx->cyj", arrived, source_cols, preferred_element_type=jnp.float32
        ).astype(jnp.bfloat16)
        result = result + jnp.einsum(
            "iy,cyj->icj", row_part, widened, preferred_element_type=jnp.float32
        )
    return result


def solution(mesh):
    placed = (
        P(("groups", "member"), None, "space", None),
        P("groups"),
        P(),
        P(),
        P(),
        P(),
        P(),
        P(),
    )
    return jax.shard_map(
        shards,
        mesh=mesh,
        in_specs=placed,
        out_specs=P(("groups", "space", "member"), None, None),
        check_vma=False,
    )
```

```python
import functools

import jax
import jax.numpy as jnp
from jax import lax
from jax.experimental import pallas as pl
from jax.experimental.pallas import tpu as pltpu
from jax.sharding import PartitionSpec as P

UP = 4
LOW_CODE = 8
HIGH_CODE = 29


def with_halo(block, sides, width):
    for axis, dim in sides:
        count = lax.axis_size(axis)
        forward = [(i, i + 1) for i in range(count - 1)]
        backward = [(target, source) for source, target in forward]
        low = lax.ppermute(
            lax.slice_in_dim(block, block.shape[dim] - width, None, axis=dim), axis, forward
        )
        high = lax.ppermute(lax.slice_in_dim(block, 0, width, axis=dim), axis, backward)
        block = jnp.concatenate([low, block, high], axis=dim)
    return block


def gather_rows(block, axis, need):
    count = lax.axis_size(axis)
    if count & (count - 1):
        return lax.all_gather(block, axis, axis=1, tiled=True)
    me = lax.axis_index(axis)
    lead, rows, rest = block.shape[0], block.shape[1], block.shape[2:]
    held = block[:, None]
    bit = count // 2
    while bit:
        span = 2 * bit
        routes = {}
        for p in range(held.shape[1]):
            pairs = []
            for i in range(count):
                j = i ^ bit
                wanted = set().union(*[need[g] for g in range(count) if g // bit == j // bit])
                if p * span + i % span in wanted:
                    pairs.append((i, j))
            routes.setdefault(tuple(pairs), []).append(p)
        if bit == 1 or len(routes) == 1:
            pairs = sorted(set().union(*[set(r) for r in routes]))
            other = lax.ppermute(held, axis, pairs)
        else:
            parts = [None] * held.shape[1]
            for pairs, places in routes.items():
                if pairs:
                    for p in places:
                        parts[p] = lax.ppermute(held[:, p:p + 1], axis, list(pairs))
            empty = jnp.zeros_like(held[:, :1])
            other = jnp.concatenate([empty if x is None else x for x in parts], 1)
        upper = (me & bit) != 0
        held = jnp.where(upper, jnp.stack([other, held], 2), jnp.stack([held, other], 2))
        held = held.reshape((lead, -1, rows) + rest)
        bit //= 2
    return held.reshape((lead, count * rows) + rest)


def block_needs(spaces, members, rows_dev, low_code, high_code):
    full_rows = rows_dev * spaces
    out_rows = UP * full_rows
    own_rows = out_rows // spaces
    part_rows = own_rows // members
    window_rows = (part_rows - 1) // UP + 3
    need = []
    for place in range(spaces):
        blocks = set()
        for numer in range(low_code // 2, high_code // 2 + 1):
            valid = full_rows * numer // 14
            for target in range(members):
                first_row = place * own_rows + target * part_rows
                pos = (2 * first_row + 1) * valid - out_rows
                lower = 0 if pos < 0 else pos // (2 * out_rows)
                lower = valid - 1 if lower >= valid - 1 else lower
                begin = min(max(lower, 0), full_rows - window_rows)
                blocks |= set(range(begin // rows_dev, (begin + window_rows - 1) // rows_dev + 1))
        need.append(blocks)
    return need


def resize_matrix(positions, out_len, valid, in_len):
    numer = (2 * positions + 1) * valid - out_len
    denom = 2 * out_len
    lower = numer // denom
    frac = (numer - lower * denom).astype(jnp.float32) / denom
    below = numer < 0
    frac = jnp.where(below, jnp.float32(0.0), frac)
    lower = jnp.where(below, 0, lower)
    top_index = valid - 1
    over = lower >= top_index
    frac = jnp.where(over, jnp.float32(0.0), frac)
    lower = jnp.where(over, top_index, lower)
    columns = jnp.arange(in_len, dtype=jnp.int32)
    first = jnp.where(columns[None, :] == lower[:, None], 1.0 - frac[:, None], jnp.float32(0.0))
    second = jnp.where(columns[None, :] == lower[:, None] + 1, frac[:, None], jnp.float32(0.0))
    return (first + second).astype(jnp.bfloat16)


def run_conv(x_ref, w_ref, bias, lo, hi, good_cols, o_ref, width, block, head=None):
    flat = block * width
    outs = w_ref.shape[2]
    place = lax.broadcasted_iota(jnp.int32, (1, flat), 1)
    col = place % width
    stacked = jnp.concatenate(
        [jnp.concatenate([w_ref[a, b] for a in range(3)], axis=1) for b in range(3)], axis=0
    )

    def step(i, carry):
        r0 = i * block
        rhs = jnp.concatenate(
            [x_ref[:, pl.ds(pl.multiple_of((r0 + a) * width, width), flat)] for a in range(3)],
            axis=0,
        )
        res = jnp.dot(stacked, rhs, preferred_element_type=jnp.float32)
        taps = [res[b * outs:(b + 1) * outs] for b in range(3)]
        left = jnp.where(col == 0, 0.0, pltpu.roll(taps[0], 1, 1))
        right = jnp.where(col == width - 1, 0.0, pltpu.roll(taps[2], flat - 1, 1))
        total = jnp.maximum(taps[1] + left + right + bias, 0.0)
        row = r0 + place // width
        keep = (row >= lo) & (row < hi) & (col < good_cols)
        out = jnp.where(keep, total, 0.0).astype(jnp.bfloat16)
        if head is not None:
            out = jnp.dot(head[0], out, preferred_element_type=jnp.float32) + head[1]
        o_ref[:, pl.ds(pl.multiple_of(r0 * width, width), flat)] = out.astype(o_ref.dtype)
        return carry

    lax.fori_loop(0, o_ref.shape[1] // flat, step, 0, unroll=True)


def first_body(main_ref, top_ref, low_ref, w_ref, b_ref, s_ref, o_ref, x_ref, *, width, block, halo):
    lo_in, hi_in, good_cols, lo, hi = s_ref[0], s_ref[1], s_ref[2], s_ref[3], s_ref[4]
    chans = main_ref.shape[0]
    rows_main = main_ref.shape[1] // width

    def put(src, offset, rows):
        place = lax.broadcasted_iota(jnp.int32, (1, rows * width), 1)
        row = offset + place // width
        keep = (row >= lo_in) & (row < hi_in) & (place % width < good_cols)
        x_ref[:, pl.ds(pl.multiple_of(offset * width, width), rows * width)] = jnp.where(
            keep, src, jnp.zeros_like(src)
        )

    put(top_ref[...], 0, halo)
    put(low_ref[...], halo + rows_main, halo)

    def chunk(i, carry):
        start = pl.multiple_of(i * 2 * width, width)
        put(main_ref[:, pl.ds(start, 2 * width)], halo + 2 * i, 2)
        return carry

    lax.fori_loop(0, rows_main // 2, chunk, 0)
    run_conv(x_ref, w_ref, b_ref[pl.ds(0, chans), 0:1], lo, hi, good_cols, o_ref, width, block)


def second_body(x_ref, w_ref, b_ref, k_ref, s_ref, o_ref, *, width, block):
    chans = x_ref.shape[0]
    classes = k_ref.shape[0]
    head = (k_ref[...], b_ref[pl.ds(2 * chans, classes), 0:1])
    lo, hi, good_cols = s_ref[5], s_ref[6], s_ref[2]
    run_conv(x_ref, w_ref, b_ref[pl.ds(chans, chans), 0:1], lo, hi, good_cols, o_ref, width, block, head)


def pick_block(rows):
    return next(k for k in (4, 3, 2, 1) if rows % k == 0)


def conv_first_layer(feat, top, low, width, weights, biases, limits):
    chans = feat.shape[0]
    rows_main = feat.shape[1] // width
    halo = top.shape[1] // width
    rows_in = rows_main + 2 * halo
    rows_out = rows_in - 2
    outs = weights.shape[2]
    block = pick_block(rows_out)
    vmem = pl.BlockSpec(memory_space=pltpu.VMEM)
    cost = pl.CostEstimate(
        flops=2 * 9 * rows_out * width * chans * outs,
        bytes_accessed=2 * (chans * rows_in * width + weights.size + rows_out * width * outs),
        transcendentals=0,
    )
    out = pl.pallas_call(
        functools.partial(first_body, width=width, block=block, halo=halo),
        out_shape=jax.ShapeDtypeStruct((outs, rows_out * width), jnp.bfloat16),
        in_specs=[vmem] * 5 + [pl.BlockSpec(memory_space=pltpu.SMEM)],
        out_specs=vmem,
        scratch_shapes=[pltpu.VMEM((chans, rows_in * width), jnp.bfloat16)],
        cost_estimate=cost,
    )(
        feat,
        top,
        low,
        weights,
        biases,
        limits,
    )
    return out


def conv_second_layer(x, width, weights, biases, head, limits):
    chans, flat_in = x.shape
    rows_out = flat_in // width - 2
    outs = weights.shape[2]
    classes = head.shape[0]
    block = pick_block(rows_out)
    vmem = pl.BlockSpec(memory_space=pltpu.VMEM)
    cost = pl.CostEstimate(
        flops=2 * 9 * rows_out * width * chans * outs + 2 * rows_out * width * outs * classes,
        bytes_accessed=2 * (x.size + weights.size + rows_out * width * classes),
        transcendentals=0,
    )
    out = pl.pallas_call(
        functools.partial(second_body, width=width, block=block),
        out_shape=jax.ShapeDtypeStruct((classes, rows_out * width), jnp.bfloat16),
        in_specs=[vmem] * 4 + [pl.BlockSpec(memory_space=pltpu.SMEM)],
        out_specs=vmem,
        cost_estimate=cost,
    )(x, weights, biases, head, limits)
    return out.reshape(classes, rows_out, width)


def window_start(numer, first_row, full_rows, out_rows, window_rows):
    valid = full_rows * numer // 14
    numer_pos = (2 * first_row + 1) * valid - out_rows
    lower = numer_pos // (2 * out_rows)
    lower = jnp.where(numer_pos < 0, 0, lower)
    lower = jnp.where(lower >= valid - 1, valid - 1, lower)
    return jnp.clip(lower, 0, full_rows - window_rows)


def column_table(numer, flip, cols, out_cols):
    valid_cols = cols * numer // 14
    col_pos = jnp.arange(out_cols, dtype=jnp.int32)
    col_pos = jnp.where(flip == 1, out_cols - 1 - col_pos, col_pos)
    return resize_matrix(col_pos, out_cols, valid_cols, cols)


def shards(features, views, conv_first, bias_first, conv_second, bias_second, classify, class_bias):
    feat = features[0]
    rows_dev, cols = (feat.shape[1], feat.shape[2])
    spaces = lax.axis_size("space")
    full_rows = rows_dev * spaces
    place = lax.axis_index("space")
    member_index = lax.axis_index("member")
    members = views.shape[0]
    picked = jnp.arange(members, dtype=jnp.int32) == member_index
    code = jnp.sum(jnp.where(picked, views, 0))
    numer = code // 2
    valid_rows = full_rows * numer // 14
    valid_cols = cols * numer // 14
    count = lax.axis_size("space")
    halo = 2
    forward = [(i, i + 1) for i in range(count - 1)]
    backward = [(target, source) for source, target in forward]
    flat_feat = feat.reshape(feat.shape[0], rows_dev * cols)
    top_rows = lax.ppermute(flat_feat[:, (rows_dev - halo) * cols:], "space", forward)
    low_rows = lax.ppermute(flat_feat[:, : halo * cols], "space", backward)
    top = place * rows_dev
    slot = lax.broadcasted_iota(jnp.int32, (7,), 0)
    offsets = jnp.where(slot < 2, halo, jnp.where((slot == 3) | (slot == 4), 1, 0))
    of_top = jnp.where(slot == 2, 0, -1)
    of_rows = jnp.where((slot == 1) | (slot == 4) | (slot == 6), 1, 0)
    of_cols = jnp.where(slot == 2, 1, 0)
    limits = offsets + of_top * top + of_rows * valid_rows + of_cols * valid_cols
    biases = jnp.concatenate([bias_first, bias_second, class_bias])
    biases = jnp.broadcast_to(biases[:, None], (biases.shape[0], 128))
    hidden = conv_first_layer(flat_feat, top_rows, low_rows, cols, conv_first, biases, limits)
    logits = conv_second_layer(hidden, cols, conv_second, biases, classify, limits)
    out_rows = UP * full_rows
    out_cols = UP * cols
    own_rows = out_rows // spaces
    part_rows = own_rows // members
    window_rows = (part_rows - 1) // UP + 3
    need = block_needs(spaces, members, rows_dev, LOW_CODE, HIGH_CODE)
    gathered = gather_rows(logits, "space", need)
    pieces = []
    for target in range(members):
        first_row = place * own_rows + target * part_rows
        begin = window_start(numer, first_row, full_rows, out_rows, window_rows)
        pieces.append(lax.dynamic_slice_in_dim(gathered, begin, window_rows, 1))
    outgoing = jnp.stack(pieces, 0)
    own_first = place * own_rows + member_index * part_rows
    positions = own_first + jnp.arange(part_rows, dtype=jnp.int32)
    result = jnp.zeros((part_rows, logits.shape[0], out_cols), jnp.float32)
    for shift in range(members):
        if shift == 0:
            arrived = lax.dynamic_index_in_dim(outgoing, member_index, 0, keepdims=False)
        else:
            send = lax.dynamic_index_in_dim(
                outgoing, (member_index + shift) % members, 0, keepdims=False
            )
            arrived = lax.ppermute(
                send, "member", [(i, (i + shift) % members) for i in range(members)]
            )
        source = (member_index - shift) % members
        source_code = jnp.sum(jnp.where(jnp.arange(members) == source, views, 0))
        source_numer = source_code // 2
        source_flip = source_code % 2
        source_valid = full_rows * source_numer // 14
        begin = window_start(source_numer, own_first, full_rows, out_rows, window_rows)
        source_cols = column_table(source_numer, source_flip, cols, out_cols)
        row_table = resize_matrix(positions, out_rows, source_valid, full_rows)
        row_part = lax.dynamic_slice_in_dim(row_table, begin, window_rows, 1)
        widened = jnp.einsum(
            "cyx,jx->cyj", arrived, source_cols, preferred_element_type=jnp.float32
        ).astype(jnp.bfloat16)
        result = result + jnp.einsum(
            "iy,cyj->icj", row_part, widened, preferred_element_type=jnp.float32
        )
    return result


def solution(mesh):
    placed = (
        P(("groups", "member"), None, "space", None),
        P("groups"),
        P(),
        P(),
        P(),
        P(),
        P(),
        P(),
    )
    return jax.shard_map(
        shards,
        mesh=mesh,
        in_specs=placed,
        out_specs=P(("groups", "space", "member"), None, None),
        check_vma=False,
    )
```

```python
import functools

import jax
import jax.numpy as jnp
from jax import lax
from jax.experimental import pallas as pl
from jax.experimental.pallas import tpu as pltpu
from jax.sharding import PartitionSpec as P

UP = 4
LOW_CODE = 8
HIGH_CODE = 29


def with_halo(block, sides, width):
    for axis, dim in sides:
        count = lax.axis_size(axis)
        forward = [(i, i + 1) for i in range(count - 1)]
        backward = [(target, source) for source, target in forward]
        low = lax.ppermute(
            lax.slice_in_dim(block, block.shape[dim] - width, None, axis=dim), axis, forward
        )
        high = lax.ppermute(lax.slice_in_dim(block, 0, width, axis=dim), axis, backward)
        block = jnp.concatenate([low, block, high], axis=dim)
    return block


def gather_rows(block, axis, need):
    count = lax.axis_size(axis)
    if count & (count - 1):
        return lax.all_gather(block, axis, axis=1, tiled=True)
    me = lax.axis_index(axis)
    lead, rows, rest = block.shape[0], block.shape[1], block.shape[2:]
    held = block[:, None]
    bit = count // 2
    while bit:
        span = 2 * bit
        routes = {}
        for p in range(held.shape[1]):
            pairs = []
            for i in range(count):
                j = i ^ bit
                wanted = set().union(*[need[g] for g in range(count) if g // bit == j // bit])
                if p * span + i % span in wanted:
                    pairs.append((i, j))
            routes.setdefault(tuple(pairs), []).append(p)
        if bit == 1 or len(routes) == 1:
            pairs = sorted(set().union(*[set(r) for r in routes]))
            other = lax.ppermute(held, axis, pairs)
        else:
            parts = [None] * held.shape[1]
            for pairs, places in routes.items():
                if pairs:
                    for p in places:
                        parts[p] = lax.ppermute(held[:, p:p + 1], axis, list(pairs))
            empty = jnp.zeros_like(held[:, :1])
            other = jnp.concatenate([empty if x is None else x for x in parts], 1)
        upper = (me & bit) != 0
        held = jnp.where(upper, jnp.stack([other, held], 2), jnp.stack([held, other], 2))
        held = held.reshape((lead, -1, rows) + rest)
        bit //= 2
    return held.reshape((lead, count * rows) + rest)


def block_needs(spaces, members, rows_dev, low_code, high_code):
    full_rows = rows_dev * spaces
    out_rows = UP * full_rows
    own_rows = out_rows // spaces
    part_rows = own_rows // members
    window_rows = (part_rows - 1) // UP + 3
    need = []
    for place in range(spaces):
        blocks = set()
        for numer in range(low_code // 2, high_code // 2 + 1):
            valid = full_rows * numer // 14
            for target in range(members):
                first_row = place * own_rows + target * part_rows
                pos = (2 * first_row + 1) * valid - out_rows
                lower = 0 if pos < 0 else pos // (2 * out_rows)
                lower = valid - 1 if lower >= valid - 1 else lower
                begin = min(max(lower, 0), full_rows - window_rows)
                blocks |= set(range(begin // rows_dev, (begin + window_rows - 1) // rows_dev + 1))
        need.append(blocks)
    return need


def resize_matrix(positions, out_len, valid, in_len):
    numer = (2 * positions + 1) * valid - out_len
    denom = 2 * out_len
    lower = numer // denom
    frac = (numer - lower * denom).astype(jnp.float32) / denom
    below = numer < 0
    frac = jnp.where(below, jnp.float32(0.0), frac)
    lower = jnp.where(below, 0, lower)
    top_index = valid - 1
    over = lower >= top_index
    frac = jnp.where(over, jnp.float32(0.0), frac)
    lower = jnp.where(over, top_index, lower)
    columns = jnp.arange(in_len, dtype=jnp.int32)
    first = jnp.where(columns[None, :] == lower[:, None], 1.0 - frac[:, None], jnp.float32(0.0))
    second = jnp.where(columns[None, :] == lower[:, None] + 1, frac[:, None], jnp.float32(0.0))
    return (first + second).astype(jnp.bfloat16)


def run_conv(x_ref, w_ref, bias, lo, hi, good_cols, o_ref, width, block, head=None):
    flat = block * width
    outs = w_ref.shape[2]
    place = lax.broadcasted_iota(jnp.int32, (1, flat), 1)
    col = place % width
    stacked = jnp.concatenate(
        [jnp.concatenate([w_ref[a, b] for a in range(3)], axis=1) for b in range(3)], axis=0
    )

    def step(i, carry):
        r0 = i * block
        rhs = jnp.concatenate(
            [x_ref[:, pl.ds(pl.multiple_of((r0 + a) * width, width), flat)] for a in range(3)],
            axis=0,
        )
        res = jnp.dot(stacked, rhs, preferred_element_type=jnp.float32)
        taps = [res[b * outs:(b + 1) * outs] for b in range(3)]
        left = jnp.where(col == 0, 0.0, pltpu.roll(taps[0], 1, 1))
        right = jnp.where(col == width - 1, 0.0, pltpu.roll(taps[2], flat - 1, 1))
        total = jnp.maximum(taps[1] + left + right + bias, 0.0)
        row = r0 + place // width
        keep = (row >= lo) & (row < hi) & (col < good_cols)
        out = jnp.where(keep, total, 0.0).astype(jnp.bfloat16)
        if head is not None:
            out = jnp.dot(head[0], out, preferred_element_type=jnp.float32) + head[1]
        o_ref[:, pl.ds(pl.multiple_of(r0 * width, width), flat)] = out.astype(o_ref.dtype)
        return carry

    lax.fori_loop(0, o_ref.shape[1] // flat, step, 0, unroll=True)


def first_body(main_ref, top_ref, low_ref, w_ref, b_ref, s_ref, o_ref, x_ref, *, width, block, halo):
    lo_in, hi_in, good_cols, lo, hi = s_ref[0], s_ref[1], s_ref[2], s_ref[3], s_ref[4]
    chans = main_ref.shape[0]
    rows_main = main_ref.shape[1] // width

    def put(src, offset, rows):
        place = lax.broadcasted_iota(jnp.int32, (1, rows * width), 1)
        row = offset + place // width
        keep = (row >= lo_in) & (row < hi_in) & (place % width < good_cols)
        x_ref[:, pl.ds(pl.multiple_of(offset * width, width), rows * width)] = jnp.where(
            keep, src, jnp.zeros_like(src)
        )

    put(top_ref[...], 0, halo)
    put(low_ref[...], halo + rows_main, halo)

    def chunk(i, carry):
        start = pl.multiple_of(i * 2 * width, width)
        put(main_ref[:, pl.ds(start, 2 * width)], halo + 2 * i, 2)
        return carry

    lax.fori_loop(0, rows_main // 2, chunk, 0, unroll=True)
    run_conv(x_ref, w_ref, b_ref[pl.ds(0, chans), 0:1], lo, hi, good_cols, o_ref, width, block)


def second_body(x_ref, w_ref, b_ref, k_ref, s_ref, o_ref, *, width, block):
    chans = x_ref.shape[0]
    classes = k_ref.shape[0]
    head = (k_ref[...], b_ref[pl.ds(2 * chans, classes), 0:1])
    lo, hi, good_cols = s_ref[5], s_ref[6], s_ref[2]
    run_conv(x_ref, w_ref, b_ref[pl.ds(chans, chans), 0:1], lo, hi, good_cols, o_ref, width, block, head)


def pick_block(rows):
    return next(k for k in (4, 3, 2, 1) if rows % k == 0)


def conv_first_layer(feat, top, low, width, weights, biases, limits):
    chans = feat.shape[0]
    rows_main = feat.shape[1] // width
    halo = top.shape[1] // width
    rows_in = rows_main + 2 * halo
    rows_out = rows_in - 2
    outs = weights.shape[2]
    block = pick_block(rows_out)
    vmem = pl.BlockSpec(memory_space=pltpu.VMEM)
    cost = pl.CostEstimate(
        flops=2 * 9 * rows_out * width * chans * outs,
        bytes_accessed=2 * (chans * rows_in * width + weights.size + rows_out * width * outs),
        transcendentals=0,
    )
    out = pl.pallas_call(
        functools.partial(first_body, width=width, block=block, halo=halo),
        out_shape=jax.ShapeDtypeStruct((outs, rows_out * width), jnp.bfloat16),
        in_specs=[vmem] * 5 + [pl.BlockSpec(memory_space=pltpu.SMEM)],
        out_specs=vmem,
        scratch_shapes=[pltpu.VMEM((chans, rows_in * width), jnp.bfloat16)],
        cost_estimate=cost,
    )(
        feat,
        top,
        low,
        weights,
        biases,
        limits,
    )
    return out


def conv_second_layer(x, width, weights, biases, head, limits):
    chans, flat_in = x.shape
    rows_out = flat_in // width - 2
    outs = weights.shape[2]
    classes = head.shape[0]
    block = pick_block(rows_out)
    vmem = pl.BlockSpec(memory_space=pltpu.VMEM)
    cost = pl.CostEstimate(
        flops=2 * 9 * rows_out * width * chans * outs + 2 * rows_out * width * outs * classes,
        bytes_accessed=2 * (x.size + weights.size + rows_out * width * classes),
        transcendentals=0,
    )
    out = pl.pallas_call(
        functools.partial(second_body, width=width, block=block),
        out_shape=jax.ShapeDtypeStruct((classes, rows_out * width), jnp.bfloat16),
        in_specs=[vmem] * 4 + [pl.BlockSpec(memory_space=pltpu.SMEM)],
        out_specs=vmem,
        cost_estimate=cost,
    )(x, weights, biases, head, limits)
    return out.reshape(classes, rows_out, width)


def window_start(numer, first_row, full_rows, out_rows, window_rows):
    valid = full_rows * numer // 14
    numer_pos = (2 * first_row + 1) * valid - out_rows
    lower = numer_pos // (2 * out_rows)
    lower = jnp.where(numer_pos < 0, 0, lower)
    lower = jnp.where(lower >= valid - 1, valid - 1, lower)
    return jnp.clip(lower, 0, full_rows - window_rows)


def column_table(numer, flip, cols, out_cols):
    valid_cols = cols * numer // 14
    col_pos = jnp.arange(out_cols, dtype=jnp.int32)
    col_pos = jnp.where(flip == 1, out_cols - 1 - col_pos, col_pos)
    return resize_matrix(col_pos, out_cols, valid_cols, cols)


def shards(features, views, conv_first, bias_first, conv_second, bias_second, classify, class_bias):
    feat = features[0]
    rows_dev, cols = (feat.shape[1], feat.shape[2])
    spaces = lax.axis_size("space")
    full_rows = rows_dev * spaces
    place = lax.axis_index("space")
    member_index = lax.axis_index("member")
    members = views.shape[0]
    picked = jnp.arange(members, dtype=jnp.int32) == member_index
    code = jnp.sum(jnp.where(picked, views, 0))
    numer = code // 2
    valid_rows = full_rows * numer // 14
    valid_cols = cols * numer // 14
    count = lax.axis_size("space")
    halo = 2
    forward = [(i, i + 1) for i in range(count - 1)]
    backward = [(target, source) for source, target in forward]
    flat_feat = feat.reshape(feat.shape[0], rows_dev * cols)
    top_rows = lax.ppermute(flat_feat[:, (rows_dev - halo) * cols:], "space", forward)
    low_rows = lax.ppermute(flat_feat[:, : halo * cols], "space", backward)
    top = place * rows_dev
    offsets = jnp.array([halo, halo, 0, 1, 1, 0, 0], jnp.int32)
    of_top = jnp.array([-1, -1, 0, -1, -1, -1, -1], jnp.int32)
    of_rows = jnp.array([0, 1, 0, 0, 1, 0, 1], jnp.int32)
    of_cols = jnp.array([0, 0, 1, 0, 0, 0, 0], jnp.int32)
    limits = offsets + of_top * top + of_rows * valid_rows + of_cols * valid_cols
    biases = jnp.concatenate([bias_first, bias_second, class_bias])
    biases = jnp.broadcast_to(biases[:, None], (biases.shape[0], 128))
    hidden = conv_first_layer(flat_feat, top_rows, low_rows, cols, conv_first, biases, limits)
    logits = conv_second_layer(hidden, cols, conv_second, biases, classify, limits)
    out_rows = UP * full_rows
    out_cols = UP * cols
    own_rows = out_rows // spaces
    part_rows = own_rows // members
    window_rows = (part_rows - 1) // UP + 3
    need = block_needs(spaces, members, rows_dev, LOW_CODE, HIGH_CODE)
    gathered = gather_rows(logits, "space", need)
    pieces = []
    for target in range(members):
        first_row = place * own_rows + target * part_rows
        begin = window_start(numer, first_row, full_rows, out_rows, window_rows)
        pieces.append(lax.dynamic_slice_in_dim(gathered, begin, window_rows, 1))
    outgoing = jnp.stack(pieces, 0)
    own_first = place * own_rows + member_index * part_rows
    positions = own_first + jnp.arange(part_rows, dtype=jnp.int32)
    result = jnp.zeros((part_rows, logits.shape[0], out_cols), jnp.float32)
    for shift in range(members):
        if shift == 0:
            arrived = lax.dynamic_index_in_dim(outgoing, member_index, 0, keepdims=False)
        else:
            send = lax.dynamic_index_in_dim(
                outgoing, (member_index + shift) % members, 0, keepdims=False
            )
            arrived = lax.ppermute(
                send, "member", [(i, (i + shift) % members) for i in range(members)]
            )
        source = (member_index - shift) % members
        source_code = jnp.sum(jnp.where(jnp.arange(members) == source, views, 0))
        source_numer = source_code // 2
        source_flip = source_code % 2
        source_valid = full_rows * source_numer // 14
        begin = window_start(source_numer, own_first, full_rows, out_rows, window_rows)
        source_cols = column_table(source_numer, source_flip, cols, out_cols)
        row_table = resize_matrix(positions, out_rows, source_valid, full_rows)
        row_part = lax.dynamic_slice_in_dim(row_table, begin, window_rows, 1)
        widened = jnp.einsum(
            "cyx,jx->cyj", arrived, source_cols, preferred_element_type=jnp.float32
        ).astype(jnp.bfloat16)
        result = result + jnp.einsum(
            "iy,cyj->icj", row_part, widened, preferred_element_type=jnp.float32
        )
    return result


def solution(mesh):
    placed = (
        P(("groups", "member"), None, "space", None),
        P("groups"),
        P(),
        P(),
        P(),
        P(),
        P(),
        P(),
    )
    return jax.shard_map(
        shards,
        mesh=mesh,
        in_specs=placed,
        out_specs=P(("groups", "space", "member"), None, None),
        check_vma=False,
    )
```

```python
import functools

import jax
import jax.numpy as jnp
from jax import lax
from jax.experimental import pallas as pl
from jax.experimental.pallas import tpu as pltpu
from jax.sharding import PartitionSpec as P

UP = 4
LOW_CODE = 8
HIGH_CODE = 29


def with_halo(block, sides, width):
    for axis, dim in sides:
        count = lax.axis_size(axis)
        forward = [(i, i + 1) for i in range(count - 1)]
        backward = [(target, source) for source, target in forward]
        low = lax.ppermute(
            lax.slice_in_dim(block, block.shape[dim] - width, None, axis=dim), axis, forward
        )
        high = lax.ppermute(lax.slice_in_dim(block, 0, width, axis=dim), axis, backward)
        block = jnp.concatenate([low, block, high], axis=dim)
    return block


def gather_rows(block, axis, need):
    count = lax.axis_size(axis)
    if count & (count - 1):
        return lax.all_gather(block, axis, axis=1, tiled=True)
    me = lax.axis_index(axis)
    lead, rows, rest = block.shape[0], block.shape[1], block.shape[2:]
    held = block[:, None]
    bit = count // 2
    while bit:
        span = 2 * bit
        routes = {}
        for p in range(held.shape[1]):
            pairs = []
            for i in range(count):
                j = i ^ bit
                wanted = set().union(*[need[g] for g in range(count) if g // bit == j // bit])
                if p * span + i % span in wanted:
                    pairs.append((i, j))
            routes.setdefault(tuple(pairs), []).append(p)
        if bit == 1 or len(routes) == 1:
            pairs = sorted(set().union(*[set(r) for r in routes]))
            other = lax.ppermute(held, axis, pairs)
        else:
            parts = [None] * held.shape[1]
            for pairs, places in routes.items():
                if pairs:
                    for p in places:
                        parts[p] = lax.ppermute(held[:, p:p + 1], axis, list(pairs))
            empty = jnp.zeros_like(held[:, :1])
            other = jnp.concatenate([empty if x is None else x for x in parts], 1)
        upper = (me & bit) != 0
        held = jnp.where(upper, jnp.stack([other, held], 2), jnp.stack([held, other], 2))
        held = held.reshape((lead, -1, rows) + rest)
        bit //= 2
    return held.reshape((lead, count * rows) + rest)


def block_needs(spaces, members, rows_dev, low_code, high_code):
    full_rows = rows_dev * spaces
    out_rows = UP * full_rows
    own_rows = out_rows // spaces
    part_rows = own_rows // members
    window_rows = (part_rows - 1) // UP + 3
    need = []
    for place in range(spaces):
        blocks = set()
        for numer in range(low_code // 2, high_code // 2 + 1):
            valid = full_rows * numer // 14
            for target in range(members):
                first_row = place * own_rows + target * part_rows
                pos = (2 * first_row + 1) * valid - out_rows
                lower = 0 if pos < 0 else pos // (2 * out_rows)
                lower = valid - 1 if lower >= valid - 1 else lower
                begin = min(max(lower, 0), full_rows - window_rows)
                blocks |= set(range(begin // rows_dev, (begin + window_rows - 1) // rows_dev + 1))
        need.append(blocks)
    return need


def resize_matrix(positions, out_len, valid, in_len):
    numer = (2 * positions + 1) * valid - out_len
    denom = 2 * out_len
    lower = numer // denom
    frac = (numer - lower * denom).astype(jnp.float32) / denom
    below = numer < 0
    frac = jnp.where(below, jnp.float32(0.0), frac)
    lower = jnp.where(below, 0, lower)
    top_index = valid - 1
    over = lower >= top_index
    frac = jnp.where(over, jnp.float32(0.0), frac)
    lower = jnp.where(over, top_index, lower)
    columns = jnp.arange(in_len, dtype=jnp.int32)
    first = jnp.where(columns[None, :] == lower[:, None], 1.0 - frac[:, None], jnp.float32(0.0))
    second = jnp.where(columns[None, :] == lower[:, None] + 1, frac[:, None], jnp.float32(0.0))
    return (first + second).astype(jnp.bfloat16)


def run_conv(x_ref, w_ref, bias, lo, hi, good_cols, o_ref, width, block, head=None):
    flat = block * width
    outs = w_ref.shape[2]
    place = lax.broadcasted_iota(jnp.int32, (1, flat), 1)
    col = place % width
    stacked = jnp.concatenate(
        [jnp.concatenate([w_ref[a, b] for a in range(3)], axis=1) for b in range(3)], axis=0
    )

    def step(i, carry):
        r0 = i * block
        rhs = jnp.concatenate(
            [x_ref[:, pl.ds(pl.multiple_of((r0 + a) * width, width), flat)] for a in range(3)],
            axis=0,
        )
        res = jnp.dot(stacked, rhs, preferred_element_type=jnp.float32)
        taps = [res[b * outs:(b + 1) * outs] for b in range(3)]
        left = jnp.where(col == 0, 0.0, pltpu.roll(taps[0], 1, 1))
        right = jnp.where(col == width - 1, 0.0, pltpu.roll(taps[2], flat - 1, 1))
        total = jnp.maximum(taps[1] + left + right + bias, 0.0)
        row = r0 + place // width
        keep = (row >= lo) & (row < hi) & (col < good_cols)
        out = jnp.where(keep, total, 0.0).astype(jnp.bfloat16)
        if head is not None:
            out = jnp.dot(head[0], out, preferred_element_type=jnp.float32) + head[1]
        o_ref[:, pl.ds(pl.multiple_of(r0 * width, width), flat)] = out.astype(o_ref.dtype)
        return carry

    lax.fori_loop(0, o_ref.shape[1] // flat, step, 0, unroll=True)


def first_body(main_ref, top_ref, low_ref, w_ref, b_ref, s_ref, o_ref, x_ref, *, width, block, halo):
    lo_in, hi_in, good_cols, lo, hi = s_ref[0], s_ref[1], s_ref[2], s_ref[3], s_ref[4]
    chans = main_ref.shape[0]
    rows_main = main_ref.shape[1] // width

    def put(src, offset, rows):
        place = lax.broadcasted_iota(jnp.int32, (1, rows * width), 1)
        row = offset + place // width
        keep = (row >= lo_in) & (row < hi_in) & (place % width < good_cols)
        x_ref[:, pl.ds(pl.multiple_of(offset * width, width), rows * width)] = jnp.where(
            keep, src, jnp.zeros_like(src)
        )

    put(top_ref[...], 0, halo)
    put(low_ref[...], halo + rows_main, halo)

    def chunk(i, carry):
        start = pl.multiple_of(i * 2 * width, width)
        put(main_ref[:, pl.ds(start, 2 * width)], halo + 2 * i, 2)
        return carry

    lax.fori_loop(0, rows_main // 2, chunk, 0)
    run_conv(x_ref, w_ref, b_ref[pl.ds(0, chans), 0:1], lo, hi, good_cols, o_ref, width, block)


def second_body(x_ref, w_ref, b_ref, k_ref, s_ref, o_ref, *, width, block):
    chans = x_ref.shape[0]
    classes = k_ref.shape[0]
    head = (k_ref[...], b_ref[pl.ds(2 * chans, classes), 0:1])
    lo, hi, good_cols = s_ref[5], s_ref[6], s_ref[2]
    run_conv(x_ref, w_ref, b_ref[pl.ds(chans, chans), 0:1], lo, hi, good_cols, o_ref, width, block, head)


def pick_block(rows):
    return next(k for k in (6, 4, 3, 2, 1) if rows % k == 0)


def conv_first_layer(feat, top, low, width, weights, biases, limits):
    chans = feat.shape[0]
    rows_main = feat.shape[1] // width
    halo = top.shape[1] // width
    rows_in = rows_main + 2 * halo
    rows_out = rows_in - 2
    outs = weights.shape[2]
    block = pick_block(rows_out)
    vmem = pl.BlockSpec(memory_space=pltpu.VMEM)
    cost = pl.CostEstimate(
        flops=2 * 9 * rows_out * width * chans * outs,
        bytes_accessed=2 * (chans * rows_in * width + weights.size + rows_out * width * outs),
        transcendentals=0,
    )
    out = pl.pallas_call(
        functools.partial(first_body, width=width, block=block, halo=halo),
        out_shape=jax.ShapeDtypeStruct((outs, rows_out * width), jnp.bfloat16),
        in_specs=[vmem] * 5 + [pl.BlockSpec(memory_space=pltpu.SMEM)],
        out_specs=vmem,
        scratch_shapes=[pltpu.VMEM((chans, rows_in * width), jnp.bfloat16)],
        cost_estimate=cost,
    )(
        feat,
        top,
        low,
        weights,
        biases,
        limits,
    )
    return out


def conv_second_layer(x, width, weights, biases, head, limits):
    chans, flat_in = x.shape
    rows_out = flat_in // width - 2
    outs = weights.shape[2]
    classes = head.shape[0]
    block = pick_block(rows_out)
    vmem = pl.BlockSpec(memory_space=pltpu.VMEM)
    cost = pl.CostEstimate(
        flops=2 * 9 * rows_out * width * chans * outs + 2 * rows_out * width * outs * classes,
        bytes_accessed=2 * (x.size + weights.size + rows_out * width * classes),
        transcendentals=0,
    )
    out = pl.pallas_call(
        functools.partial(second_body, width=width, block=block),
        out_shape=jax.ShapeDtypeStruct((classes, rows_out * width), jnp.bfloat16),
        in_specs=[vmem] * 4 + [pl.BlockSpec(memory_space=pltpu.SMEM)],
        out_specs=vmem,
        cost_estimate=cost,
    )(x, weights, biases, head, limits)
    return out.reshape(classes, rows_out, width)


def window_start(numer, first_row, full_rows, out_rows, window_rows):
    valid = full_rows * numer // 14
    numer_pos = (2 * first_row + 1) * valid - out_rows
    lower = numer_pos // (2 * out_rows)
    lower = jnp.where(numer_pos < 0, 0, lower)
    lower = jnp.where(lower >= valid - 1, valid - 1, lower)
    return jnp.clip(lower, 0, full_rows - window_rows)


def column_table(numer, flip, cols, out_cols):
    valid_cols = cols * numer // 14
    col_pos = jnp.arange(out_cols, dtype=jnp.int32)
    col_pos = jnp.where(flip == 1, out_cols - 1 - col_pos, col_pos)
    return resize_matrix(col_pos, out_cols, valid_cols, cols)


def shards(features, views, conv_first, bias_first, conv_second, bias_second, classify, class_bias):
    feat = features[0]
    rows_dev, cols = (feat.shape[1], feat.shape[2])
    spaces = lax.axis_size("space")
    full_rows = rows_dev * spaces
    place = lax.axis_index("space")
    member_index = lax.axis_index("member")
    members = views.shape[0]
    picked = jnp.arange(members, dtype=jnp.int32) == member_index
    code = jnp.sum(jnp.where(picked, views, 0))
    numer = code // 2
    valid_rows = full_rows * numer // 14
    valid_cols = cols * numer // 14
    count = lax.axis_size("space")
    halo = 2
    forward = [(i, i + 1) for i in range(count - 1)]
    backward = [(target, source) for source, target in forward]
    flat_feat = feat.reshape(feat.shape[0], rows_dev * cols)
    top_rows = lax.ppermute(flat_feat[:, (rows_dev - halo) * cols:], "space", forward)
    low_rows = lax.ppermute(flat_feat[:, : halo * cols], "space", backward)
    top = place * rows_dev
    offsets = jnp.array([halo, halo, 0, 1, 1, 0, 0], jnp.int32)
    of_top = jnp.array([-1, -1, 0, -1, -1, -1, -1], jnp.int32)
    of_rows = jnp.array([0, 1, 0, 0, 1, 0, 1], jnp.int32)
    of_cols = jnp.array([0, 0, 1, 0, 0, 0, 0], jnp.int32)
    limits = offsets + of_top * top + of_rows * valid_rows + of_cols * valid_cols
    biases = jnp.concatenate([bias_first, bias_second, class_bias])
    biases = jnp.broadcast_to(biases[:, None], (biases.shape[0], 128))
    hidden = conv_first_layer(flat_feat, top_rows, low_rows, cols, conv_first, biases, limits)
    logits = conv_second_layer(hidden, cols, conv_second, biases, classify, limits)
    out_rows = UP * full_rows
    out_cols = UP * cols
    own_rows = out_rows // spaces
    part_rows = own_rows // members
    window_rows = (part_rows - 1) // UP + 3
    need = block_needs(spaces, members, rows_dev, LOW_CODE, HIGH_CODE)
    gathered = gather_rows(logits, "space", need)
    pieces = []
    for target in range(members):
        first_row = place * own_rows + target * part_rows
        begin = window_start(numer, first_row, full_rows, out_rows, window_rows)
        pieces.append(lax.dynamic_slice_in_dim(gathered, begin, window_rows, 1))
    outgoing = jnp.stack(pieces, 0)
    own_first = place * own_rows + member_index * part_rows
    positions = own_first + jnp.arange(part_rows, dtype=jnp.int32)
    result = jnp.zeros((part_rows, logits.shape[0], out_cols), jnp.float32)
    for shift in range(members):
        if shift == 0:
            arrived = lax.dynamic_index_in_dim(outgoing, member_index, 0, keepdims=False)
        else:
            send = lax.dynamic_index_in_dim(
                outgoing, (member_index + shift) % members, 0, keepdims=False
            )
            arrived = lax.ppermute(
                send, "member", [(i, (i + shift) % members) for i in range(members)]
            )
        source = (member_index - shift) % members
        source_code = jnp.sum(jnp.where(jnp.arange(members) == source, views, 0))
        source_numer = source_code // 2
        source_flip = source_code % 2
        source_valid = full_rows * source_numer // 14
        begin = window_start(source_numer, own_first, full_rows, out_rows, window_rows)
        source_cols = column_table(source_numer, source_flip, cols, out_cols)
        row_table = resize_matrix(positions, out_rows, source_valid, full_rows)
        row_part = lax.dynamic_slice_in_dim(row_table, begin, window_rows, 1)
        widened = jnp.einsum(
            "cyx,jx->cyj", arrived, source_cols, preferred_element_type=jnp.float32
        ).astype(jnp.bfloat16)
        result = result + jnp.einsum(
            "iy,cyj->icj", row_part, widened, preferred_element_type=jnp.float32
        )
    return result


def solution(mesh):
    placed = (
        P(("groups", "member"), None, "space", None),
        P("groups"),
        P(),
        P(),
        P(),
        P(),
        P(),
        P(),
    )
    return jax.shard_map(
        shards,
        mesh=mesh,
        in_specs=placed,
        out_specs=P(("groups", "space", "member"), None, None),
        check_vma=False,
    )
```

```python
import functools

import jax
import jax.numpy as jnp
from jax import lax
from jax.experimental import pallas as pl
from jax.experimental.pallas import tpu as pltpu
from jax.sharding import PartitionSpec as P

UP = 4
LOW_CODE = 8
HIGH_CODE = 29


def with_halo(block, sides, width):
    for axis, dim in sides:
        count = lax.axis_size(axis)
        forward = [(i, i + 1) for i in range(count - 1)]
        backward = [(target, source) for source, target in forward]
        low = lax.ppermute(
            lax.slice_in_dim(block, block.shape[dim] - width, None, axis=dim), axis, forward
        )
        high = lax.ppermute(lax.slice_in_dim(block, 0, width, axis=dim), axis, backward)
        block = jnp.concatenate([low, block, high], axis=dim)
    return block


def gather_rows(block, axis, need):
    count = lax.axis_size(axis)
    if count & (count - 1):
        return lax.all_gather(block, axis, axis=1, tiled=True)
    me = lax.axis_index(axis)
    lead, rows, rest = block.shape[0], block.shape[1], block.shape[2:]
    held = block[:, None]
    bit = count // 2
    while bit:
        span = 2 * bit
        routes = {}
        for p in range(held.shape[1]):
            pairs = []
            for i in range(count):
                j = i ^ bit
                wanted = set().union(*[need[g] for g in range(count) if g // bit == j // bit])
                if p * span + i % span in wanted:
                    pairs.append((i, j))
            routes.setdefault(tuple(pairs), []).append(p)
        if bit == 1 or len(routes) == 1:
            pairs = sorted(set().union(*[set(r) for r in routes]))
            other = lax.ppermute(held, axis, pairs)
        else:
            parts = [None] * held.shape[1]
            for pairs, places in routes.items():
                if pairs:
                    for p in places:
                        parts[p] = lax.ppermute(held[:, p:p + 1], axis, list(pairs))
            empty = jnp.zeros_like(held[:, :1])
            other = jnp.concatenate([empty if x is None else x for x in parts], 1)
        upper = (me & bit) != 0
        held = jnp.where(upper, jnp.stack([other, held], 2), jnp.stack([held, other], 2))
        held = held.reshape((lead, -1, rows) + rest)
        bit //= 2
    return held.reshape((lead, count * rows) + rest)


def block_needs(spaces, members, rows_dev, low_code, high_code):
    full_rows = rows_dev * spaces
    out_rows = UP * full_rows
    own_rows = out_rows // spaces
    part_rows = own_rows // members
    window_rows = (part_rows - 1) // UP + 3
    need = []
    for place in range(spaces):
        blocks = set()
        for numer in range(low_code // 2, high_code // 2 + 1):
            valid = full_rows * numer // 14
            for target in range(members):
                first_row = place * own_rows + target * part_rows
                pos = (2 * first_row + 1) * valid - out_rows
                lower = 0 if pos < 0 else pos // (2 * out_rows)
                lower = valid - 1 if lower >= valid - 1 else lower
                begin = min(max(lower, 0), full_rows - window_rows)
                blocks |= set(range(begin // rows_dev, (begin + window_rows - 1) // rows_dev + 1))
        need.append(blocks)
    return need


def resize_matrix(positions, out_len, valid, in_len):
    numer = (2 * positions + 1) * valid - out_len
    denom = 2 * out_len
    lower = numer // denom
    frac = (numer - lower * denom).astype(jnp.float32) / denom
    below = numer < 0
    frac = jnp.where(below, jnp.float32(0.0), frac)
    lower = jnp.where(below, 0, lower)
    top_index = valid - 1
    over = lower >= top_index
    frac = jnp.where(over, jnp.float32(0.0), frac)
    lower = jnp.where(over, top_index, lower)
    columns = jnp.arange(in_len, dtype=jnp.int32)
    first = jnp.where(columns[None, :] == lower[:, None], 1.0 - frac[:, None], jnp.float32(0.0))
    second = jnp.where(columns[None, :] == lower[:, None] + 1, frac[:, None], jnp.float32(0.0))
    return (first + second).astype(jnp.bfloat16)


def run_conv(x_ref, w_ref, bias, lo, hi, good_cols, o_ref, width, block, head=None):
    flat = block * width
    outs = w_ref.shape[2]
    place = lax.broadcasted_iota(jnp.int32, (1, flat), 1)
    col = place % width
    stacked = jnp.concatenate(
        [jnp.concatenate([w_ref[a, b] for a in range(3)], axis=1) for b in range(3)], axis=0
    )

    def step(i, carry):
        r0 = i * block
        rhs = jnp.concatenate(
            [x_ref[:, pl.ds(pl.multiple_of((r0 + a) * width, width), flat)] for a in range(3)],
            axis=0,
        )
        res = jnp.dot(stacked, rhs, preferred_element_type=jnp.float32)
        taps = [res[b * outs:(b + 1) * outs] for b in range(3)]
        left = jnp.where(col == 0, 0.0, pltpu.roll(taps[0], 1, 1))
        right = jnp.where(col == width - 1, 0.0, pltpu.roll(taps[2], flat - 1, 1))
        total = jnp.maximum(taps[1] + left + right + bias, 0.0)
        row = r0 + place // width
        keep = (row >= lo) & (row < hi) & (col < good_cols)
        out = jnp.where(keep, total, 0.0).astype(jnp.bfloat16)
        if head is not None:
            out = jnp.dot(head[0], out, preferred_element_type=jnp.float32) + head[1]
        o_ref[:, pl.ds(pl.multiple_of(r0 * width, width), flat)] = out.astype(o_ref.dtype)
        return carry

    lax.fori_loop(0, o_ref.shape[1] // flat, step, 0, unroll=True)


def first_body(main_ref, top_ref, low_ref, w_ref, b_ref, s_ref, o_ref, x_ref, *, width, block, halo):
    lo_in, hi_in, good_cols, lo, hi = s_ref[0], s_ref[1], s_ref[2], s_ref[3], s_ref[4]
    chans = main_ref.shape[0]
    rows_main = main_ref.shape[1] // width

    def put(src, offset, rows):
        place = lax.broadcasted_iota(jnp.int32, (1, rows * width), 1)
        row = offset + place // width
        keep = (row >= lo_in) & (row < hi_in) & (place % width < good_cols)
        x_ref[:, pl.ds(pl.multiple_of(offset * width, width), rows * width)] = jnp.where(
            keep, src, jnp.zeros_like(src)
        )

    put(top_ref[...], 0, halo)
    put(low_ref[...], halo + rows_main, halo)

    def chunk(i, carry):
        start = pl.multiple_of(i * 2 * width, width)
        put(main_ref[:, pl.ds(start, 2 * width)], halo + 2 * i, 2)
        return carry

    lax.fori_loop(0, rows_main // 2, chunk, 0)
    run_conv(x_ref, w_ref, b_ref[pl.ds(0, chans), 0:1], lo, hi, good_cols, o_ref, width, block)


def second_body(x_ref, w_ref, b_ref, k_ref, s_ref, o_ref, *, width, block):
    chans = x_ref.shape[0]
    classes = k_ref.shape[0]
    head = (k_ref[...], b_ref[pl.ds(2 * chans, classes), 0:1])
    lo, hi, good_cols = s_ref[5], s_ref[6], s_ref[2]
    run_conv(x_ref, w_ref, b_ref[pl.ds(chans, chans), 0:1], lo, hi, good_cols, o_ref, width, block, head)


def pick_block(rows):
    return next(k for k in (4, 3, 2, 1) if rows % k == 0)


def conv_first_layer(feat, top, low, width, weights, biases, limits):
    chans = feat.shape[0]
    rows_main = feat.shape[1] // width
    halo = top.shape[1] // width
    rows_in = rows_main + 2 * halo
    rows_out = rows_in - 2
    outs = weights.shape[2]
    block = pick_block(rows_out)
    vmem = pl.BlockSpec(memory_space=pltpu.VMEM)
    cost = pl.CostEstimate(
        flops=2 * 9 * rows_out * width * chans * outs,
        bytes_accessed=2 * (chans * rows_in * width + weights.size + rows_out * width * outs),
        transcendentals=0,
    )
    out = pl.pallas_call(
        functools.partial(first_body, width=width, block=block, halo=halo),
        out_shape=jax.ShapeDtypeStruct((outs, rows_out * width), jnp.bfloat16),
        in_specs=[vmem] * 5 + [pl.BlockSpec(memory_space=pltpu.SMEM)],
        out_specs=vmem,
        scratch_shapes=[pltpu.VMEM((chans, rows_in * width), jnp.bfloat16)],
        cost_estimate=cost,
    )(
        feat,
        top,
        low,
        weights,
        biases,
        limits,
    )
    return out


def conv_second_layer(x, width, weights, biases, head, limits):
    chans, flat_in = x.shape
    rows_out = flat_in // width - 2
    outs = weights.shape[2]
    classes = head.shape[0]
    block = pick_block(rows_out)
    vmem = pl.BlockSpec(memory_space=pltpu.VMEM)
    cost = pl.CostEstimate(
        flops=2 * 9 * rows_out * width * chans * outs + 2 * rows_out * width * outs * classes,
        bytes_accessed=2 * (x.size + weights.size + rows_out * width * classes),
        transcendentals=0,
    )
    out = pl.pallas_call(
        functools.partial(second_body, width=width, block=block),
        out_shape=jax.ShapeDtypeStruct((classes, rows_out * width), jnp.bfloat16),
        in_specs=[vmem] * 4 + [pl.BlockSpec(memory_space=pltpu.SMEM)],
        out_specs=vmem,
        cost_estimate=cost,
    )(x, weights, biases, head, limits)
    return out.reshape(classes, rows_out, width)


def window_start(numer, first_row, full_rows, out_rows, window_rows):
    valid = full_rows * numer // 14
    numer_pos = (2 * first_row + 1) * valid - out_rows
    lower = numer_pos // (2 * out_rows)
    lower = jnp.where(numer_pos < 0, 0, lower)
    lower = jnp.where(lower >= valid - 1, valid - 1, lower)
    return jnp.clip(lower, 0, full_rows - window_rows)


def column_table(numer, flip, cols, out_cols):
    valid_cols = cols * numer // 14
    col_pos = jnp.arange(out_cols, dtype=jnp.int32)
    col_pos = jnp.where(flip == 1, out_cols - 1 - col_pos, col_pos)
    return resize_matrix(col_pos, out_cols, valid_cols, cols)


def shards(features, views, conv_first, bias_first, conv_second, bias_second, classify, class_bias):
    feat = features[0]
    rows_dev, cols = (feat.shape[1], feat.shape[2])
    spaces = lax.axis_size("space")
    full_rows = rows_dev * spaces
    place = lax.axis_index("space")
    member_index = lax.axis_index("member")
    members = views.shape[0]
    picked = jnp.arange(members, dtype=jnp.int32) == member_index
    code = jnp.sum(jnp.where(picked, views, 0))
    numer = code // 2
    valid_rows = full_rows * numer // 14
    valid_cols = cols * numer // 14
    count = lax.axis_size("space")
    halo = 2
    forward = [(i, i + 1) for i in range(count - 1)]
    backward = [(target, source) for source, target in forward]
    flat_feat = feat.reshape(feat.shape[0], rows_dev * cols)
    top_rows = lax.ppermute(flat_feat[:, (rows_dev - halo) * cols:], "space", forward)
    low_rows = lax.ppermute(flat_feat[:, : halo * cols], "space", backward)
    top = place * rows_dev
    offsets = jnp.array([halo, halo, 0, 1, 1, 0, 0], jnp.int32)
    of_top = jnp.array([-1, -1, 0, -1, -1, -1, -1], jnp.int32)
    of_rows = jnp.array([0, 1, 0, 0, 1, 0, 1], jnp.int32)
    of_cols = jnp.array([0, 0, 1, 0, 0, 0, 0], jnp.int32)
    limits = offsets + of_top * top + of_rows * valid_rows + of_cols * valid_cols
    biases = jnp.concatenate([bias_first, bias_second, class_bias])
    biases = jnp.broadcast_to(biases[:, None], (biases.shape[0], 128))
    hidden = conv_first_layer(flat_feat, top_rows, low_rows, cols, conv_first, biases, limits)
    logits = conv_second_layer(hidden, cols, conv_second, biases, classify, limits)
    out_rows = UP * full_rows
    out_cols = UP * cols
    own_rows = out_rows // spaces
    part_rows = own_rows // members
    window_rows = (part_rows - 1) // UP + 3
    need = block_needs(spaces, members, rows_dev, LOW_CODE, HIGH_CODE)
    gathered = gather_rows(logits, "space", need)
    pieces = []
    for target in range(members):
        first_row = place * own_rows + target * part_rows
        begin = window_start(numer, first_row, full_rows, out_rows, window_rows)
        pieces.append(lax.dynamic_slice_in_dim(gathered, begin, window_rows, 1))
    outgoing = jnp.stack(pieces, 0)
    own_first = place * own_rows + member_index * part_rows
    positions = own_first + jnp.arange(part_rows, dtype=jnp.int32)
    result = jnp.zeros((part_rows, logits.shape[0], out_cols), jnp.float32)
    arrivals = [lax.dynamic_index_in_dim(outgoing, member_index, 0, keepdims=False)]
    for shift in range(1, members):
        send = lax.dynamic_index_in_dim(outgoing, (member_index + shift) % members, 0, keepdims=False)
        arrivals.append(
            lax.ppermute(send, "member", [(i, (i + shift) % members) for i in range(members)])
        )

    def contribution(shift, arrived):
        source = (member_index - shift) % members
        source_code = jnp.sum(jnp.where(jnp.arange(members) == source, views, 0))
        source_numer = source_code // 2
        source_flip = source_code % 2
        source_valid = full_rows * source_numer // 14
        begin = window_start(source_numer, own_first, full_rows, out_rows, window_rows)
        source_cols = column_table(source_numer, source_flip, cols, out_cols)
        row_table = resize_matrix(positions, out_rows, source_valid, full_rows)
        row_part = lax.dynamic_slice_in_dim(row_table, begin, window_rows, 1)
        widened = jnp.einsum(
            "cyx,jx->cyj", arrived, source_cols, preferred_element_type=jnp.float32
        ).astype(jnp.bfloat16)
        return jnp.einsum("iy,cyj->icj", row_part, widened, preferred_element_type=jnp.float32)

    result = result + contribution(0, arrivals[0])
    if members > 1:
        result, *others = lax.optimization_barrier([result] + arrivals[1:])
        for shift in range(1, members):
            result = result + contribution(shift, others[shift - 1])
    return result


def solution(mesh):
    placed = (
        P(("groups", "member"), None, "space", None),
        P("groups"),
        P(),
        P(),
        P(),
        P(),
        P(),
        P(),
    )
    return jax.shard_map(
        shards,
        mesh=mesh,
        in_specs=placed,
        out_specs=P(("groups", "space", "member"), None, None),
        check_vma=False,
    )
```

```python
import functools

import jax
import jax.numpy as jnp
from jax import lax
from jax.experimental import pallas as pl
from jax.experimental.pallas import tpu as pltpu
from jax.sharding import PartitionSpec as P

UP = 4
LOW_CODE = 8
HIGH_CODE = 29


def with_halo(block, sides, width):
    for axis, dim in sides:
        count = lax.axis_size(axis)
        forward = [(i, i + 1) for i in range(count - 1)]
        backward = [(target, source) for source, target in forward]
        low = lax.ppermute(
            lax.slice_in_dim(block, block.shape[dim] - width, None, axis=dim), axis, forward
        )
        high = lax.ppermute(lax.slice_in_dim(block, 0, width, axis=dim), axis, backward)
        block = jnp.concatenate([low, block, high], axis=dim)
    return block


def gather_rows(block, axis, need):
    count = lax.axis_size(axis)
    if count & (count - 1):
        return lax.all_gather(block, axis, axis=1, tiled=True)
    me = lax.axis_index(axis)
    lead, rows, rest = block.shape[0], block.shape[1], block.shape[2:]
    held = block[:, None]
    bit = count // 2
    while bit:
        span = 2 * bit
        routes = {}
        for p in range(held.shape[1]):
            pairs = []
            for i in range(count):
                j = i ^ bit
                wanted = set().union(*[need[g] for g in range(count) if g // bit == j // bit])
                if p * span + i % span in wanted:
                    pairs.append((i, j))
            routes.setdefault(tuple(pairs), []).append(p)
        if bit == 1 or len(routes) == 1:
            pairs = sorted(set().union(*[set(r) for r in routes]))
            other = lax.ppermute(held, axis, pairs)
        else:
            parts = [None] * held.shape[1]
            for pairs, places in routes.items():
                if pairs:
                    for p in places:
                        parts[p] = lax.ppermute(held[:, p:p + 1], axis, list(pairs))
            empty = jnp.zeros_like(held[:, :1])
            other = jnp.concatenate([empty if x is None else x for x in parts], 1)
        upper = (me & bit) != 0
        held = jnp.where(upper, jnp.stack([other, held], 2), jnp.stack([held, other], 2))
        held = held.reshape((lead, -1, rows) + rest)
        bit //= 2
    return held.reshape((lead, count * rows) + rest)


def block_needs(spaces, members, rows_dev, low_code, high_code):
    full_rows = rows_dev * spaces
    out_rows = UP * full_rows
    own_rows = out_rows // spaces
    part_rows = own_rows // members
    window_rows = (part_rows - 1) // UP + 3
    need = []
    for place in range(spaces):
        blocks = set()
        for numer in range(low_code // 2, high_code // 2 + 1):
            valid = full_rows * numer // 14
            for target in range(members):
                first_row = place * own_rows + target * part_rows
                pos = (2 * first_row + 1) * valid - out_rows
                lower = 0 if pos < 0 else pos // (2 * out_rows)
                lower = valid - 1 if lower >= valid - 1 else lower
                begin = min(max(lower, 0), full_rows - window_rows)
                blocks |= set(range(begin // rows_dev, (begin + window_rows - 1) // rows_dev + 1))
        need.append(blocks)
    return need


def resize_matrix(positions, out_len, valid, in_len):
    numer = (2 * positions + 1) * valid - out_len
    denom = 2 * out_len
    lower = numer // denom
    frac = (numer - lower * denom).astype(jnp.float32) / denom
    below = numer < 0
    frac = jnp.where(below, jnp.float32(0.0), frac)
    lower = jnp.where(below, 0, lower)
    top_index = valid - 1
    over = lower >= top_index
    frac = jnp.where(over, jnp.float32(0.0), frac)
    lower = jnp.where(over, top_index, lower)
    columns = jnp.arange(in_len, dtype=jnp.int32)
    first = jnp.where(columns[None, :] == lower[:, None], 1.0 - frac[:, None], jnp.float32(0.0))
    second = jnp.where(columns[None, :] == lower[:, None] + 1, frac[:, None], jnp.float32(0.0))
    return (first + second).astype(jnp.bfloat16)


def run_conv(x_ref, w_ref, bias, lo, hi, good_cols, o_ref, width, block, head=None):
    flat = block * width
    outs = w_ref.shape[2]
    place = lax.broadcasted_iota(jnp.int32, (1, flat), 1)
    col = place % width
    stacked = jnp.concatenate(
        [jnp.concatenate([w_ref[a, b] for a in range(3)], axis=1) for b in range(3)], axis=0
    )

    def step(i, carry):
        r0 = i * block
        rhs = jnp.concatenate(
            [x_ref[:, pl.ds(pl.multiple_of((r0 + a) * width, width), flat)] for a in range(3)],
            axis=0,
        )
        res = jnp.dot(stacked, rhs, preferred_element_type=jnp.float32)
        taps = [res[b * outs:(b + 1) * outs] for b in range(3)]
        left = jnp.where(col == 0, 0.0, pltpu.roll(taps[0], 1, 1))
        right = jnp.where(col == width - 1, 0.0, pltpu.roll(taps[2], flat - 1, 1))
        total = jnp.maximum(taps[1] + left + right + bias, 0.0)
        row = r0 + place // width
        keep = (row >= lo) & (row < hi) & (col < good_cols)
        out = jnp.where(keep, total, 0.0).astype(jnp.bfloat16)
        if head is not None:
            out = jnp.dot(head[0], out, preferred_element_type=jnp.float32) + head[1]
        o_ref[:, pl.ds(pl.multiple_of(r0 * width, width), flat)] = out.astype(o_ref.dtype)
        return carry

    lax.fori_loop(0, o_ref.shape[1] // flat, step, 0, unroll=True)


def first_body(main_ref, top_ref, low_ref, w_ref, b_ref, s_ref, o_ref, x_ref, *, width, block, halo):
    lo_in, hi_in, good_cols, lo, hi = s_ref[0], s_ref[1], s_ref[2], s_ref[3], s_ref[4]
    chans = main_ref.shape[0]
    rows_main = main_ref.shape[1] // width

    def put(src, offset, rows):
        place = lax.broadcasted_iota(jnp.int32, (1, rows * width), 1)
        row = offset + place // width
        keep = (row >= lo_in) & (row < hi_in) & (place % width < good_cols)
        x_ref[:, pl.ds(pl.multiple_of(offset * width, width), rows * width)] = jnp.where(
            keep, src, jnp.zeros_like(src)
        )

    put(top_ref[...], 0, halo)
    put(low_ref[...], halo + rows_main, halo)

    def chunk(i, carry):
        start = pl.multiple_of(i * 2 * width, width)
        put(main_ref[:, pl.ds(start, 2 * width)], halo + 2 * i, 2)
        return carry

    lax.fori_loop(0, rows_main // 2, chunk, 0)
    run_conv(x_ref, w_ref, b_ref[pl.ds(0, chans), 0:1], lo, hi, good_cols, o_ref, width, block)


def second_body(x_ref, w_ref, b_ref, k_ref, s_ref, o_ref, *, width, block):
    chans = x_ref.shape[0]
    classes = k_ref.shape[0]
    head = (k_ref[...], b_ref[pl.ds(2 * chans, classes), 0:1])
    lo, hi, good_cols = s_ref[5], s_ref[6], s_ref[2]
    run_conv(x_ref, w_ref, b_ref[pl.ds(chans, chans), 0:1], lo, hi, good_cols, o_ref, width, block, head)


def pick_block(rows):
    return next(k for k in (8, 3, 4, 2, 1) if rows % k == 0)


def conv_first_layer(feat, top, low, width, weights, biases, limits):
    chans = feat.shape[0]
    rows_main = feat.shape[1] // width
    halo = top.shape[1] // width
    rows_in = rows_main + 2 * halo
    rows_out = rows_in - 2
    outs = weights.shape[2]
    block = pick_block(rows_out)
    vmem = pl.BlockSpec(memory_space=pltpu.VMEM)
    cost = pl.CostEstimate(
        flops=2 * 9 * rows_out * width * chans * outs,
        bytes_accessed=2 * (chans * rows_in * width + weights.size + rows_out * width * outs),
        transcendentals=0,
    )
    out = pl.pallas_call(
        functools.partial(first_body, width=width, block=block, halo=halo),
        out_shape=jax.ShapeDtypeStruct((outs, rows_out * width), jnp.bfloat16),
        in_specs=[vmem] * 5 + [pl.BlockSpec(memory_space=pltpu.SMEM)],
        out_specs=vmem,
        scratch_shapes=[pltpu.VMEM((chans, rows_in * width), jnp.bfloat16)],
        cost_estimate=cost,
    )(
        feat,
        top,
        low,
        weights,
        biases,
        limits,
    )
    return out


def conv_second_layer(x, width, weights, biases, head, limits):
    chans, flat_in = x.shape
    rows_out = flat_in // width - 2
    outs = weights.shape[2]
    classes = head.shape[0]
    block = pick_block(rows_out)
    vmem = pl.BlockSpec(memory_space=pltpu.VMEM)
    cost = pl.CostEstimate(
        flops=2 * 9 * rows_out * width * chans * outs + 2 * rows_out * width * outs * classes,
        bytes_accessed=2 * (x.size + weights.size + rows_out * width * classes),
        transcendentals=0,
    )
    out = pl.pallas_call(
        functools.partial(second_body, width=width, block=block),
        out_shape=jax.ShapeDtypeStruct((classes, rows_out * width), jnp.bfloat16),
        in_specs=[vmem] * 4 + [pl.BlockSpec(memory_space=pltpu.SMEM)],
        out_specs=vmem,
        cost_estimate=cost,
    )(x, weights, biases, head, limits)
    return out.reshape(classes, rows_out, width)


def window_start(numer, first_row, full_rows, out_rows, window_rows):
    valid = full_rows * numer // 14
    numer_pos = (2 * first_row + 1) * valid - out_rows
    lower = numer_pos // (2 * out_rows)
    lower = jnp.where(numer_pos < 0, 0, lower)
    lower = jnp.where(lower >= valid - 1, valid - 1, lower)
    return jnp.clip(lower, 0, full_rows - window_rows)


def column_table(numer, flip, cols, out_cols):
    valid_cols = cols * numer // 14
    col_pos = jnp.arange(out_cols, dtype=jnp.int32)
    col_pos = jnp.where(flip == 1, out_cols - 1 - col_pos, col_pos)
    return resize_matrix(col_pos, out_cols, valid_cols, cols)


def shards(features, views, conv_first, bias_first, conv_second, bias_second, classify, class_bias):
    feat = features[0]
    rows_dev, cols = (feat.shape[1], feat.shape[2])
    spaces = lax.axis_size("space")
    full_rows = rows_dev * spaces
    place = lax.axis_index("space")
    member_index = lax.axis_index("member")
    members = views.shape[0]
    picked = jnp.arange(members, dtype=jnp.int32) == member_index
    code = jnp.sum(jnp.where(picked, views, 0))
    numer = code // 2
    valid_rows = full_rows * numer // 14
    valid_cols = cols * numer // 14
    count = lax.axis_size("space")
    halo = 2
    forward = [(i, i + 1) for i in range(count - 1)]
    backward = [(target, source) for source, target in forward]
    flat_feat = feat.reshape(feat.shape[0], rows_dev * cols)
    top_rows = lax.ppermute(flat_feat[:, (rows_dev - halo) * cols:], "space", forward)
    low_rows = lax.ppermute(flat_feat[:, : halo * cols], "space", backward)
    top = place * rows_dev
    offsets = jnp.array([halo, halo, 0, 1, 1, 0, 0], jnp.int32)
    of_top = jnp.array([-1, -1, 0, -1, -1, -1, -1], jnp.int32)
    of_rows = jnp.array([0, 1, 0, 0, 1, 0, 1], jnp.int32)
    of_cols = jnp.array([0, 0, 1, 0, 0, 0, 0], jnp.int32)
    limits = offsets + of_top * top + of_rows * valid_rows + of_cols * valid_cols
    biases = jnp.concatenate([bias_first, bias_second, class_bias])
    biases = jnp.broadcast_to(biases[:, None], (biases.shape[0], 128))
    hidden = conv_first_layer(flat_feat, top_rows, low_rows, cols, conv_first, biases, limits)
    logits = conv_second_layer(hidden, cols, conv_second, biases, classify, limits)
    out_rows = UP * full_rows
    out_cols = UP * cols
    own_rows = out_rows // spaces
    part_rows = own_rows // members
    window_rows = (part_rows - 1) // UP + 3
    need = block_needs(spaces, members, rows_dev, LOW_CODE, HIGH_CODE)
    gathered = gather_rows(logits, "space", need)
    pieces = []
    for target in range(members):
        first_row = place * own_rows + target * part_rows
        begin = window_start(numer, first_row, full_rows, out_rows, window_rows)
        pieces.append(lax.dynamic_slice_in_dim(gathered, begin, window_rows, 1))
    outgoing = jnp.stack(pieces, 0)
    own_first = place * own_rows + member_index * part_rows
    positions = own_first + jnp.arange(part_rows, dtype=jnp.int32)
    result = jnp.zeros((part_rows, logits.shape[0], out_cols), jnp.float32)
    for shift in range(members):
        if shift == 0:
            arrived = lax.dynamic_index_in_dim(outgoing, member_index, 0, keepdims=False)
        else:
            send = lax.dynamic_index_in_dim(
                outgoing, (member_index + shift) % members, 0, keepdims=False
            )
            arrived = lax.ppermute(
                send, "member", [(i, (i + shift) % members) for i in range(members)]
            )
        source = (member_index - shift) % members
        source_code = jnp.sum(jnp.where(jnp.arange(members) == source, views, 0))
        source_numer = source_code // 2
        source_flip = source_code % 2
        source_valid = full_rows * source_numer // 14
        begin = window_start(source_numer, own_first, full_rows, out_rows, window_rows)
        source_cols = column_table(source_numer, source_flip, cols, out_cols)
        row_table = resize_matrix(positions, out_rows, source_valid, full_rows)
        row_part = lax.dynamic_slice_in_dim(row_table, begin, window_rows, 1)
        widened = jnp.einsum(
            "cyx,jx->cyj", arrived, source_cols, preferred_element_type=jnp.float32
        ).astype(jnp.bfloat16)
        result = result + jnp.einsum(
            "iy,cyj->icj", row_part, widened, preferred_element_type=jnp.float32
        )
    return result


def solution(mesh):
    placed = (
        P(("groups", "member"), None, "space", None),
        P("groups"),
        P(),
        P(),
        P(),
        P(),
        P(),
        P(),
    )
    return jax.shard_map(
        shards,
        mesh=mesh,
        in_specs=placed,
        out_specs=P(("groups", "space", "member"), None, None),
        check_vma=False,
    )
```

```python
import functools

import jax
import jax.numpy as jnp
from jax import lax
from jax.experimental import pallas as pl
from jax.experimental.pallas import tpu as pltpu
from jax.sharding import PartitionSpec as P

UP = 4
LOW_CODE = 8
HIGH_CODE = 29


def with_halo(block, sides, width):
    for axis, dim in sides:
        count = lax.axis_size(axis)
        forward = [(i, i + 1) for i in range(count - 1)]
        backward = [(target, source) for source, target in forward]
        low = lax.ppermute(
            lax.slice_in_dim(block, block.shape[dim] - width, None, axis=dim), axis, forward
        )
        high = lax.ppermute(lax.slice_in_dim(block, 0, width, axis=dim), axis, backward)
        block = jnp.concatenate([low, block, high], axis=dim)
    return block


def gather_rows(block, axis, need):
    count = lax.axis_size(axis)
    if count & (count - 1):
        return lax.all_gather(block, axis, axis=1, tiled=True)
    me = lax.axis_index(axis)
    lead, rows, rest = block.shape[0], block.shape[1], block.shape[2:]
    held = block[:, None]
    bit = count // 2
    while bit:
        span = 2 * bit
        routes = {}
        for p in range(held.shape[1]):
            pairs = []
            for i in range(count):
                j = i ^ bit
                wanted = set().union(*[need[g] for g in range(count) if g // bit == j // bit])
                if p * span + i % span in wanted:
                    pairs.append((i, j))
            routes.setdefault(tuple(pairs), []).append(p)
        if bit == 1 or len(routes) == 1:
            pairs = sorted(set().union(*[set(r) for r in routes]))
            other = lax.ppermute(held, axis, pairs)
        else:
            parts = [None] * held.shape[1]
            for pairs, places in routes.items():
                if pairs:
                    for p in places:
                        parts[p] = lax.ppermute(held[:, p:p + 1], axis, list(pairs))
            empty = jnp.zeros_like(held[:, :1])
            other = jnp.concatenate([empty if x is None else x for x in parts], 1)
        upper = (me & bit) != 0
        held = jnp.where(upper, jnp.stack([other, held], 2), jnp.stack([held, other], 2))
        held = held.reshape((lead, -1, rows) + rest)
        bit //= 2
    return held.reshape((lead, count * rows) + rest)


def block_needs(spaces, members, rows_dev, low_code, high_code):
    full_rows = rows_dev * spaces
    out_rows = UP * full_rows
    own_rows = out_rows // spaces
    part_rows = own_rows // members
    window_rows = (part_rows - 1) // UP + 3
    need = []
    for place in range(spaces):
        blocks = set()
        for numer in range(low_code // 2, high_code // 2 + 1):
            valid = full_rows * numer // 14
            for target in range(members):
                first_row = place * own_rows + target * part_rows
                pos = (2 * first_row + 1) * valid - out_rows
                lower = 0 if pos < 0 else pos // (2 * out_rows)
                lower = valid - 1 if lower >= valid - 1 else lower
                begin = min(max(lower, 0), full_rows - window_rows)
                blocks |= set(range(begin // rows_dev, (begin + window_rows - 1) // rows_dev + 1))
        need.append(blocks)
    return need


def resize_matrix(positions, out_len, valid, in_len):
    numer = (2 * positions + 1) * valid - out_len
    denom = 2 * out_len
    lower = numer // denom
    frac = (numer - lower * denom).astype(jnp.float32) / denom
    below = numer < 0
    frac = jnp.where(below, jnp.float32(0.0), frac)
    lower = jnp.where(below, 0, lower)
    top_index = valid - 1
    over = lower >= top_index
    frac = jnp.where(over, jnp.float32(0.0), frac)
    lower = jnp.where(over, top_index, lower)
    columns = jnp.arange(in_len, dtype=jnp.int32)
    first = jnp.where(columns[None, :] == lower[:, None], 1.0 - frac[:, None], jnp.float32(0.0))
    second = jnp.where(columns[None, :] == lower[:, None] + 1, frac[:, None], jnp.float32(0.0))
    return (first + second).astype(jnp.bfloat16)


def run_conv(x_ref, w_ref, bias, lo, hi, good_cols, o_ref, width, block, head=None):
    flat = block * width
    outs = w_ref.shape[2]
    place = lax.broadcasted_iota(jnp.int32, (1, flat), 1)
    col = place % width
    stacked = jnp.concatenate(
        [jnp.concatenate([w_ref[a, b] for a in range(3)], axis=1) for b in range(3)], axis=0
    )

    def step(i, carry):
        r0 = i * block
        rhs = jnp.concatenate(
            [x_ref[:, pl.ds(pl.multiple_of((r0 + a) * width, width), flat)] for a in range(3)],
            axis=0,
        )
        res = jnp.dot(stacked, rhs, preferred_element_type=jnp.float32)
        taps = [res[b * outs:(b + 1) * outs] for b in range(3)]
        left = jnp.where(col == 0, 0.0, pltpu.roll(taps[0], 1, 1))
        right = jnp.where(col == width - 1, 0.0, pltpu.roll(taps[2], flat - 1, 1))
        total = jnp.maximum(taps[1] + left + right + bias, 0.0)
        row = r0 + place // width
        keep = (row >= lo) & (row < hi) & (col < good_cols)
        out = jnp.where(keep, total, 0.0).astype(jnp.bfloat16)
        if head is not None:
            out = jnp.dot(head[0], out, preferred_element_type=jnp.float32) + head[1]
        o_ref[:, pl.ds(pl.multiple_of(r0 * width, width), flat)] = out.astype(o_ref.dtype)
        return carry

    lax.fori_loop(0, o_ref.shape[1] // flat, step, 0, unroll=True)


def first_body(main_ref, top_ref, low_ref, w_ref, b_ref, s_ref, o_ref, x_ref, *, width, block, halo):
    lo_in, hi_in, good_cols, lo, hi = s_ref[0], s_ref[1], s_ref[2], s_ref[3], s_ref[4]
    chans = main_ref.shape[0]
    rows_main = main_ref.shape[1] // width

    def put(src, offset, rows):
        place = lax.broadcasted_iota(jnp.int32, (1, rows * width), 1)
        row = offset + place // width
        keep = (row >= lo_in) & (row < hi_in) & (place % width < good_cols)
        x_ref[:, pl.ds(pl.multiple_of(offset * width, width), rows * width)] = jnp.where(
            keep, src, jnp.zeros_like(src)
        )

    put(top_ref[...], 0, halo)
    put(low_ref[...], halo + rows_main, halo)

    def chunk(i, carry):
        start = pl.multiple_of(i * 2 * width, width)
        put(main_ref[:, pl.ds(start, 2 * width)], halo + 2 * i, 2)
        return carry

    lax.fori_loop(0, rows_main // 2, chunk, 0)
    run_conv(x_ref, w_ref, b_ref[pl.ds(0, chans), 0:1], lo, hi, good_cols, o_ref, width, block)


def second_body(x_ref, w_ref, b_ref, k_ref, s_ref, o_ref, *, width, block):
    chans = x_ref.shape[0]
    classes = k_ref.shape[0]
    head = (k_ref[...], b_ref[pl.ds(2 * chans, classes), 0:1])
    lo, hi, good_cols = s_ref[5], s_ref[6], s_ref[2]
    run_conv(x_ref, w_ref, b_ref[pl.ds(chans, chans), 0:1], lo, hi, good_cols, o_ref, width, block, head)


def pick_block(rows):
    return next(k for k in (16, 3, 4, 2, 1) if rows % k == 0)


def conv_first_layer(feat, top, low, width, weights, biases, limits):
    chans = feat.shape[0]
    rows_main = feat.shape[1] // width
    halo = top.shape[1] // width
    rows_in = rows_main + 2 * halo
    rows_out = rows_in - 2
    outs = weights.shape[2]
    block = pick_block(rows_out)
    vmem = pl.BlockSpec(memory_space=pltpu.VMEM)
    cost = pl.CostEstimate(
        flops=2 * 9 * rows_out * width * chans * outs,
        bytes_accessed=2 * (chans * rows_in * width + weights.size + rows_out * width * outs),
        transcendentals=0,
    )
    out = pl.pallas_call(
        functools.partial(first_body, width=width, block=block, halo=halo),
        out_shape=jax.ShapeDtypeStruct((outs, rows_out * width), jnp.bfloat16),
        in_specs=[vmem] * 5 + [pl.BlockSpec(memory_space=pltpu.SMEM)],
        out_specs=vmem,
        scratch_shapes=[pltpu.VMEM((chans, rows_in * width), jnp.bfloat16)],
        cost_estimate=cost,
    )(
        feat,
        top,
        low,
        weights,
        biases,
        limits,
    )
    return out


def conv_second_layer(x, width, weights, biases, head, limits):
    chans, flat_in = x.shape
    rows_out = flat_in // width - 2
    outs = weights.shape[2]
    classes = head.shape[0]
    block = pick_block(rows_out)
    vmem = pl.BlockSpec(memory_space=pltpu.VMEM)
    cost = pl.CostEstimate(
        flops=2 * 9 * rows_out * width * chans * outs + 2 * rows_out * width * outs * classes,
        bytes_accessed=2 * (x.size + weights.size + rows_out * width * classes),
        transcendentals=0,
    )
    out = pl.pallas_call(
        functools.partial(second_body, width=width, block=block),
        out_shape=jax.ShapeDtypeStruct((classes, rows_out * width), jnp.bfloat16),
        in_specs=[vmem] * 4 + [pl.BlockSpec(memory_space=pltpu.SMEM)],
        out_specs=vmem,
        cost_estimate=cost,
    )(x, weights, biases, head, limits)
    return out.reshape(classes, rows_out, width)


def window_start(numer, first_row, full_rows, out_rows, window_rows):
    valid = full_rows * numer // 14
    numer_pos = (2 * first_row + 1) * valid - out_rows
    lower = numer_pos // (2 * out_rows)
    lower = jnp.where(numer_pos < 0, 0, lower)
    lower = jnp.where(lower >= valid - 1, valid - 1, lower)
    return jnp.clip(lower, 0, full_rows - window_rows)


def column_table(numer, flip, cols, out_cols):
    valid_cols = cols * numer // 14
    col_pos = jnp.arange(out_cols, dtype=jnp.int32)
    col_pos = jnp.where(flip == 1, out_cols - 1 - col_pos, col_pos)
    return resize_matrix(col_pos, out_cols, valid_cols, cols)


def shards(features, views, conv_first, bias_first, conv_second, bias_second, classify, class_bias):
    feat = features[0]
    rows_dev, cols = (feat.shape[1], feat.shape[2])
    spaces = lax.axis_size("space")
    full_rows = rows_dev * spaces
    place = lax.axis_index("space")
    member_index = lax.axis_index("member")
    members = views.shape[0]
    picked = jnp.arange(members, dtype=jnp.int32) == member_index
    code = jnp.sum(jnp.where(picked, views, 0))
    numer = code // 2
    valid_rows = full_rows * numer // 14
    valid_cols = cols * numer // 14
    count = lax.axis_size("space")
    halo = 2
    forward = [(i, i + 1) for i in range(count - 1)]
    backward = [(target, source) for source, target in forward]
    flat_feat = feat.reshape(feat.shape[0], rows_dev * cols)
    top_rows = lax.ppermute(flat_feat[:, (rows_dev - halo) * cols:], "space", forward)
    low_rows = lax.ppermute(flat_feat[:, : halo * cols], "space", backward)
    top = place * rows_dev
    offsets = jnp.array([halo, halo, 0, 1, 1, 0, 0], jnp.int32)
    of_top = jnp.array([-1, -1, 0, -1, -1, -1, -1], jnp.int32)
    of_rows = jnp.array([0, 1, 0, 0, 1, 0, 1], jnp.int32)
    of_cols = jnp.array([0, 0, 1, 0, 0, 0, 0], jnp.int32)
    limits = offsets + of_top * top + of_rows * valid_rows + of_cols * valid_cols
    biases = jnp.concatenate([bias_first, bias_second, class_bias])
    biases = jnp.broadcast_to(biases[:, None], (biases.shape[0], 128))
    hidden = conv_first_layer(flat_feat, top_rows, low_rows, cols, conv_first, biases, limits)
    logits = conv_second_layer(hidden, cols, conv_second, biases, classify, limits)
    out_rows = UP * full_rows
    out_cols = UP * cols
    own_rows = out_rows // spaces
    part_rows = own_rows // members
    window_rows = (part_rows - 1) // UP + 3
    need = block_needs(spaces, members, rows_dev, LOW_CODE, HIGH_CODE)
    gathered = gather_rows(logits, "space", need)
    pieces = []
    for target in range(members):
        first_row = place * own_rows + target * part_rows
        begin = window_start(numer, first_row, full_rows, out_rows, window_rows)
        pieces.append(lax.dynamic_slice_in_dim(gathered, begin, window_rows, 1))
    outgoing = jnp.stack(pieces, 0)
    own_first = place * own_rows + member_index * part_rows
    positions = own_first + jnp.arange(part_rows, dtype=jnp.int32)
    result = jnp.zeros((part_rows, logits.shape[0], out_cols), jnp.float32)
    for shift in range(members):
        if shift == 0:
            arrived = lax.dynamic_index_in_dim(outgoing, member_index, 0, keepdims=False)
        else:
            send = lax.dynamic_index_in_dim(
                outgoing, (member_index + shift) % members, 0, keepdims=False
            )
            arrived = lax.ppermute(
                send, "member", [(i, (i + shift) % members) for i in range(members)]
            )
        source = (member_index - shift) % members
        source_code = jnp.sum(jnp.where(jnp.arange(members) == source, views, 0))
        source_numer = source_code // 2
        source_flip = source_code % 2
        source_valid = full_rows * source_numer // 14
        begin = window_start(source_numer, own_first, full_rows, out_rows, window_rows)
        source_cols = column_table(source_numer, source_flip, cols, out_cols)
        row_table = resize_matrix(positions, out_rows, source_valid, full_rows)
        row_part = lax.dynamic_slice_in_dim(row_table, begin, window_rows, 1)
        widened = jnp.einsum(
            "cyx,jx->cyj", arrived, source_cols, preferred_element_type=jnp.float32
        ).astype(jnp.bfloat16)
        result = result + jnp.einsum(
            "iy,cyj->icj", row_part, widened, preferred_element_type=jnp.float32
        )
    return result


def solution(mesh):
    placed = (
        P(("groups", "member"), None, "space", None),
        P("groups"),
        P(),
        P(),
        P(),
        P(),
        P(),
        P(),
    )
    return jax.shard_map(
        shards,
        mesh=mesh,
        in_specs=placed,
        out_specs=P(("groups", "space", "member"), None, None),
        check_vma=False,
    )
```

```python
import functools

import jax
import jax.numpy as jnp
from jax import lax
from jax.experimental import pallas as pl
from jax.experimental.pallas import tpu as pltpu
from jax.sharding import PartitionSpec as P

UP = 4
LOW_CODE = 8
HIGH_CODE = 29


def with_halo(block, sides, width):
    for axis, dim in sides:
        count = lax.axis_size(axis)
        forward = [(i, i + 1) for i in range(count - 1)]
        backward = [(target, source) for source, target in forward]
        low = lax.ppermute(
            lax.slice_in_dim(block, block.shape[dim] - width, None, axis=dim), axis, forward
        )
        high = lax.ppermute(lax.slice_in_dim(block, 0, width, axis=dim), axis, backward)
        block = jnp.concatenate([low, block, high], axis=dim)
    return block


def gather_rows(block, axis, need):
    count = lax.axis_size(axis)
    if count & (count - 1):
        return lax.all_gather(block, axis, axis=1, tiled=True)
    me = lax.axis_index(axis)
    lead, rows, rest = block.shape[0], block.shape[1], block.shape[2:]
    held = block[:, None]
    bit = count // 2
    while bit:
        span = 2 * bit
        routes = {}
        for p in range(held.shape[1]):
            pairs = []
            for i in range(count):
                j = i ^ bit
                wanted = set().union(*[need[g] for g in range(count) if g // bit == j // bit])
                if p * span + i % span in wanted:
                    pairs.append((i, j))
            routes.setdefault(tuple(pairs), []).append(p)
        if bit == 1 or len(routes) == 1:
            pairs = sorted(set().union(*[set(r) for r in routes]))
            other = lax.ppermute(held, axis, pairs)
        else:
            parts = [None] * held.shape[1]
            for pairs, places in routes.items():
                if pairs:
                    for p in places:
                        parts[p] = lax.ppermute(held[:, p:p + 1], axis, list(pairs))
            empty = jnp.zeros_like(held[:, :1])
            other = jnp.concatenate([empty if x is None else x for x in parts], 1)
        upper = (me & bit) != 0
        held = jnp.where(upper, jnp.stack([other, held], 2), jnp.stack([held, other], 2))
        held = held.reshape((lead, -1, rows) + rest)
        bit //= 2
    return held.reshape((lead, count * rows) + rest)


def block_needs(spaces, members, rows_dev, low_code, high_code):
    full_rows = rows_dev * spaces
    out_rows = UP * full_rows
    own_rows = out_rows // spaces
    part_rows = own_rows // members
    window_rows = (part_rows - 1) // UP + 3
    need = []
    for place in range(spaces):
        blocks = set()
        for numer in range(low_code // 2, high_code // 2 + 1):
            valid = full_rows * numer // 14
            for target in range(members):
                first_row = place * own_rows + target * part_rows
                pos = (2 * first_row + 1) * valid - out_rows
                lower = 0 if pos < 0 else pos // (2 * out_rows)
                lower = valid - 1 if lower >= valid - 1 else lower
                begin = min(max(lower, 0), full_rows - window_rows)
                blocks |= set(range(begin // rows_dev, (begin + window_rows - 1) // rows_dev + 1))
        need.append(blocks)
    return need


def resize_matrix(positions, out_len, valid, in_len):
    numer = (2 * positions + 1) * valid - out_len
    denom = 2 * out_len
    lower = numer // denom
    frac = (numer - lower * denom).astype(jnp.float32) / denom
    below = numer < 0
    frac = jnp.where(below, jnp.float32(0.0), frac)
    lower = jnp.where(below, 0, lower)
    top_index = valid - 1
    over = lower >= top_index
    frac = jnp.where(over, jnp.float32(0.0), frac)
    lower = jnp.where(over, top_index, lower)
    columns = jnp.arange(in_len, dtype=jnp.int32)
    first = jnp.where(columns[None, :] == lower[:, None], 1.0 - frac[:, None], jnp.float32(0.0))
    second = jnp.where(columns[None, :] == lower[:, None] + 1, frac[:, None], jnp.float32(0.0))
    return (first + second).astype(jnp.bfloat16)


def run_conv(x_ref, w_ref, bias, lo, hi, good_cols, o_ref, width, block, head=None):
    flat = block * width
    outs = w_ref.shape[2]
    place = lax.broadcasted_iota(jnp.int32, (1, flat), 1)
    col = place % width
    stacked = jnp.concatenate(
        [jnp.concatenate([w_ref[a, b] for a in range(3)], axis=1) for b in range(3)], axis=0
    )

    def step(i, carry):
        r0 = i * block
        rhs = jnp.concatenate(
            [x_ref[:, pl.ds(pl.multiple_of((r0 + a) * width, width), flat)] for a in range(3)],
            axis=0,
        )
        res = jnp.dot(stacked, rhs, preferred_element_type=jnp.float32)
        taps = [res[b * outs:(b + 1) * outs] for b in range(3)]
        left = jnp.where(col == 0, 0.0, pltpu.roll(taps[0], 1, 1))
        right = jnp.where(col == width - 1, 0.0, pltpu.roll(taps[2], flat - 1, 1))
        total = jnp.maximum(taps[1] + left + right + bias, 0.0)
        row = r0 + place // width
        keep = (row >= lo) & (row < hi) & (col < good_cols)
        out = jnp.where(keep, total, 0.0).astype(jnp.bfloat16)
        if head is not None:
            out = jnp.dot(head[0], out, preferred_element_type=jnp.float32) + head[1]
        o_ref[:, pl.ds(pl.multiple_of(r0 * width, width), flat)] = out.astype(o_ref.dtype)
        return carry

    lax.fori_loop(0, o_ref.shape[1] // flat, step, 0, unroll=True)


def first_body(main_ref, top_ref, low_ref, w_ref, b_ref, s_ref, o_ref, x_ref, *, width, block, halo):
    lo_in, hi_in, good_cols, lo, hi = s_ref[0], s_ref[1], s_ref[2], s_ref[3], s_ref[4]
    chans = main_ref.shape[0]
    rows_main = main_ref.shape[1] // width

    def put(src, offset, rows):
        place = lax.broadcasted_iota(jnp.int32, (1, rows * width), 1)
        row = offset + place // width
        keep = (row >= lo_in) & (row < hi_in) & (place % width < good_cols)
        x_ref[:, pl.ds(pl.multiple_of(offset * width, width), rows * width)] = jnp.where(
            keep, src, jnp.zeros_like(src)
        )

    put(top_ref[...], 0, halo)
    put(low_ref[...], halo + rows_main, halo)

    def chunk(i, carry):
        start = pl.multiple_of(i * 2 * width, width)
        put(main_ref[:, pl.ds(start, 2 * width)], halo + 2 * i, 2)
        return carry

    lax.fori_loop(0, rows_main // 2, chunk, 0)
    run_conv(x_ref, w_ref, b_ref[pl.ds(0, chans), 0:1], lo, hi, good_cols, o_ref, width, block)


def second_body(x_ref, w_ref, b_ref, k_ref, s_ref, o_ref, *, width, block):
    chans = x_ref.shape[0]
    classes = k_ref.shape[0]
    head = (k_ref[...], b_ref[pl.ds(2 * chans, classes), 0:1])
    lo, hi, good_cols = s_ref[5], s_ref[6], s_ref[2]
    run_conv(x_ref, w_ref, b_ref[pl.ds(chans, chans), 0:1], lo, hi, good_cols, o_ref, width, block, head)


def pick_block(rows):
    return next(k for k in (18, 16, 3, 4, 2, 1) if rows % k == 0)


def conv_first_layer(feat, top, low, width, weights, biases, limits):
    chans = feat.shape[0]
    rows_main = feat.shape[1] // width
    halo = top.shape[1] // width
    rows_in = rows_main + 2 * halo
    rows_out = rows_in - 2
    outs = weights.shape[2]
    block = pick_block(rows_out)
    vmem = pl.BlockSpec(memory_space=pltpu.VMEM)
    cost = pl.CostEstimate(
        flops=2 * 9 * rows_out * width * chans * outs,
        bytes_accessed=2 * (chans * rows_in * width + weights.size + rows_out * width * outs),
        transcendentals=0,
    )
    out = pl.pallas_call(
        functools.partial(first_body, width=width, block=block, halo=halo),
        out_shape=jax.ShapeDtypeStruct((outs, rows_out * width), jnp.bfloat16),
        in_specs=[vmem] * 5 + [pl.BlockSpec(memory_space=pltpu.SMEM)],
        out_specs=vmem,
        scratch_shapes=[pltpu.VMEM((chans, rows_in * width), jnp.bfloat16)],
        cost_estimate=cost,
    )(
        feat,
        top,
        low,
        weights,
        biases,
        limits,
    )
    return out


def conv_second_layer(x, width, weights, biases, head, limits):
    chans, flat_in = x.shape
    rows_out = flat_in // width - 2
    outs = weights.shape[2]
    classes = head.shape[0]
    block = pick_block(rows_out)
    vmem = pl.BlockSpec(memory_space=pltpu.VMEM)
    cost = pl.CostEstimate(
        flops=2 * 9 * rows_out * width * chans * outs + 2 * rows_out * width * outs * classes,
        bytes_accessed=2 * (x.size + weights.size + rows_out * width * classes),
        transcendentals=0,
    )
    out = pl.pallas_call(
        functools.partial(second_body, width=width, block=block),
        out_shape=jax.ShapeDtypeStruct((classes, rows_out * width), jnp.bfloat16),
        in_specs=[vmem] * 4 + [pl.BlockSpec(memory_space=pltpu.SMEM)],
        out_specs=vmem,
        cost_estimate=cost,
    )(x, weights, biases, head, limits)
    return out.reshape(classes, rows_out, width)


def window_start(numer, first_row, full_rows, out_rows, window_rows):
    valid = full_rows * numer // 14
    numer_pos = (2 * first_row + 1) * valid - out_rows
    lower = numer_pos // (2 * out_rows)
    lower = jnp.where(numer_pos < 0, 0, lower)
    lower = jnp.where(lower >= valid - 1, valid - 1, lower)
    return jnp.clip(lower, 0, full_rows - window_rows)


def column_table(numer, flip, cols, out_cols):
    valid_cols = cols * numer // 14
    col_pos = jnp.arange(out_cols, dtype=jnp.int32)
    col_pos = jnp.where(flip == 1, out_cols - 1 - col_pos, col_pos)
    return resize_matrix(col_pos, out_cols, valid_cols, cols)


def shards(features, views, conv_first, bias_first, conv_second, bias_second, classify, class_bias):
    feat = features[0]
    rows_dev, cols = (feat.shape[1], feat.shape[2])
    spaces = lax.axis_size("space")
    full_rows = rows_dev * spaces
    place = lax.axis_index("space")
    member_index = lax.axis_index("member")
    members = views.shape[0]
    picked = jnp.arange(members, dtype=jnp.int32) == member_index
    code = jnp.sum(jnp.where(picked, views, 0))
    numer = code // 2
    valid_rows = full_rows * numer // 14
    valid_cols = cols * numer // 14
    count = lax.axis_size("space")
    halo = 2
    forward = [(i, i + 1) for i in range(count - 1)]
    backward = [(target, source) for source, target in forward]
    flat_feat = feat.reshape(feat.shape[0], rows_dev * cols)
    top_rows = lax.ppermute(flat_feat[:, (rows_dev - halo) * cols:], "space", forward)
    low_rows = lax.ppermute(flat_feat[:, : halo * cols], "space", backward)
    top = place * rows_dev
    offsets = jnp.array([halo, halo, 0, 1, 1, 0, 0], jnp.int32)
    of_top = jnp.array([-1, -1, 0, -1, -1, -1, -1], jnp.int32)
    of_rows = jnp.array([0, 1, 0, 0, 1, 0, 1], jnp.int32)
    of_cols = jnp.array([0, 0, 1, 0, 0, 0, 0], jnp.int32)
    limits = offsets + of_top * top + of_rows * valid_rows + of_cols * valid_cols
    biases = jnp.concatenate([bias_first, bias_second, class_bias])
    biases = jnp.broadcast_to(biases[:, None], (biases.shape[0], 128))
    hidden = conv_first_layer(flat_feat, top_rows, low_rows, cols, conv_first, biases, limits)
    logits = conv_second_layer(hidden, cols, conv_second, biases, classify, limits)
    out_rows = UP * full_rows
    out_cols = UP * cols
    own_rows = out_rows // spaces
    part_rows = own_rows // members
    window_rows = (part_rows - 1) // UP + 3
    need = block_needs(spaces, members, rows_dev, LOW_CODE, HIGH_CODE)
    gathered = gather_rows(logits, "space", need)
    pieces = []
    for target in range(members):
        first_row = place * own_rows + target * part_rows
        begin = window_start(numer, first_row, full_rows, out_rows, window_rows)
        pieces.append(lax.dynamic_slice_in_dim(gathered, begin, window_rows, 1))
    outgoing = jnp.stack(pieces, 0)
    own_first = place * own_rows + member_index * part_rows
    positions = own_first + jnp.arange(part_rows, dtype=jnp.int32)
    result = jnp.zeros((part_rows, logits.shape[0], out_cols), jnp.float32)
    for shift in range(members):
        if shift == 0:
            arrived = lax.dynamic_index_in_dim(outgoing, member_index, 0, keepdims=False)
        else:
            send = lax.dynamic_index_in_dim(
                outgoing, (member_index + shift) % members, 0, keepdims=False
            )
            arrived = lax.ppermute(
                send, "member", [(i, (i + shift) % members) for i in range(members)]
            )
        source = (member_index - shift) % members
        source_code = jnp.sum(jnp.where(jnp.arange(members) == source, views, 0))
        source_numer = source_code // 2
        source_flip = source_code % 2
        source_valid = full_rows * source_numer // 14
        begin = window_start(source_numer, own_first, full_rows, out_rows, window_rows)
        source_cols = column_table(source_numer, source_flip, cols, out_cols)
        row_table = resize_matrix(positions, out_rows, source_valid, full_rows)
        row_part = lax.dynamic_slice_in_dim(row_table, begin, window_rows, 1)
        widened = jnp.einsum(
            "cyx,jx->cyj", arrived, source_cols, preferred_element_type=jnp.float32
        ).astype(jnp.bfloat16)
        result = result + jnp.einsum(
            "iy,cyj->icj", row_part, widened, preferred_element_type=jnp.float32
        )
    return result


def solution(mesh):
    placed = (
        P(("groups", "member"), None, "space", None),
        P("groups"),
        P(),
        P(),
        P(),
        P(),
        P(),
        P(),
    )
    return jax.shard_map(
        shards,
        mesh=mesh,
        in_specs=placed,
        out_specs=P(("groups", "space", "member"), None, None),
        check_vma=False,
    )
```
